32 devices in a mesh: grp: 2 (over x), suf: 4 (over y, core), head: 4 (over z).
Axes of the slice: x: 2, y: 2, z: 4, core: 2. Of those that a mesh axis runs over, the one named last changes fastest.
Arguments:
- prefix_x: bfloat16 [1024, 8192], P(('grp', 'suf'), 'head'), parts along dimension 0, may hold values from -6 to 6
- prefix_b: bfloat16 [1024, 1024], P(('grp', 'suf'), 'head'), parts along dimension 0, may hold values from -6 to 6
- prefix_c: bfloat16 [1024, 1024], P(('grp', 'suf'), 'head'), parts along dimension 0, may hold values from -6 to 6
- prefix_dt: float32 [128, 1024], P('head', ('grp', 'suf')), parts along dimension 1, may hold values from -3 to 3
- prefix_grad: bfloat16 [1024, 8192], P(('grp', 'suf'), 'head'), parts along dimension 0, may hold values from -0.59765625 to 0.59765625
- suffix_x: bfloat16 [8, 128, 8192], P(('grp', 'suf'), None, 'head'), parts along dimension 0, may hold values from -6 to 6
- suffix_b: bfloat16 [8, 128, 1024], P(('grp', 'suf'), None, 'head'), parts along dimension 0, may hold values from -6 to 6
- suffix_c: bfloat16 [8, 128, 1024], P(('grp', 'suf'), None, 'head'), parts along dimension 0, may hold values from -6 to 6
- suffix_dt: float32 [128, 8, 128], P('head', ('grp', 'suf')), parts along dimension 1, may hold values from -3 to 3
- suffix_grad: bfloat16 [8, 128, 8192], P(('grp', 'suf'), None, 'head'), parts along dimension 0, may hold values from -0.59765625 to 0.59765625
- lengths: int32 [8], P(('grp', 'suf')), parts along dimension 0, may hold values from 1 to 128, 384 in all
- loss_mask: int32 [8, 128], P(('grp', 'suf')), parts along dimension 0, may hold values 0 or 1
- advantage: float32 [8], P(('grp', 'suf')), parts along dimension 0, may hold values from -3 to 3
- conv_x: bfloat16 [4, 8192], P(None, 'head'), may hold values from -3 to 3
- conv_b: bfloat16 [4, 1024], P(None, 'head'), may hold values from -3 to 3
- conv_c: bfloat16 [4, 1024], P(None, 'head'), may hold values from -3 to 3
- decay_rate: float32 [128], P('head'), may hold values from 7.8125e-05 to 0.05
- dt_bias: float32 [128], P('head'), may hold values from -1 to 0.5
- skip: float32 [128], P('head'), may hold values from 0.5 to 1.5
Outputs:
- prefix_dx: bfloat16 [1024, 8192], P(('grp', 'suf'), 'head'), parts along dimension 0
- prefix_db: bfloat16 [1024, 1024], P(('grp', 'suf'), 'head'), parts along dimension 0
- prefix_dc: bfloat16 [1024, 1024], P(('grp', 'suf'), 'head'), parts along dimension 0
- prefix_ddt: float32 [128, 1024], P('head', ('grp', 'suf')), parts along dimension 1
- suffix_dx: bfloat16 [8, 128, 8192], P(('grp', 'suf'), None, 'head'), parts along dimension 0
- suffix_db: bfloat16 [8, 128, 1024], P(('grp', 'suf'), None, 'head'), parts along dimension 0
- suffix_dc: bfloat16 [8, 128, 1024], P(('grp', 'suf'), None, 'head'), parts along dimension 0
- suffix_ddt: float32 [128, 8, 128], P('head', ('grp', 'suf')), parts along dimension 1
The draws below stay inside these ranges and needn't reach their ends.
There are 2 independent parts, one for each index of `grp`. The reference program is written for one: setup_inputs(seed, part) draws one part's arguments, and reference() takes and returns one part's arrays. A program takes and returns all parts, laid end to end along the dimension named above; an argument that names none is the same for every part. Nothing has to cross between parts.
Inputs may be any that keep to these rules, and one draw needn't show every extreme that they name: `lengths`: some suffix has exactly 128 tokens.
All inputs are finite; a program needn't handle non-finite values. No bound on the sum of `lengths` or of `loss_mask` on one device may be relied on, other than what follows from the above.
Results may differ from the reference program's by a relative error of at most 0.001.
Values may be sent and summed in bfloat16 or wider, within the bound.
No kernel may reach another device: no remote copies, remote signals or barrier semaphores. Data moves between devices by JAX's collectives and lax.ppermute only.
A program may use at most 128 MiB of HBM per device.

```python
import math
import jax
import jax.numpy as jnp
import numpy as np
from jax import lax

H = 128
HD = 64
N = 128
G = 8
KW = 4
Q = 128
LEN = 128
PREFIX = 512
SUFFIXES = 4


def place_ends(values, key, least, largest):
    shape = values.shape
    index_at = [jax.random.randint(jax.random.fold_in(key, axis), (), 0, shape[axis]) for axis in range(len(shape))]
    values = values.at[tuple(index_at)].set(least)
    longest = shape.index(max(shape))
    index_at[longest] = (index_at[longest] + 1) % shape[longest]
    return values.at[tuple(index_at)].set(largest)


def block_scale(key, dims, cuts, low, top_value):
    loudness, own = 1.0, jax.random.fold_in(key, 6)
    for axis_at, shards_of in cuts:
        steps = jnp.exp(jax.random.uniform(jax.random.fold_in(own, axis_at), (shards_of,), jnp.float32, low / len(cuts), top_value / len(cuts)))
        loudness = loudness * jnp.repeat(steps, dims[axis_at] // shards_of).reshape([-1 if axis == axis_at else 1 for axis in range(len(dims))])
    return loudness


def length_profile(number_of, total, bound, slope):
    loads = [(1 << 20) // math.isqrt(standing ** slope) + 1 for standing in range(2, number_of + 1)]
    rest, counts = total - bound - (number_of - 1), [1] * (number_of - 1)
    while rest > 0:
        candidates = [i for i in range(number_of - 1) if counts[i] < bound]
        pool, budget = sum([loads[i] for i in candidates]), rest
        for i in candidates:
            addition = min(bound - counts[i], max(1, budget * loads[i] // pool), rest)
            counts[i] = counts[i] + addition
            rest = rest - addition
    return np.array([bound] + counts)


def ragged_sizes(key, number_of, total, reach, lean):
    if number_of == 2:
        one = jax.random.randint(key, (), max(1, total - reach), min(reach, total - 1) + 1)
        return jnp.stack([one, total - one])
    tallies = jnp.asarray(length_profile(number_of, total, reach, lean), jnp.int32)
    pairs = (number_of - 1) // 2
    source_of, sink = tallies[1:1 + 2 * pairs:2], tallies[2:2 + 2 * pairs:2]
    room = jnp.minimum(source_of - 1, reach - sink)
    shifted = jax.random.randint(jax.random.fold_in(key, 1), (pairs,), 0, 1 << 20) % (room + 1)
    tallies = tallies.at[1:1 + 2 * pairs:2].set(source_of - shifted).at[2:2 + 2 * pairs:2].set(sink + shifted)
    return tallies[jax.random.permutation(jax.random.fold_in(key, 2), number_of)]


def noise(stream_key, extent, width, reach, shards=(), kind=jnp.bfloat16):
    array = jax.random.normal(stream_key, extent, jnp.float32) * width
    if len(shards) > 0:
        array = block_scale(stream_key, extent, shards, -0.22, 0.18) * array
    return jnp.clip(array, min=-reach, max=reach).astype(kind)


def setup_inputs(seed: int = 0, part: int = 0) -> dict:
    key_list = jax.random.split(jax.random.key(seed), 20)
    part_splits = jax.random.split(jax.random.fold_in(key_list[19], part), 20)
    prefix_x = noise(part_splits[0], (PREFIX, H * HD), 1.0, 6.0, ((0, 4), (1, 4)))
    prefix_b = noise(part_splits[1], (PREFIX, G * N), 1.0, 6.0, ((0, 4), (1, 4)))
    prefix_c = noise(part_splits[2], (PREFIX, G * N), 1.0, 6.0, ((0, 4), (1, 4)))
    prefix_dt = noise(part_splits[3], (H, PREFIX), 0.5, 3.0, ((0, 4), (1, 4)), jnp.float32)
    prefix_grad = noise(part_splits[4], (PREFIX, H * HD), 0.1, 0.59765625, ((0, 4), (1, 4)))
    suffix_x = noise(part_splits[5], (SUFFIXES, LEN, H * HD), 1.0, 6.0, ((0, 4), (2, 4)))
    suffix_b = noise(part_splits[6], (SUFFIXES, LEN, G * N), 1.0, 6.0, ((0, 4), (2, 4)))
    suffix_c = noise(part_splits[7], (SUFFIXES, LEN, G * N), 1.0, 6.0, ((0, 4), (2, 4)))
    suffix_dt = noise(part_splits[8], (H, SUFFIXES, LEN), 0.5, 3.0, ((0, 4), (1, 4)), jnp.float32)
    suffix_grad = noise(part_splits[9], (SUFFIXES, LEN, H * HD), 0.1, 0.59765625, ((0, 4), (2, 4)))
    lengths = ragged_sizes(part_splits[10], SUFFIXES, 3 * SUFFIXES * LEN // 4, LEN, 1).astype(jnp.int32)
    loss_mask = place_ends((jax.random.randint(part_splits[11], (SUFFIXES, LEN), 0, 4) < 3).astype(jnp.int32), jax.random.fold_in(part_splits[11], 1), 0, 1)
    advantage = noise(part_splits[12], (SUFFIXES,), 1.0, 3.0, ((0, 4),), jnp.float32)
    conv_x = noise(key_list[13], (KW, H * HD), KW ** -0.5, 3.0, ((1, 4),))
    conv_b = noise(key_list[14], (KW, G * N), KW ** -0.5, 3.0, ((1, 4),))
    conv_c = noise(key_list[15], (KW, G * N), KW ** -0.5, 3.0, ((1, 4),))
    decay_rate = jnp.clip(jnp.exp(math.log(0.05) - 6.461468 * jax.random.uniform(key_list[16], (H,), jnp.float32) ** block_scale(key_list[16], (H,), ((0, 4),), -0.2, 0.2)), 7.812499825377017e-05, 0.05)
    dt_bias = jnp.clip(-1.0 + 1.5 * jax.random.uniform(key_list[17], (H,), jnp.float32) ** block_scale(key_list[17], (H,), ((0, 4),), -0.2, 0.2), -1.0, 0.5)
    skip = jnp.clip(0.5 + 1.0 * jax.random.uniform(key_list[18], (H,), jnp.float32) ** block_scale(key_list[18], (H,), ((0, 4),), -0.2, 0.2), 0.5, 1.5)
    return dict(prefix_x=prefix_x, prefix_b=prefix_b, prefix_c=prefix_c, prefix_dt=prefix_dt, prefix_grad=prefix_grad, suffix_x=suffix_x, suffix_b=suffix_b, suffix_c=suffix_c, suffix_dt=suffix_dt, suffix_grad=suffix_grad, lengths=lengths, loss_mask=loss_mask, advantage=advantage, conv_x=conv_x, conv_b=conv_b, conv_c=conv_c, decay_rate=decay_rate, dt_bias=dt_bias, skip=skip)


EXACT_DOT = lax.Precision.HIGHEST

def causal_conv(values, context, taps):
    padded = jnp.concatenate([context, values], axis=0)
    num_tokens = values.shape[0]
    result = padded[0:num_tokens] * taps[0].astype(jnp.float32)
    for tap_index in range(1, taps.shape[0]):
        result = result + padded[tap_index:tap_index + num_tokens] * taps[tap_index].astype(jnp.float32)
    return jax.nn.silu(result)

def run_scan(x_act, b_act, c_act, step_dt, decay_rates, skip_gain, start_state):
    tokens = x_act.shape[0]
    num_heads = x_act.shape[1]
    num_groups = b_act.shape[1]
    per_group = num_heads // num_groups
    blocks = tokens // Q
    x_blocks = x_act.reshape(blocks, Q, num_groups, per_group, HD)
    b_blocks = b_act.reshape(blocks, Q, num_groups, N)
    c_blocks = c_act.reshape(blocks, Q, num_groups, N)
    log_decay = (-step_dt * decay_rates[:, None]).reshape(num_groups, per_group, blocks, Q).transpose(2, 0, 1, 3)
    dt_blocks = step_dt.reshape(num_groups, per_group, blocks, Q).transpose(2, 0, 1, 3)
    lower_tri = jnp.arange(Q)[:, None] >= jnp.arange(Q)[None, :]
    skip_shaped = skip_gain.reshape(num_groups, per_group)[:, :, None]

    def advance(current, pieces):
        x_block, b_block, c_block, log_block, dt_block = pieces
        cumulative = jnp.cumsum(log_block, axis=-1)
        log_gaps = cumulative[..., :, None] - cumulative[..., None, :]
        within = jnp.where(lower_tri, jnp.exp(jnp.where(lower_tri, log_gaps, 0.0)), 0.0)
        scores = jnp.einsum('tgn,sgn->gts', c_block, b_block, precision=EXACT_DOT)
        mixing = scores[:, None] * within * dt_block[:, :, None, :]
        inner_out = jnp.einsum('gkts,sgkp->tgkp', mixing, x_block, precision=EXACT_DOT)
        carried = jnp.einsum('tgn,gkpn->tgkp', c_block, current, precision=EXACT_DOT)
        carried = carried * jnp.exp(cumulative).transpose(2, 0, 1)[..., None]
        output = inner_out + carried + skip_shaped * x_block
        weights = jnp.exp(cumulative[..., -1:] - cumulative) * dt_block
        updated = current * jnp.exp(cumulative[..., -1])[..., None, None]
        updated = updated + jnp.einsum('gks,sgkp,sgn->gkpn', weights, x_block, b_block, precision=EXACT_DOT)
        return (updated, output)
    last_state, outputs = lax.scan(jax.checkpoint(advance), start_state.reshape(num_groups, per_group, HD, N), (x_blocks, b_blocks, c_blocks, log_decay, dt_blocks))
    return (outputs.reshape(tokens, num_heads * HD), last_state.reshape(num_heads, HD, N))

def block_forward(x_feat, b_feat, c_feat, dt_raw, left_x, left_b, left_c, start_state, params):
    conv_x, conv_b, conv_c, decay_rates, dt_offset, skip_gain = params
    num_heads = decay_rates.shape[0]
    num_groups = conv_b.shape[1] // N
    x_act = causal_conv(x_feat, left_x, conv_x).reshape(-1, num_heads, HD)
    b_act = causal_conv(b_feat, left_b, conv_b).reshape(-1, num_groups, N)
    c_act = causal_conv(c_feat, left_c, conv_c).reshape(-1, num_groups, N)
    step_dt = jax.nn.softplus(dt_raw + dt_offset[:, None])
    return run_scan(x_act, b_act, c_act, step_dt, decay_rates, skip_gain, start_state)

def reference(prefix_x, prefix_b, prefix_c, prefix_dt, prefix_grad, suffix_x, suffix_b, suffix_c, suffix_dt, suffix_grad, lengths, loss_mask, advantage, conv_x, conv_b, conv_c, decay_rate, dt_bias, skip):
    margin = KW - 1
    params = (conv_x, conv_b, conv_c, decay_rate, dt_bias, skip)

    def forward(prompt_x, prompt_b, prompt_c, prompt_dt, samp_x, samp_b, samp_c, samp_dt):
        zero_x = jnp.zeros((margin, prompt_x.shape[1]), jnp.float32)
        zero_b = jnp.zeros((margin, prompt_b.shape[1]), jnp.float32)
        zero_state = jnp.zeros((H, HD, N), jnp.float32)
        prompt_out, prompt_end = block_forward(prompt_x, prompt_b, prompt_c, prompt_dt, zero_x, zero_b, zero_b, zero_state, params)

        def one_suffix(items):
            x_one, b_one, c_one, dt_one = items
            out_one, unused_end = block_forward(x_one, b_one, c_one, dt_one, prompt_x[-margin:], prompt_b[-margin:], prompt_c[-margin:], prompt_end, params)
            return out_one
        suffix_out = lax.map(one_suffix, (samp_x, samp_b, samp_c, jnp.transpose(samp_dt, (1, 0, 2))))
        return (prompt_out, suffix_out)
    primals = (prefix_x.astype(jnp.float32), prefix_b.astype(jnp.float32), prefix_c.astype(jnp.float32), prefix_dt, suffix_x.astype(jnp.float32), suffix_b.astype(jnp.float32), suffix_c.astype(jnp.float32), suffix_dt)
    unused_out, pullback = jax.vjp(forward, primals[0], primals[1], primals[2], primals[3], primals[4], primals[5], primals[6], primals[7])
    positions = jnp.arange(LEN)[None, :]
    valid = (positions < lengths[:, None]).astype(jnp.float32)
    weight = advantage[:, None] * loss_mask.astype(jnp.float32) * valid
    suffix_cot = weight[:, :, None] * suffix_grad.astype(jnp.float32)
    grads = pullback((prefix_grad.astype(jnp.float32), suffix_cot))
    return (grads[0].astype(jnp.bfloat16), grads[1].astype(jnp.bfloat16), grads[2].astype(jnp.bfloat16), grads[3], grads[4].astype(jnp.bfloat16), grads[5].astype(jnp.bfloat16), grads[6].astype(jnp.bfloat16), grads[7])
```

```python
import jax
import jax.numpy as jnp
from jax import lax
from jax.sharding import PartitionSpec as P

HD = 64
N = 128
KW = 4
Q = 128


EXACT_DOT = lax.Precision.HIGHEST


def from_behind(block, axis, distance):
    devices = range(lax.axis_size(axis))
    route = [(i - distance, i) for i in devices if i - distance in devices]
    return lax.ppermute(block, axis, route)


def prefix(shard, axis, combine, identity, reverse):
    length, here = (lax.axis_size(axis), lax.axis_index(axis))
    everything = jax.tree.map(lambda part: lax.all_gather(part, axis), shard)
    start = jax.tree.map(
        lambda part, zero: jnp.broadcast_to(jnp.asarray(zero, part.dtype), part.shape),
        shard,
        identity,
    )

    def lap(k, before):
        at = length - 1 - k if reverse else k
        reached = at > here if reverse else at < here
        new = combine(before, jax.tree.map(lambda part: part[at], everything))
        return jax.tree.map(lambda a, b: jnp.where(reached, a, b), new, before)

    return lax.fori_loop(0, length, lap, start)


def spread(block, axis, holder):
    block = jnp.where(lax.axis_index(axis) == holder, block, jnp.zeros_like(block))
    return lax.psum(block, axis)


def causal_conv(values, context, taps):
    padded = jnp.concatenate([context, values], axis=0)
    num_tokens = values.shape[0]
    result = padded[0:num_tokens] * taps[0].astype(jnp.float32)
    for tap_index in range(1, taps.shape[0]):
        result = result + padded[tap_index : tap_index + num_tokens] * taps[tap_index].astype(
            jnp.float32
        )
    return jax.nn.silu(result)


def run_scan(x_act, b_act, c_act, step_dt, decay_rates, skip_gain, start_state):
    tokens = x_act.shape[0]
    num_heads = x_act.shape[1]
    num_groups = b_act.shape[1]
    per_group = num_heads // num_groups
    blocks = tokens // Q
    x_blocks = x_act.reshape(blocks, Q, num_groups, per_group, HD)
    b_blocks = b_act.reshape(blocks, Q, num_groups, N)
    c_blocks = c_act.reshape(blocks, Q, num_groups, N)
    log_decay = (
        (-step_dt * decay_rates[:, None])
        .reshape(num_groups, per_group, blocks, Q)
        .transpose(2, 0, 1, 3)
    )
    dt_blocks = step_dt.reshape(num_groups, per_group, blocks, Q).transpose(2, 0, 1, 3)
    lower_tri = jnp.arange(Q)[:, None] >= jnp.arange(Q)[None, :]
    skip_shaped = skip_gain.reshape(num_groups, per_group)[:, :, None]

    def advance(current, pieces):
        x_block, b_block, c_block, log_block, dt_block = pieces
        cumulative = jnp.cumsum(log_block, axis=-1)
        log_gaps = cumulative[..., :, None] - cumulative[..., None, :]
        within = jnp.where(lower_tri, jnp.exp(jnp.where(lower_tri, log_gaps, 0.0)), 0.0)
        scores = jnp.einsum("tgn,sgn->gts", c_block, b_block, precision=EXACT_DOT)
        mixing = scores[:, None] * within * dt_block[:, :, None, :]
        inner_out = jnp.einsum("gkts,sgkp->tgkp", mixing, x_block, precision=EXACT_DOT)
        carried = jnp.einsum("tgn,gkpn->tgkp", c_block, current, precision=EXACT_DOT)
        carried = carried * jnp.exp(cumulative).transpose(2, 0, 1)[..., None]
        output = inner_out + carried + skip_shaped * x_block
        weights = jnp.exp(cumulative[..., -1:] - cumulative) * dt_block
        updated = current * jnp.exp(cumulative[..., -1])[..., None, None]
        updated = updated + jnp.einsum(
            "gks,sgkp,sgn->gkpn", weights, x_block, b_block, precision=EXACT_DOT
        )
        return (updated, output)

    last_state, outputs = lax.scan(
        jax.checkpoint(advance),
        start_state.reshape(num_groups, per_group, HD, N),
        (x_blocks, b_blocks, c_blocks, log_decay, dt_blocks),
    )
    return (outputs.reshape(tokens, num_heads * HD), last_state.reshape(num_heads, HD, N))


def block_forward(x_feat, b_feat, c_feat, dt_raw, left_x, left_b, left_c, start_state, params):
    conv_x, conv_b, conv_c, decay_rates, dt_offset, skip_gain = params
    num_heads = decay_rates.shape[0]
    num_groups = conv_b.shape[1] // N
    x_act = causal_conv(x_feat, left_x, conv_x).reshape(-1, num_heads, HD)
    b_act = causal_conv(b_feat, left_b, conv_b).reshape(-1, num_groups, N)
    c_act = causal_conv(c_feat, left_c, conv_c).reshape(-1, num_groups, N)
    step_dt = jax.nn.softplus(dt_raw + dt_offset[:, None])
    return run_scan(x_act, b_act, c_act, step_dt, decay_rates, skip_gain, start_state)


def combine_pairs(early, later):
    scaled = jnp.exp(later[0])[:, None, None] * early[1] + later[1]
    others = tuple((early[member] + later[member] for member in range(2, len(early))))
    return (early[0] + later[0], scaled) + others


def shards(
    prefix_x,
    prefix_b,
    prefix_c,
    prefix_dt,
    prefix_grad,
    suffix_x,
    suffix_b,
    suffix_c,
    suffix_dt,
    suffix_grad,
    lengths,
    loss_mask,
    advantage,
    conv_x,
    conv_b,
    conv_c,
    decay_rate,
    dt_bias,
    skip,
):
    num_ways = lax.axis_size("suf")
    my_index = lax.axis_index("suf")
    num_heads = decay_rate.shape[0]
    num_groups = conv_b.shape[1] // N
    per_group = num_heads // num_groups
    margin = KW - 1
    prompt_len = prefix_x.shape[0]
    params = (conv_x, conv_b, conv_c, decay_rate, dt_bias, skip)
    tails = (prefix_x[-margin:], prefix_b[-margin:], prefix_c[-margin:])
    from_left = from_behind(tails, "suf", 1)
    all_tails = lax.all_gather(tails, "suf")
    ctx_x = all_tails[0][num_ways - 1].astype(jnp.float32)
    ctx_b = all_tails[1][num_ways - 1].astype(jnp.float32)
    ctx_c = all_tails[2][num_ways - 1].astype(jnp.float32)
    left_x = from_left[0].astype(jnp.float32)
    left_b = from_left[1].astype(jnp.float32)
    left_c = from_left[2].astype(jnp.float32)
    prompt_x = prefix_x.astype(jnp.float32)
    prompt_b = prefix_b.astype(jnp.float32)
    prompt_c = prefix_c.astype(jnp.float32)
    prompt_cot = prefix_grad.astype(jnp.float32)
    x_act = causal_conv(prompt_x, left_x, conv_x).reshape(prompt_len, num_groups, per_group, HD)
    b_act = causal_conv(prompt_b, left_b, conv_b).reshape(prompt_len, num_groups, N)
    c_act = causal_conv(prompt_c, left_c, conv_c).reshape(prompt_len, num_groups, N)
    prompt_step = jax.nn.softplus(prefix_dt + dt_bias[:, None])
    cumulative = jnp.cumsum(-prompt_step * decay_rate[:, None], axis=1)
    total_log = cumulative[:, -1]
    push_weight = (jnp.exp(total_log[:, None] - cumulative) * prompt_step).reshape(
        num_groups, per_group, prompt_len
    )
    own_state = jnp.einsum(
        "gkt,tgkp,tgn->gkpn", push_weight, x_act, b_act, precision=EXACT_DOT
    ).reshape(num_heads, HD, N)
    pull_weight = jnp.exp(cumulative).reshape(num_groups, per_group, prompt_len)
    own_adjoint = jnp.einsum(
        "gkt,tgkp,tgn->gkpn",
        pull_weight,
        prompt_cot.reshape(prompt_len, num_groups, per_group, HD),
        c_act,
        precision=EXACT_DOT,
    ).reshape(num_heads, HD, N)
    every_log, every_state = lax.all_gather((total_log, own_state), "suf")
    running = jnp.zeros_like(own_state)
    start_state = running
    for block in range(num_ways):
        start_state = jnp.where(my_index == block, running, start_state)
        running = jnp.exp(every_log[block])[:, None, None] * running + every_state[block]
    prompt_end = running
    positions = jnp.arange(suffix_x.shape[1])[None, :]
    weight = (
        advantage[:, None]
        * loss_mask.astype(jnp.float32)
        * (positions < lengths[:, None]).astype(jnp.float32)
    )
    suffix_cot = weight[:, :, None] * suffix_grad.astype(jnp.float32)
    zero_end = jnp.zeros((num_heads, HD, N), jnp.float32)

    def forward_block(x_feat, b_feat, c_feat, dt_raw, left_xin, left_bin, left_cin, first_state):
        return block_forward(
            x_feat, b_feat, c_feat, dt_raw, left_xin, left_bin, left_cin, first_state, params
        )

    def one_back(x_one, b_one, c_one, dt_one, cot_one):
        unused_out, pullback = jax.vjp(
            forward_block, x_one, b_one, c_one, dt_one, ctx_x, ctx_b, ctx_c, prompt_end
        )
        return pullback((cot_one, zero_end))

    suffix_back = jax.vmap(one_back)(
        suffix_x.astype(jnp.float32),
        suffix_b.astype(jnp.float32),
        suffix_c.astype(jnp.float32),
        jnp.transpose(suffix_dt, (1, 0, 2)),
        suffix_cot,
    )
    summed = lax.psum(
        (
            jnp.sum(suffix_back[7], axis=0),
            jnp.sum(suffix_back[4], axis=0),
            jnp.sum(suffix_back[5], axis=0),
        ),
        "suf",
    )
    summed_c = lax.psum(jnp.sum(suffix_back[6], axis=0), "suf")
    every_adjoint = lax.all_gather(own_adjoint, "suf")
    running = summed[0]
    end_grad = running
    for block in reversed(range(num_ways)):
        end_grad = jnp.where(my_index == block, running, end_grad)
        running = every_adjoint[block] + jnp.exp(every_log[block])[:, None, None] * running
    last_device = my_index == num_ways - 1
    tail_grads = tuple(
        (jnp.where(last_device, member, 0.0) for member in (summed[1], summed[2], summed_c))
    )
    unused_prompt, pullback = jax.vjp(
        forward_block, prompt_x, prompt_b, prompt_c, prefix_dt, left_x, left_b, left_c, start_state
    )
    prompt_grads = pullback((prompt_cot, end_grad))
    from_right = from_behind((prompt_grads[4], prompt_grads[5], prompt_grads[6]), "suf", -1)

    def finish(grad_full, from_next, from_suffix):
        return grad_full.at[-margin:].add(from_next + from_suffix).astype(jnp.bfloat16)

    prefix_dx = finish(prompt_grads[0], from_right[0], tail_grads[0])
    prefix_db = finish(prompt_grads[1], from_right[1], tail_grads[1])
    prefix_dc = finish(prompt_grads[2], from_right[2], tail_grads[2])
    return (
        prefix_dx,
        prefix_db,
        prefix_dc,
        prompt_grads[3],
        suffix_back[0].astype(jnp.bfloat16),
        suffix_back[1].astype(jnp.bfloat16),
        suffix_back[2].astype(jnp.bfloat16),
        jnp.transpose(suffix_back[3], (1, 0, 2)),
    )


def solution(mesh):
    return jax.shard_map(
        shards,
        mesh=mesh,
        in_specs=(
            P(("grp", "suf"), "head"),
            P(("grp", "suf"), "head"),
            P(("grp", "suf"), "head"),
            P("head", ("grp", "suf")),
            P(("grp", "suf"), "head"),
            P(("grp", "suf"), None, "head"),
            P(("grp", "suf"), None, "head"),
            P(("grp", "suf"), None, "head"),
            P("head", ("grp", "suf"), None),
            P(("grp", "suf"), None, "head"),
            P(("grp", "suf")),
            P(("grp", "suf"), None),
            P(("grp", "suf")),
            P(None, "head"),
            P(None, "head"),
            P(None, "head"),
            P("head"),
            P("head"),
            P("head"),
        ),
        out_specs=(
            P(("grp", "suf"), "head"),
            P(("grp", "suf"), "head"),
            P(("grp", "suf"), "head"),
            P("head", ("grp", "suf")),
            P(("grp", "suf"), None, "head"),
            P(("grp", "suf"), None, "head"),
            P(("grp", "suf"), None, "head"),
            P("head", ("grp", "suf"), None),
        ),
        check_vma=False,
    )
```

```python
import jax
import jax.numpy as jnp
from jax import lax
from jax.sharding import PartitionSpec as P

HD = 64
N = 128
KW = 4
Q = 128


EXACT_DOT = lax.Precision.HIGHEST


def from_behind(block, axis, distance):
    devices = range(lax.axis_size(axis))
    route = [(i - distance, i) for i in devices if i - distance in devices]
    return lax.ppermute(block, axis, route)


def prefix(shard, axis, combine, identity, reverse):
    length, here = (lax.axis_size(axis), lax.axis_index(axis))
    everything = jax.tree.map(lambda part: lax.all_gather(part, axis), shard)
    start = jax.tree.map(
        lambda part, zero: jnp.broadcast_to(jnp.asarray(zero, part.dtype), part.shape),
        shard,
        identity,
    )

    def lap(k, before):
        at = length - 1 - k if reverse else k
        reached = at > here if reverse else at < here
        new = combine(before, jax.tree.map(lambda part: part[at], everything))
        return jax.tree.map(lambda a, b: jnp.where(reached, a, b), new, before)

    return lax.fori_loop(0, length, lap, start)


def spread(block, axis, holder):
    block = jnp.where(lax.axis_index(axis) == holder, block, jnp.zeros_like(block))
    return lax.psum(block, axis)


def causal_conv(values, context, taps):
    padded = jnp.concatenate([context, values], axis=0)
    num_tokens = values.shape[0]
    result = padded[0:num_tokens] * taps[0].astype(jnp.float32)
    for tap_index in range(1, taps.shape[0]):
        result = result + padded[tap_index : tap_index + num_tokens] * taps[tap_index].astype(
            jnp.float32
        )
    return jax.nn.silu(result)


def run_scan(x_act, b_act, c_act, step_dt, decay_rates, skip_gain, start_state):
    tokens = x_act.shape[0]
    num_heads = x_act.shape[1]
    num_groups = b_act.shape[1]
    per_group = num_heads // num_groups
    blocks = tokens // Q
    x_blocks = x_act.reshape(blocks, Q, num_groups, per_group, HD)
    b_blocks = b_act.reshape(blocks, Q, num_groups, N)
    c_blocks = c_act.reshape(blocks, Q, num_groups, N)
    log_decay = (
        (-step_dt * decay_rates[:, None])
        .reshape(num_groups, per_group, blocks, Q)
        .transpose(2, 0, 1, 3)
    )
    dt_blocks = step_dt.reshape(num_groups, per_group, blocks, Q).transpose(2, 0, 1, 3)
    lower_tri = jnp.arange(Q)[:, None] >= jnp.arange(Q)[None, :]
    skip_shaped = skip_gain.reshape(num_groups, per_group)[:, :, None]

    def advance(current, pieces):
        x_block, b_block, c_block, log_block, dt_block = pieces
        cumulative = jnp.cumsum(log_block, axis=-1)
        log_gaps = cumulative[..., :, None] - cumulative[..., None, :]
        within = jnp.where(lower_tri, jnp.exp(jnp.where(lower_tri, log_gaps, 0.0)), 0.0)
        scores = jnp.einsum("tgn,sgn->gts", c_block, b_block, precision=EXACT_DOT)
        mixing = scores[:, None] * within * dt_block[:, :, None, :]
        inner_out = jnp.einsum("gkts,sgkp->tgkp", mixing, x_block, precision=EXACT_DOT)
        carried = jnp.einsum("tgn,gkpn->tgkp", c_block, current, precision=EXACT_DOT)
        carried = carried * jnp.exp(cumulative).transpose(2, 0, 1)[..., None]
        output = inner_out + carried + skip_shaped * x_block
        weights = jnp.exp(cumulative[..., -1:] - cumulative) * dt_block
        updated = current * jnp.exp(cumulative[..., -1])[..., None, None]
        updated = updated + jnp.einsum(
            "gks,sgkp,sgn->gkpn", weights, x_block, b_block, precision=EXACT_DOT
        )
        return (updated, output)

    last_state, outputs = lax.scan(
        jax.checkpoint(advance),
        start_state.reshape(num_groups, per_group, HD, N),
        (x_blocks, b_blocks, c_blocks, log_decay, dt_blocks),
    )
    return (outputs.reshape(tokens, num_heads * HD), last_state.reshape(num_heads, HD, N))


def block_forward(x_feat, b_feat, c_feat, dt_raw, left_x, left_b, left_c, start_state, params):
    conv_x, conv_b, conv_c, decay_rates, dt_offset, skip_gain = params
    num_heads = decay_rates.shape[0]
    num_groups = conv_b.shape[1] // N
    x_act = causal_conv(x_feat, left_x, conv_x).reshape(-1, num_heads, HD)
    b_act = causal_conv(b_feat, left_b, conv_b).reshape(-1, num_groups, N)
    c_act = causal_conv(c_feat, left_c, conv_c).reshape(-1, num_groups, N)
    step_dt = jax.nn.softplus(dt_raw + dt_offset[:, None])
    return run_scan(x_act, b_act, c_act, step_dt, decay_rates, skip_gain, start_state)


def block_grads(xa, ba, ca, step, rate, skip, S0, G, lam):
    T = xa.shape[0]
    tri = jnp.arange(T)[:, None] >= jnp.arange(T)[None, :]
    cum = jnp.cumsum(-step * rate[:, :, None], axis=-1)
    gaps = cum[..., :, None] - cum[..., None, :]
    within = jnp.where(tri, jnp.exp(jnp.where(tri, gaps, 0.0)), 0.0)
    scores = jnp.einsum("tgn,sgn->gts", ca, ba, precision=EXACT_DOT)
    score_w = scores[:, None] * within
    mixing = score_w * step[:, :, None, :]
    d_mix = jnp.einsum("tgkp,sgkp->gkts", G, xa, precision=EXACT_DOT)
    dx = jnp.einsum("gkts,tgkp->sgkp", mixing, G, precision=EXACT_DOT) + skip[None, :, :, None] * G
    d_sw = d_mix * within
    d_scores = jnp.sum(d_sw * step[:, :, None, :], axis=1)
    dc = jnp.einsum("gts,sgn->tgn", d_scores, ba, precision=EXACT_DOT)
    db = jnp.einsum("gts,tgn->sgn", d_scores, ca, precision=EXACT_DOT)
    grow = jnp.exp(cum)
    g_grow = G * grow.transpose(2, 0, 1)[..., None]
    carried = jnp.einsum("tgn,gkpn->tgkp", ca, S0, precision=EXACT_DOT)
    dc = dc + jnp.einsum("tgkp,gkpn->tgn", g_grow, S0, precision=EXACT_DOT)
    d_cum = jnp.sum(g_grow * carried, axis=-1).transpose(1, 2, 0)
    q_mat = d_mix * score_w
    d_step = jnp.sum(q_mat, axis=-2)
    p_mat = q_mat * step[:, :, None, :]
    d_cum = d_cum + jnp.sum(p_mat, axis=-1) - jnp.sum(p_mat, axis=-2)
    if lam is not None:
        to_end = jnp.exp(cum[..., -1:] - cum)
        push = to_end * step
        lam_b = jnp.einsum("gkpn,sgn->sgkp", lam, ba, precision=EXACT_DOT)
        dx = dx + push.transpose(2, 0, 1)[..., None] * lam_b
        db = db + jnp.einsum("gkpn,sgkp,gks->sgn", lam, xa, push, precision=EXACT_DOT)
        q_end = jnp.sum(xa * lam_b, axis=-1).transpose(1, 2, 0)
        d_step = d_step + to_end * q_end
        wq = push * q_end
        end_total = jnp.sum(wq, axis=-1) + jnp.exp(cum[..., -1]) * jnp.sum(lam * S0, axis=(-2, -1))
        d_cum = d_cum - wq
        d_cum = d_cum.at[..., -1].add(end_total)
    d_log = jnp.flip(jnp.cumsum(jnp.flip(d_cum, -1), axis=-1), -1)
    d_step = d_step - rate[:, :, None] * d_log
    return dx, db, dc, d_step


def shards(
    prefix_x,
    prefix_b,
    prefix_c,
    prefix_dt,
    prefix_grad,
    suffix_x,
    suffix_b,
    suffix_c,
    suffix_dt,
    suffix_grad,
    lengths,
    loss_mask,
    advantage,
    conv_x,
    conv_b,
    conv_c,
    decay_rate,
    dt_bias,
    skip,
):
    num_ways = lax.axis_size("suf")
    my_index = lax.axis_index("suf")
    num_heads = decay_rate.shape[0]
    num_groups = conv_b.shape[1] // N
    per_group = num_heads // num_groups
    margin = KW - 1
    prompt_len = prefix_x.shape[0]
    width_x = prefix_x.shape[1]
    width_b = prefix_b.shape[1]
    rate = decay_rate.reshape(num_groups, per_group)
    gain = skip.reshape(num_groups, per_group)

    def split_tokens(tokens):
        return (
            tokens[:, :width_x],
            tokens[:, width_x : width_x + width_b],
            tokens[:, width_x + width_b :],
        )

    def convs(ux, ub, uc, cx, cb, cc):
        return (
            causal_conv(ux, cx, conv_x),
            causal_conv(ub, cb, conv_b),
            causal_conv(uc, cc, conv_c),
        )

    def softplus_of(raw):
        return jax.nn.softplus(raw + dt_bias[:, None])

    prompt_step, step_pullback = jax.vjp(softplus_of, prefix_dt)
    cumulative = jnp.cumsum(-prompt_step * decay_rate[:, None], axis=1)
    total_log = cumulative[:, -1]
    tails = jnp.concatenate(
        [prefix_x[-margin:], prefix_b[-margin:], prefix_c[-margin:]], axis=1
    ).astype(jnp.float32)
    tail_size = tails.size
    every = lax.all_gather(jnp.concatenate([tails.reshape(-1), total_log]), "suf")
    every_tails = every[:, :tail_size].reshape((num_ways,) + tails.shape)
    every_log = every[:, tail_size:]
    behind = lax.dynamic_index_in_dim(every_tails, jnp.maximum(my_index - 1, 0), 0, False)
    behind = jnp.where(my_index > 0, behind, 0.0)
    left_x, left_b, left_c = split_tokens(behind)
    ctx_x, ctx_b, ctx_c = split_tokens(every_tails[num_ways - 1])

    acts, prompt_conv_pullback = jax.vjp(
        convs,
        prefix_x.astype(jnp.float32),
        prefix_b.astype(jnp.float32),
        prefix_c.astype(jnp.float32),
        left_x,
        left_b,
        left_c,
    )
    x_act = acts[0].reshape(prompt_len, num_groups, per_group, HD)
    b_act = acts[1].reshape(prompt_len, num_groups, N)
    c_act = acts[2].reshape(prompt_len, num_groups, N)
    prompt_cot = prefix_grad.astype(jnp.float32).reshape(prompt_len, num_groups, per_group, HD)
    push_weight = (jnp.exp(total_log[:, None] - cumulative) * prompt_step).reshape(
        num_groups, per_group, prompt_len
    )
    own_state = jnp.einsum("gkt,tgkp,tgn->gkpn", push_weight, x_act, b_act, precision=EXACT_DOT)
    pull_weight = jnp.exp(cumulative).reshape(num_groups, per_group, prompt_len)
    own_adjoint = jnp.einsum(
        "gkt,tgkp,tgn->gkpn", pull_weight, prompt_cot, c_act, precision=EXACT_DOT
    )
    every_pair = lax.all_gather(jnp.stack([own_state, own_adjoint]), "suf")
    every_decay = jnp.exp(every_log).reshape(num_ways, num_groups, per_group, 1, 1)
    running = jnp.zeros_like(own_state)
    start_state = running
    for block in range(num_ways):
        start_state = jnp.where(my_index == block, running, start_state)
        running = every_decay[block] * running + every_pair[block, 0]
    prompt_end = running

    positions = jnp.arange(suffix_x.shape[1])[None, :]
    weight = (
        advantage[:, None]
        * loss_mask.astype(jnp.float32)
        * (positions < lengths[:, None]).astype(jnp.float32)
    )

    def one_suffix(x_one, b_one, c_one, dt_one, grad_one, weight_one):
        suffix_len = x_one.shape[0]
        step_one, one_step_pullback = jax.vjp(softplus_of, dt_one)
        s_acts, conv_pullback = jax.vjp(convs, x_one, b_one, c_one, ctx_x, ctx_b, ctx_c)
        sx = s_acts[0].reshape(suffix_len, num_groups, per_group, HD)
        sb = s_acts[1].reshape(suffix_len, num_groups, N)
        sc = s_acts[2].reshape(suffix_len, num_groups, N)
        cot = (weight_one[:, None] * grad_one).reshape(suffix_len, num_groups, per_group, HD)
        step_g = step_one.reshape(num_groups, per_group, suffix_len)
        grow = jnp.exp(jnp.cumsum(-step_g * rate[:, :, None], axis=-1))
        adjoint = jnp.einsum("gkt,tgkp,tgn->gkpn", grow, cot, sc, precision=EXACT_DOT)
        dx, db, dc, d_step = block_grads(sx, sb, sc, step_g, rate, gain, prompt_end, cot, None)
        conv_grads = conv_pullback(
            (dx.reshape(suffix_len, -1), db.reshape(suffix_len, -1), dc.reshape(suffix_len, -1))
        )
        d_dt = one_step_pullback(d_step.reshape(num_heads, suffix_len))[0]
        return conv_grads, d_dt, adjoint

    conv_grads, suffix_ddt, adjoints = jax.vmap(one_suffix, in_axes=(0, 0, 0, 1, 0, 0), out_axes=(0, 1, 0))(
        suffix_x.astype(jnp.float32),
        suffix_b.astype(jnp.float32),
        suffix_c.astype(jnp.float32),
        suffix_dt,
        suffix_grad.astype(jnp.float32),
        weight,
    )
    summed = lax.psum(
        (jnp.sum(adjoints, axis=0), jnp.sum(conv_grads[3], axis=0), jnp.sum(conv_grads[4], axis=0)),
        "suf",
    )
    summed_c = lax.psum(jnp.sum(conv_grads[5], axis=0), "suf")
    running = summed[0]
    end_grad = running
    for block in reversed(range(num_ways)):
        end_grad = jnp.where(my_index == block, running, end_grad)
        running = every_pair[block, 1] + every_decay[block] * running

    step_g = prompt_step.reshape(num_groups, per_group, prompt_len)
    dx, db, dc, d_step = block_grads(
        x_act, b_act, c_act, step_g, rate, gain, start_state, prompt_cot, end_grad
    )
    prompt_grads = prompt_conv_pullback(
        (dx.reshape(prompt_len, -1), db.reshape(prompt_len, -1), dc.reshape(prompt_len, -1))
    )
    prefix_ddt = step_pullback(d_step.reshape(num_heads, prompt_len))[0]
    left_grads = jnp.concatenate([prompt_grads[3], prompt_grads[4], prompt_grads[5]], axis=1)
    from_right = from_behind(left_grads, "suf", -1)
    last_device = my_index == num_ways - 1
    from_suffix = jnp.concatenate([summed[1], summed[2], summed_c], axis=1)
    tail_add = split_tokens(from_right + jnp.where(last_device, from_suffix, 0.0))

    def finish(grad_full, extra):
        return grad_full.at[-margin:].add(extra).astype(jnp.bfloat16)

    return (
        finish(prompt_grads[0], tail_add[0]),
        finish(prompt_grads[1], tail_add[1]),
        finish(prompt_grads[2], tail_add[2]),
        prefix_ddt,
        conv_grads[0].astype(jnp.bfloat16),
        conv_grads[1].astype(jnp.bfloat16),
        conv_grads[2].astype(jnp.bfloat16),
        suffix_ddt,
    )


def solution(mesh):
    return jax.shard_map(
        shards,
        mesh=mesh,
        in_specs=(
            P(("grp", "suf"), "head"),
            P(("grp", "suf"), "head"),
            P(("grp", "suf"), "head"),
            P("head", ("grp", "suf")),
            P(("grp", "suf"), "head"),
            P(("grp", "suf"), None, "head"),
            P(("grp", "suf"), None, "head"),
            P(("grp", "suf"), None, "head"),
            P("head", ("grp", "suf"), None),
            P(("grp", "suf"), None, "head"),
            P(("grp", "suf")),
            P(("grp", "suf"), None),
            P(("grp", "suf")),
            P(None, "head"),
            P(None, "head"),
            P(None, "head"),
            P("head"),
            P("head"),
            P("head"),
        ),
        out_specs=(
            P(("grp", "suf"), "head"),
            P(("grp", "suf"), "head"),
            P(("grp", "suf"), "head"),
            P("head", ("grp", "suf")),
            P(("grp", "suf"), None, "head"),
            P(("grp", "suf"), None, "head"),
            P(("grp", "suf"), None, "head"),
            P("head", ("grp", "suf"), None),
        ),
        check_vma=False,
    )
```

```python
import jax
import jax.numpy as jnp
from jax import lax
from jax.sharding import PartitionSpec as P

HD = 64
N = 128
KW = 4
Q = 128


EXACT_DOT = lax.Precision.HIGHEST


def from_behind(block, axis, distance):
    devices = range(lax.axis_size(axis))
    route = [(i - distance, i) for i in devices if i - distance in devices]
    return lax.ppermute(block, axis, route)


def prefix(shard, axis, combine, identity, reverse):
    length, here = (lax.axis_size(axis), lax.axis_index(axis))
    everything = jax.tree.map(lambda part: lax.all_gather(part, axis), shard)
    start = jax.tree.map(
        lambda part, zero: jnp.broadcast_to(jnp.asarray(zero, part.dtype), part.shape),
        shard,
        identity,
    )

    def lap(k, before):
        at = length - 1 - k if reverse else k
        reached = at > here if reverse else at < here
        new = combine(before, jax.tree.map(lambda part: part[at], everything))
        return jax.tree.map(lambda a, b: jnp.where(reached, a, b), new, before)

    return lax.fori_loop(0, length, lap, start)


def spread(block, axis, holder):
    block = jnp.where(lax.axis_index(axis) == holder, block, jnp.zeros_like(block))
    return lax.psum(block, axis)


def causal_conv(values, context, taps):
    padded = jnp.concatenate([context, values], axis=0)
    num_tokens = values.shape[0]
    result = padded[0:num_tokens] * taps[0].astype(jnp.float32)
    for tap_index in range(1, taps.shape[0]):
        result = result + padded[tap_index : tap_index + num_tokens] * taps[tap_index].astype(
            jnp.float32
        )
    return jax.nn.silu(result)


def run_scan(x_act, b_act, c_act, step_dt, decay_rates, skip_gain, start_state):
    tokens = x_act.shape[0]
    num_heads = x_act.shape[1]
    num_groups = b_act.shape[1]
    per_group = num_heads // num_groups
    blocks = tokens // Q
    x_blocks = x_act.reshape(blocks, Q, num_groups, per_group, HD)
    b_blocks = b_act.reshape(blocks, Q, num_groups, N)
    c_blocks = c_act.reshape(blocks, Q, num_groups, N)
    log_decay = (
        (-step_dt * decay_rates[:, None])
        .reshape(num_groups, per_group, blocks, Q)
        .transpose(2, 0, 1, 3)
    )
    dt_blocks = step_dt.reshape(num_groups, per_group, blocks, Q).transpose(2, 0, 1, 3)
    lower_tri = jnp.arange(Q)[:, None] >= jnp.arange(Q)[None, :]
    skip_shaped = skip_gain.reshape(num_groups, per_group)[:, :, None]

    def advance(current, pieces):
        x_block, b_block, c_block, log_block, dt_block = pieces
        cumulative = jnp.cumsum(log_block, axis=-1)
        log_gaps = cumulative[..., :, None] - cumulative[..., None, :]
        within = jnp.where(lower_tri, jnp.exp(jnp.where(lower_tri, log_gaps, 0.0)), 0.0)
        scores = jnp.einsum("tgn,sgn->gts", c_block, b_block, precision=EXACT_DOT)
        mixing = scores[:, None] * within * dt_block[:, :, None, :]
        inner_out = jnp.einsum("gkts,sgkp->tgkp", mixing, x_block, precision=EXACT_DOT)
        carried = jnp.einsum("tgn,gkpn->tgkp", c_block, current, precision=EXACT_DOT)
        carried = carried * jnp.exp(cumulative).transpose(2, 0, 1)[..., None]
        output = inner_out + carried + skip_shaped * x_block
        weights = jnp.exp(cumulative[..., -1:] - cumulative) * dt_block
        updated = current * jnp.exp(cumulative[..., -1])[..., None, None]
        updated = updated + jnp.einsum(
            "gks,sgkp,sgn->gkpn", weights, x_block, b_block, precision=EXACT_DOT
        )
        return (updated, output)

    last_state, outputs = lax.scan(
        jax.checkpoint(advance),
        start_state.reshape(num_groups, per_group, HD, N),
        (x_blocks, b_blocks, c_blocks, log_decay, dt_blocks),
    )
    return (outputs.reshape(tokens, num_heads * HD), last_state.reshape(num_heads, HD, N))


def block_forward(x_feat, b_feat, c_feat, dt_raw, left_x, left_b, left_c, start_state, params):
    conv_x, conv_b, conv_c, decay_rates, dt_offset, skip_gain = params
    num_heads = decay_rates.shape[0]
    num_groups = conv_b.shape[1] // N
    x_act = causal_conv(x_feat, left_x, conv_x).reshape(-1, num_heads, HD)
    b_act = causal_conv(b_feat, left_b, conv_b).reshape(-1, num_groups, N)
    c_act = causal_conv(c_feat, left_c, conv_c).reshape(-1, num_groups, N)
    step_dt = jax.nn.softplus(dt_raw + dt_offset[:, None])
    return run_scan(x_act, b_act, c_act, step_dt, decay_rates, skip_gain, start_state)


def block_grads(xa, ba, ca, step, rate, skip, S0, G, lam):
    T = xa.shape[0]
    tri = jnp.arange(T)[:, None] >= jnp.arange(T)[None, :]
    cum = jnp.cumsum(-step * rate[:, :, None], axis=-1)
    gaps = cum[..., :, None] - cum[..., None, :]
    within = jnp.where(tri, jnp.exp(jnp.where(tri, gaps, 0.0)), 0.0)
    scores = jnp.einsum("tgn,sgn->gts", ca, ba, precision=EXACT_DOT)
    score_w = scores[:, None] * within
    mixing = score_w * step[:, :, None, :]
    d_mix = jnp.einsum("tgkp,sgkp->gkts", G, xa, precision=EXACT_DOT)
    dx = jnp.einsum("gkts,tgkp->sgkp", mixing, G, precision=EXACT_DOT) + skip[None, :, :, None] * G
    d_sw = d_mix * within
    d_scores = jnp.sum(d_sw * step[:, :, None, :], axis=1)
    dc = jnp.einsum("gts,sgn->tgn", d_scores, ba, precision=EXACT_DOT)
    db = jnp.einsum("gts,tgn->sgn", d_scores, ca, precision=EXACT_DOT)
    grow = jnp.exp(cum)
    g_grow = G * grow.transpose(2, 0, 1)[..., None]
    carried = jnp.einsum("tgn,gkpn->tgkp", ca, S0, precision=EXACT_DOT)
    dc = dc + jnp.einsum("tgkp,gkpn->tgn", g_grow, S0, precision=EXACT_DOT)
    d_cum = jnp.sum(g_grow * carried, axis=-1).transpose(1, 2, 0)
    q_mat = d_mix * score_w
    d_step = jnp.sum(q_mat, axis=-2)
    p_mat = q_mat * step[:, :, None, :]
    d_cum = d_cum + jnp.sum(p_mat, axis=-1) - jnp.sum(p_mat, axis=-2)
    if lam is not None:
        to_end = jnp.exp(cum[..., -1:] - cum)
        push = to_end * step
        lam_b = jnp.einsum("gkpn,sgn->sgkp", lam, ba, precision=EXACT_DOT)
        dx = dx + push.transpose(2, 0, 1)[..., None] * lam_b
        db = db + jnp.einsum("gkpn,sgkp,gks->sgn", lam, xa, push, precision=EXACT_DOT)
        q_end = jnp.sum(xa * lam_b, axis=-1).transpose(1, 2, 0)
        d_step = d_step + to_end * q_end
        wq = push * q_end
        end_total = jnp.sum(wq, axis=-1) + jnp.exp(cum[..., -1]) * jnp.sum(lam * S0, axis=(-2, -1))
        d_cum = d_cum - wq
        d_cum = d_cum.at[..., -1].add(end_total)
    d_log = jnp.flip(jnp.cumsum(jnp.flip(d_cum, -1), axis=-1), -1)
    d_step = d_step - rate[:, :, None] * d_log
    return dx, db, dc, d_step


def shards(
    prefix_x,
    prefix_b,
    prefix_c,
    prefix_dt,
    prefix_grad,
    suffix_x,
    suffix_b,
    suffix_c,
    suffix_dt,
    suffix_grad,
    lengths,
    loss_mask,
    advantage,
    conv_x,
    conv_b,
    conv_c,
    decay_rate,
    dt_bias,
    skip,
):
    num_ways = lax.axis_size("suf")
    my_index = lax.axis_index("suf")
    num_heads = decay_rate.shape[0]
    num_groups = conv_b.shape[1] // N
    per_group = num_heads // num_groups
    margin = KW - 1
    prompt_len = prefix_x.shape[0]
    width_x = prefix_x.shape[1]
    width_b = prefix_b.shape[1]
    rate = decay_rate.reshape(num_groups, per_group)
    gain = skip.reshape(num_groups, per_group)

    def split_tokens(tokens):
        return (
            tokens[:, :width_x],
            tokens[:, width_x : width_x + width_b],
            tokens[:, width_x + width_b :],
        )

    def convs(ux, ub, uc, cx, cb, cc):
        return (
            causal_conv(ux, cx, conv_x),
            causal_conv(ub, cb, conv_b),
            causal_conv(uc, cc, conv_c),
        )

    def softplus_of(raw):
        return jax.nn.softplus(raw + dt_bias[:, None])

    prompt_step, step_pullback = jax.vjp(softplus_of, prefix_dt)
    cumulative = jnp.cumsum(-prompt_step * decay_rate[:, None], axis=1)
    total_log = cumulative[:, -1]
    tails = jnp.concatenate(
        [prefix_x[-margin:], prefix_b[-margin:], prefix_c[-margin:]], axis=1
    ).astype(jnp.float32)
    tail_size = tails.size
    own_pack = jnp.concatenate([tails.reshape(-1), total_log])
    received = [own_pack] + [
        lax.ppermute(own_pack, "suf", [(j, (j + shift) % num_ways) for j in range(num_ways)])
        for shift in range(1, num_ways)
    ]
    every = jnp.take(
        jnp.stack(received), (my_index - jnp.arange(num_ways)) % num_ways, axis=0
    )
    every_tails = every[:, :tail_size].reshape((num_ways,) + tails.shape)
    every_log = every[:, tail_size:]
    behind = lax.dynamic_index_in_dim(every_tails, jnp.maximum(my_index - 1, 0), 0, False)
    behind = jnp.where(my_index > 0, behind, 0.0)
    left_x, left_b, left_c = split_tokens(behind)
    ctx_x, ctx_b, ctx_c = split_tokens(every_tails[num_ways - 1])

    acts, prompt_conv_pullback = jax.vjp(
        convs,
        prefix_x.astype(jnp.float32),
        prefix_b.astype(jnp.float32),
        prefix_c.astype(jnp.float32),
        left_x,
        left_b,
        left_c,
    )
    x_act = acts[0].reshape(prompt_len, num_groups, per_group, HD)
    b_act = acts[1].reshape(prompt_len, num_groups, N)
    c_act = acts[2].reshape(prompt_len, num_groups, N)
    prompt_cot = prefix_grad.astype(jnp.float32).reshape(prompt_len, num_groups, per_group, HD)
    push_weight = (jnp.exp(total_log[:, None] - cumulative) * prompt_step).reshape(
        num_groups, per_group, prompt_len
    )
    own_state = jnp.einsum("gkt,tgkp,tgn->gkpn", push_weight, x_act, b_act, precision=EXACT_DOT)
    pull_weight = jnp.exp(cumulative).reshape(num_groups, per_group, prompt_len)
    own_adjoint = jnp.einsum(
        "gkt,tgkp,tgn->gkpn", pull_weight, prompt_cot, c_act, precision=EXACT_DOT
    )
    every_pair = lax.all_gather(jnp.stack([own_state, own_adjoint]), "suf")
    every_decay = jnp.exp(every_log).reshape(num_ways, num_groups, per_group, 1, 1)
    running = jnp.zeros_like(own_state)
    start_state = running
    for block in range(num_ways):
        start_state = jnp.where(my_index == block, running, start_state)
        running = every_decay[block] * running + every_pair[block, 0]
    prompt_end = running

    positions = jnp.arange(suffix_x.shape[1])[None, :]
    weight = (
        advantage[:, None]
        * loss_mask.astype(jnp.float32)
        * (positions < lengths[:, None]).astype(jnp.float32)
    )

    def one_suffix(x_one, b_one, c_one, dt_one, grad_one, weight_one):
        suffix_len = x_one.shape[0]
        step_one, one_step_pullback = jax.vjp(softplus_of, dt_one)
        s_acts, conv_pullback = jax.vjp(convs, x_one, b_one, c_one, ctx_x, ctx_b, ctx_c)
        sx = s_acts[0].reshape(suffix_len, num_groups, per_group, HD)
        sb = s_acts[1].reshape(suffix_len, num_groups, N)
        sc = s_acts[2].reshape(suffix_len, num_groups, N)
        cot = (weight_one[:, None] * grad_one).reshape(suffix_len, num_groups, per_group, HD)
        step_g = step_one.reshape(num_groups, per_group, suffix_len)
        grow = jnp.exp(jnp.cumsum(-step_g * rate[:, :, None], axis=-1))
        adjoint = jnp.einsum("gkt,tgkp,tgn->gkpn", grow, cot, sc, precision=EXACT_DOT)
        dx, db, dc, d_step = block_grads(sx, sb, sc, step_g, rate, gain, prompt_end, cot, None)
        conv_grads = conv_pullback(
            (dx.reshape(suffix_len, -1), db.reshape(suffix_len, -1), dc.reshape(suffix_len, -1))
        )
        d_dt = one_step_pullback(d_step.reshape(num_heads, suffix_len))[0]
        return conv_grads, d_dt, adjoint

    conv_grads, suffix_ddt, adjoints = jax.vmap(one_suffix, in_axes=(0, 0, 0, 1, 0, 0), out_axes=(0, 1, 0))(
        suffix_x.astype(jnp.float32),
        suffix_b.astype(jnp.float32),
        suffix_c.astype(jnp.float32),
        suffix_dt,
        suffix_grad.astype(jnp.float32),
        weight,
    )
    suffix_total = lax.psum(jnp.sum(adjoints, axis=0), "suf")
    ctx_grads = jnp.concatenate(
        [jnp.sum(conv_grads[3], axis=0), jnp.sum(conv_grads[4], axis=0), jnp.sum(conv_grads[5], axis=0)],
        axis=1,
    )
    from_suffix = ctx_grads
    for sender in range(num_ways - 1):
        from_suffix = from_suffix + lax.ppermute(ctx_grads, "suf", [(sender, num_ways - 1)])
    running = suffix_total
    end_grad = running
    for block in reversed(range(num_ways)):
        end_grad = jnp.where(my_index == block, running, end_grad)
        running = every_pair[block, 1] + every_decay[block] * running

    step_g = prompt_step.reshape(num_groups, per_group, prompt_len)
    dx, db, dc, d_step = block_grads(
        x_act, b_act, c_act, step_g, rate, gain, start_state, prompt_cot, end_grad
    )
    prompt_grads = prompt_conv_pullback(
        (dx.reshape(prompt_len, -1), db.reshape(prompt_len, -1), dc.reshape(prompt_len, -1))
    )
    prefix_ddt = step_pullback(d_step.reshape(num_heads, prompt_len))[0]
    left_grads = jnp.concatenate([prompt_grads[3], prompt_grads[4], prompt_grads[5]], axis=1)
    from_right = from_behind(left_grads, "suf", -1)
    last_device = my_index == num_ways - 1
    tail_add = split_tokens(from_right + jnp.where(last_device, from_suffix, 0.0))

    def finish(grad_full, extra):
        return grad_full.at[-margin:].add(extra).astype(jnp.bfloat16)

    return (
        finish(prompt_grads[0], tail_add[0]),
        finish(prompt_grads[1], tail_add[1]),
        finish(prompt_grads[2], tail_add[2]),
        prefix_ddt,
        conv_grads[0].astype(jnp.bfloat16),
        conv_grads[1].astype(jnp.bfloat16),
        conv_grads[2].astype(jnp.bfloat16),
        suffix_ddt,
    )


def solution(mesh):
    return jax.shard_map(
        shards,
        mesh=mesh,
        in_specs=(
            P(("grp", "suf"), "head"),
            P(("grp", "suf"), "head"),
            P(("grp", "suf"), "head"),
            P("head", ("grp", "suf")),
            P(("grp", "suf"), "head"),
            P(("grp", "suf"), None, "head"),
            P(("grp", "suf"), None, "head"),
            P(("grp", "suf"), None, "head"),
            P("head", ("grp", "suf"), None),
            P(("grp", "suf"), None, "head"),
            P(("grp", "suf")),
            P(("grp", "suf"), None),
            P(("grp", "suf")),
            P(None, "head"),
            P(None, "head"),
            P(None, "head"),
            P("head"),
            P("head"),
            P("head"),
        ),
        out_specs=(
            P(("grp", "suf"), "head"),
            P(("grp", "suf"), "head"),
            P(("grp", "suf"), "head"),
            P("head", ("grp", "suf")),
            P(("grp", "suf"), None, "head"),
            P(("grp", "suf"), None, "head"),
            P(("grp", "suf"), None, "head"),
            P("head", ("grp", "suf"), None),
        ),
        check_vma=False,
    )
```

```python
import jax
import jax.numpy as jnp
from jax import lax
from jax.sharding import PartitionSpec as P

HD = 64
N = 128
KW = 4
Q = 128


EXACT_DOT = lax.Precision.HIGHEST


def from_behind(block, axis, distance):
    devices = range(lax.axis_size(axis))
    route = [(i - distance, i) for i in devices if i - distance in devices]
    return lax.ppermute(block, axis, route)


def prefix(shard, axis, combine, identity, reverse):
    length, here = (lax.axis_size(axis), lax.axis_index(axis))
    everything = jax.tree.map(lambda part: lax.all_gather(part, axis), shard)
    start = jax.tree.map(
        lambda part, zero: jnp.broadcast_to(jnp.asarray(zero, part.dtype), part.shape),
        shard,
        identity,
    )

    def lap(k, before):
        at = length - 1 - k if reverse else k
        reached = at > here if reverse else at < here
        new = combine(before, jax.tree.map(lambda part: part[at], everything))
        return jax.tree.map(lambda a, b: jnp.where(reached, a, b), new, before)

    return lax.fori_loop(0, length, lap, start)


def spread(block, axis, holder):
    block = jnp.where(lax.axis_index(axis) == holder, block, jnp.zeros_like(block))
    return lax.psum(block, axis)


def causal_conv(values, context, taps):
    padded = jnp.concatenate([context, values], axis=0)
    num_tokens = values.shape[0]
    result = padded[0:num_tokens] * taps[0].astype(jnp.float32)
    for tap_index in range(1, taps.shape[0]):
        result = result + padded[tap_index : tap_index + num_tokens] * taps[tap_index].astype(
            jnp.float32
        )
    return jax.nn.silu(result)


def run_scan(x_act, b_act, c_act, step_dt, decay_rates, skip_gain, start_state):
    tokens = x_act.shape[0]
    num_heads = x_act.shape[1]
    num_groups = b_act.shape[1]
    per_group = num_heads // num_groups
    blocks = tokens // Q
    x_blocks = x_act.reshape(blocks, Q, num_groups, per_group, HD)
    b_blocks = b_act.reshape(blocks, Q, num_groups, N)
    c_blocks = c_act.reshape(blocks, Q, num_groups, N)
    log_decay = (
        (-step_dt * decay_rates[:, None])
        .reshape(num_groups, per_group, blocks, Q)
        .transpose(2, 0, 1, 3)
    )
    dt_blocks = step_dt.reshape(num_groups, per_group, blocks, Q).transpose(2, 0, 1, 3)
    lower_tri = jnp.arange(Q)[:, None] >= jnp.arange(Q)[None, :]
    skip_shaped = skip_gain.reshape(num_groups, per_group)[:, :, None]

    def advance(current, pieces):
        x_block, b_block, c_block, log_block, dt_block = pieces
        cumulative = jnp.cumsum(log_block, axis=-1)
        log_gaps = cumulative[..., :, None] - cumulative[..., None, :]
        within = jnp.where(lower_tri, jnp.exp(jnp.where(lower_tri, log_gaps, 0.0)), 0.0)
        scores = jnp.einsum("tgn,sgn->gts", c_block, b_block, precision=EXACT_DOT)
        mixing = scores[:, None] * within * dt_block[:, :, None, :]
        inner_out = jnp.einsum("gkts,sgkp->tgkp", mixing, x_block, precision=EXACT_DOT)
        carried = jnp.einsum("tgn,gkpn->tgkp", c_block, current, precision=EXACT_DOT)
        carried = carried * jnp.exp(cumulative).transpose(2, 0, 1)[..., None]
        output = inner_out + carried + skip_shaped * x_block
        weights = jnp.exp(cumulative[..., -1:] - cumulative) * dt_block
        updated = current * jnp.exp(cumulative[..., -1])[..., None, None]
        updated = updated + jnp.einsum(
            "gks,sgkp,sgn->gkpn", weights, x_block, b_block, precision=EXACT_DOT
        )
        return (updated, output)

    last_state, outputs = lax.scan(
        jax.checkpoint(advance),
        start_state.reshape(num_groups, per_group, HD, N),
        (x_blocks, b_blocks, c_blocks, log_decay, dt_blocks),
    )
    return (outputs.reshape(tokens, num_heads * HD), last_state.reshape(num_heads, HD, N))


def block_forward(x_feat, b_feat, c_feat, dt_raw, left_x, left_b, left_c, start_state, params):
    conv_x, conv_b, conv_c, decay_rates, dt_offset, skip_gain = params
    num_heads = decay_rates.shape[0]
    num_groups = conv_b.shape[1] // N
    x_act = causal_conv(x_feat, left_x, conv_x).reshape(-1, num_heads, HD)
    b_act = causal_conv(b_feat, left_b, conv_b).reshape(-1, num_groups, N)
    c_act = causal_conv(c_feat, left_c, conv_c).reshape(-1, num_groups, N)
    step_dt = jax.nn.softplus(dt_raw + dt_offset[:, None])
    return run_scan(x_act, b_act, c_act, step_dt, decay_rates, skip_gain, start_state)


def block_grads(xa, ba, ca, step, rate, skip, S0, G, lam):
    T = xa.shape[0]
    tri = jnp.arange(T)[:, None] >= jnp.arange(T)[None, :]
    cum = jnp.cumsum(-step * rate[:, :, None], axis=-1)
    gaps = cum[..., :, None] - cum[..., None, :]
    within = jnp.where(tri, jnp.exp(jnp.where(tri, gaps, 0.0)), 0.0)
    scores = jnp.einsum("tgn,sgn->gts", ca, ba, precision=EXACT_DOT)
    score_w = scores[:, None] * within
    mixing = score_w * step[:, :, None, :]
    d_mix = jnp.einsum("tgkp,sgkp->gkts", G, xa, precision=EXACT_DOT)
    dx = jnp.einsum("gkts,tgkp->sgkp", mixing, G, precision=EXACT_DOT) + skip[None, :, :, None] * G
    d_sw = d_mix * within
    d_scores = jnp.sum(d_sw * step[:, :, None, :], axis=1)
    dc = jnp.einsum("gts,sgn->tgn", d_scores, ba, precision=EXACT_DOT)
    db = jnp.einsum("gts,tgn->sgn", d_scores, ca, precision=EXACT_DOT)
    grow = jnp.exp(cum)
    g_grow = G * grow.transpose(2, 0, 1)[..., None]
    carried = jnp.einsum("tgn,gkpn->tgkp", ca, S0, precision=EXACT_DOT)
    dc = dc + jnp.einsum("tgkp,gkpn->tgn", g_grow, S0, precision=EXACT_DOT)
    d_cum = jnp.sum(g_grow * carried, axis=-1).transpose(1, 2, 0)
    q_mat = d_mix * score_w
    d_step = jnp.sum(q_mat, axis=-2)
    p_mat = q_mat * step[:, :, None, :]
    d_cum = d_cum + jnp.sum(p_mat, axis=-1) - jnp.sum(p_mat, axis=-2)
    if lam is not None:
        to_end = jnp.exp(cum[..., -1:] - cum)
        push = to_end * step
        lam_b = jnp.einsum("gkpn,sgn->sgkp", lam, ba, precision=EXACT_DOT)
        dx = dx + push.transpose(2, 0, 1)[..., None] * lam_b
        db = db + jnp.einsum("gkpn,sgkp,gks->sgn", lam, xa, push, precision=EXACT_DOT)
        q_end = jnp.sum(xa * lam_b, axis=-1).transpose(1, 2, 0)
        d_step = d_step + to_end * q_end
        wq = push * q_end
        end_total = jnp.sum(wq, axis=-1) + jnp.exp(cum[..., -1]) * jnp.sum(lam * S0, axis=(-2, -1))
        d_cum = d_cum - wq
        d_cum = d_cum.at[..., -1].add(end_total)
    d_log = jnp.flip(jnp.cumsum(jnp.flip(d_cum, -1), axis=-1), -1)
    d_step = d_step - rate[:, :, None] * d_log
    return dx, db, dc, d_step


def shards(
    prefix_x,
    prefix_b,
    prefix_c,
    prefix_dt,
    prefix_grad,
    suffix_x,
    suffix_b,
    suffix_c,
    suffix_dt,
    suffix_grad,
    lengths,
    loss_mask,
    advantage,
    conv_x,
    conv_b,
    conv_c,
    decay_rate,
    dt_bias,
    skip,
):
    num_ways = lax.axis_size("suf")
    my_index = lax.axis_index("suf")
    num_heads = decay_rate.shape[0]
    num_groups = conv_b.shape[1] // N
    per_group = num_heads // num_groups
    margin = KW - 1
    prompt_len = prefix_x.shape[0]
    width_x = prefix_x.shape[1]
    width_b = prefix_b.shape[1]
    rate = decay_rate.reshape(num_groups, per_group)
    gain = skip.reshape(num_groups, per_group)

    def split_tokens(tokens):
        return (
            tokens[:, :width_x],
            tokens[:, width_x : width_x + width_b],
            tokens[:, width_x + width_b :],
        )

    def convs(ux, ub, uc, cx, cb, cc):
        return (
            causal_conv(ux, cx, conv_x),
            causal_conv(ub, cb, conv_b),
            causal_conv(uc, cc, conv_c),
        )

    def softplus_of(raw):
        return jax.nn.softplus(raw + dt_bias[:, None])

    prompt_step, step_pullback = jax.vjp(softplus_of, prefix_dt)
    cumulative = jnp.cumsum(-prompt_step * decay_rate[:, None], axis=1)
    total_log = cumulative[:, -1]
    tails = jnp.concatenate(
        [prefix_x[-margin:], prefix_b[-margin:], prefix_c[-margin:]], axis=1
    ).astype(jnp.float32)
    tail_size = tails.size
    own_pack = jnp.concatenate([tails.reshape(-1), total_log])
    received = [own_pack] + [
        lax.ppermute(own_pack, "suf", [(j, (j + shift) % num_ways) for j in range(num_ways)])
        for shift in range(1, num_ways)
    ]
    every = jnp.take(
        jnp.stack(received), (my_index - jnp.arange(num_ways)) % num_ways, axis=0
    )
    every_tails = every[:, :tail_size].reshape((num_ways,) + tails.shape)
    every_log = every[:, tail_size:]
    behind = lax.dynamic_index_in_dim(every_tails, jnp.maximum(my_index - 1, 0), 0, False)
    behind = jnp.where(my_index > 0, behind, 0.0)
    left_x, left_b, left_c = split_tokens(behind)
    ctx_x, ctx_b, ctx_c = split_tokens(every_tails[num_ways - 1])

    acts, prompt_conv_pullback = jax.vjp(
        convs,
        prefix_x.astype(jnp.float32),
        prefix_b.astype(jnp.float32),
        prefix_c.astype(jnp.float32),
        left_x,
        left_b,
        left_c,
    )
    x_act = acts[0].reshape(prompt_len, num_groups, per_group, HD)
    b_act = acts[1].reshape(prompt_len, num_groups, N)
    c_act = acts[2].reshape(prompt_len, num_groups, N)
    prompt_cot = prefix_grad.astype(jnp.float32).reshape(prompt_len, num_groups, per_group, HD)
    push_weight = (jnp.exp(total_log[:, None] - cumulative) * prompt_step).reshape(
        num_groups, per_group, prompt_len
    )
    own_state = jnp.einsum("gkt,tgkp,tgn->gkpn", push_weight, x_act, b_act, precision=EXACT_DOT)
    pull_weight = jnp.exp(cumulative).reshape(num_groups, per_group, prompt_len)
    own_adjoint = jnp.einsum(
        "gkt,tgkp,tgn->gkpn", pull_weight, prompt_cot, c_act, precision=EXACT_DOT
    )
    positions = jnp.arange(suffix_x.shape[1])[None, :]
    weight = (
        advantage[:, None]
        * loss_mask.astype(jnp.float32)
        * (positions < lengths[:, None]).astype(jnp.float32)
    )

    def suffix_parts(x_one, b_one, c_one, dt_one, grad_one, weight_one):
        suffix_len = x_one.shape[0]
        step_one, one_step_pullback = jax.vjp(softplus_of, dt_one)
        s_acts, conv_pullback = jax.vjp(convs, x_one, b_one, c_one, ctx_x, ctx_b, ctx_c)
        sx = s_acts[0].reshape(suffix_len, num_groups, per_group, HD)
        sb = s_acts[1].reshape(suffix_len, num_groups, N)
        sc = s_acts[2].reshape(suffix_len, num_groups, N)
        cot = (weight_one[:, None] * grad_one).reshape(suffix_len, num_groups, per_group, HD)
        step_g = step_one.reshape(num_groups, per_group, suffix_len)
        return one_step_pullback, conv_pullback, sx, sb, sc, cot, step_g

    def suffix_front(*items):
        unused_a, unused_b, sx, sb, sc, cot, step_g = suffix_parts(*items)
        grow = jnp.exp(jnp.cumsum(-step_g * rate[:, :, None], axis=-1))
        return jnp.einsum("gkt,tgkp,tgn->gkpn", grow, cot, sc, precision=EXACT_DOT)

    def suffix_back(end_state, *items):
        one_step_pullback, conv_pullback, sx, sb, sc, cot, step_g = suffix_parts(*items)
        suffix_len = sx.shape[0]
        dx, db, dc, d_step = block_grads(sx, sb, sc, step_g, rate, gain, end_state, cot, None)
        conv_grads = conv_pullback(
            (dx.reshape(suffix_len, -1), db.reshape(suffix_len, -1), dc.reshape(suffix_len, -1))
        )
        d_dt = one_step_pullback(d_step.reshape(num_heads, suffix_len))[0]
        return conv_grads, d_dt

    suffix_items = (
        suffix_x.astype(jnp.float32),
        suffix_b.astype(jnp.float32),
        suffix_c.astype(jnp.float32),
        suffix_dt,
        suffix_grad.astype(jnp.float32),
        weight,
    )
    adjoints = jax.vmap(suffix_front, in_axes=(0, 0, 0, 1, 0, 0))(*suffix_items)
    core = my_index % 2
    chip = my_index // 2
    num_chips = num_ways // 2
    own_triple = jnp.stack([own_state, own_adjoint, jnp.sum(adjoints, axis=0)])
    partner_triple = lax.ppermute(own_triple, "suf", [(j, j ^ 1) for j in range(num_ways)])
    even = jnp.where(core == 0, own_triple, partner_triple)
    odd = jnp.where(core == 0, partner_triple, own_triple)
    block_decay = jnp.exp(every_log).reshape(num_ways, num_groups, per_group, 1, 1)
    decay_even = lax.dynamic_index_in_dim(block_decay, 2 * chip, 0, False)
    decay_odd = lax.dynamic_index_in_dim(block_decay, 2 * chip + 1, 0, False)
    chip_log = every_log.reshape(num_chips, 2, num_heads).sum(axis=1)
    later_log = jnp.sum(jnp.where((jnp.arange(num_chips) >= chip)[:, None], chip_log, 0.0), axis=0)
    chip_state = decay_odd * even[0] + odd[0]
    chip_adjoint = even[1] + decay_even * odd[1]
    chip_suffix = even[2] + odd[2]
    chip_later = chip_adjoint + jnp.exp(later_log).reshape(num_groups, per_group, 1, 1) * chip_suffix
    got_state = [chip_state]
    got_other = [chip_suffix]
    for shift in range(1, num_chips):
        wraps = chip + shift >= num_chips
        outgoing = jnp.where(core == 0, chip_state, jnp.where(wraps, chip_later, chip_suffix))
        route = [
            (2 * c + k, 2 * ((c + shift) % num_chips) + k) for c in range(num_chips) for k in range(2)
        ]
        incoming = lax.ppermute(outgoing, "suf", route)
        shared = lax.ppermute(incoming, "suf", [(j, j ^ 1) for j in range(num_ways)])
        got_state.append(jnp.where(core == 0, incoming, shared))
        got_other.append(jnp.where(core == 0, shared, incoming))
    order = (chip - jnp.arange(num_chips)) % num_chips
    chip_states = jnp.take(jnp.stack(got_state), order, axis=0)
    chip_others = jnp.take(jnp.stack(got_other), order, axis=0)
    chip_decay = jnp.exp(chip_log).reshape(num_chips, num_groups, per_group, 1, 1)
    running = jnp.zeros_like(own_state)
    chip_start = running
    for c in range(num_chips):
        chip_start = jnp.where(chip == c, running, chip_start)
        running = chip_decay[c] * running + chip_states[c]
    prompt_end_late = running
    running = jnp.sum(
        jnp.where((jnp.arange(num_chips) <= chip).reshape(num_chips, 1, 1, 1, 1), chip_others, 0.0),
        axis=0,
    )
    chip_end_grad = running
    for c in reversed(range(num_chips)):
        chip_end_grad = jnp.where(chip == c, running, chip_end_grad)
        running = chip_others[c] + chip_decay[c] * running
    start_state = jnp.where(core == 0, chip_start, decay_even * chip_start + even[0])
    end_grad = jnp.where(core == 0, odd[1] + decay_odd * chip_end_grad, chip_end_grad)
    conv_grads, suffix_ddt = jax.vmap(
        suffix_back, in_axes=(None, 0, 0, 0, 1, 0, 0), out_axes=(0, 1)
    )(prompt_end_late, *suffix_items)
    step_g = prompt_step.reshape(num_groups, per_group, prompt_len)
    dx, db, dc, d_step = block_grads(
        x_act, b_act, c_act, step_g, rate, gain, start_state, prompt_cot, end_grad
    )
    prompt_grads = prompt_conv_pullback(
        (dx.reshape(prompt_len, -1), db.reshape(prompt_len, -1), dc.reshape(prompt_len, -1))
    )
    prefix_ddt = step_pullback(d_step.reshape(num_heads, prompt_len))[0]
    left_grads = jnp.concatenate([prompt_grads[3], prompt_grads[4], prompt_grads[5]], axis=1)
    from_right = from_behind(left_grads, "suf", -1)
    ctx_grads = jnp.concatenate(
        [jnp.sum(conv_grads[3], axis=0), jnp.sum(conv_grads[4], axis=0), jnp.sum(conv_grads[5], axis=0)],
        axis=1,
    )
    from_suffix = ctx_grads
    for sender in range(num_ways - 1):
        from_suffix = from_suffix + lax.ppermute(ctx_grads, "suf", [(sender, num_ways - 1)])
    last_device = my_index == num_ways - 1
    tail_add = split_tokens(from_right + jnp.where(last_device, from_suffix, 0.0))

    def finish(grad_full, extra):
        return grad_full.at[-margin:].add(extra).astype(jnp.bfloat16)

    return (
        finish(prompt_grads[0], tail_add[0]),
        finish(prompt_grads[1], tail_add[1]),
        finish(prompt_grads[2], tail_add[2]),
        prefix_ddt,
        conv_grads[0].astype(jnp.bfloat16),
        conv_grads[1].astype(jnp.bfloat16),
        conv_grads[2].astype(jnp.bfloat16),
        suffix_ddt,
    )


def solution(mesh):
    return jax.shard_map(
        shards,
        mesh=mesh,
        in_specs=(
            P(("grp", "suf"), "head"),
            P(("grp", "suf"), "head"),
            P(("grp", "suf"), "head"),
            P("head", ("grp", "suf")),
            P(("grp", "suf"), "head"),
            P(("grp", "suf"), None, "head"),
            P(("grp", "suf"), None, "head"),
            P(("grp", "suf"), None, "head"),
            P("head", ("grp", "suf"), None),
            P(("grp", "suf"), None, "head"),
            P(("grp", "suf")),
            P(("grp", "suf"), None),
            P(("grp", "suf")),
            P(None, "head"),
            P(None, "head"),
            P(None, "head"),
            P("head"),
            P("head"),
            P("head"),
        ),
        out_specs=(
            P(("grp", "suf"), "head"),
            P(("grp", "suf"), "head"),
            P(("grp", "suf"), "head"),
            P("head", ("grp", "suf")),
            P(("grp", "suf"), None, "head"),
            P(("grp", "suf"), None, "head"),
            P(("grp", "suf"), None, "head"),
            P("head", ("grp", "suf"), None),
        ),
        check_vma=False,
    )
```

```python
import functools

import jax
import jax.numpy as jnp
from jax import lax
from jax.experimental import pallas as pl
from jax.sharding import PartitionSpec as P

HD = 64
N = 128
KW = 4
Q = 128


EXACT_DOT = lax.Precision.HIGHEST


def from_behind(block, axis, distance):
    devices = range(lax.axis_size(axis))
    route = [(i - distance, i) for i in devices if i - distance in devices]
    return lax.ppermute(block, axis, route)


def prefix(shard, axis, combine, identity, reverse):
    length, here = (lax.axis_size(axis), lax.axis_index(axis))
    everything = jax.tree.map(lambda part: lax.all_gather(part, axis), shard)
    start = jax.tree.map(
        lambda part, zero: jnp.broadcast_to(jnp.asarray(zero, part.dtype), part.shape),
        shard,
        identity,
    )

    def lap(k, before):
        at = length - 1 - k if reverse else k
        reached = at > here if reverse else at < here
        new = combine(before, jax.tree.map(lambda part: part[at], everything))
        return jax.tree.map(lambda a, b: jnp.where(reached, a, b), new, before)

    return lax.fori_loop(0, length, lap, start)


def spread(block, axis, holder):
    block = jnp.where(lax.axis_index(axis) == holder, block, jnp.zeros_like(block))
    return lax.psum(block, axis)


def causal_conv(values, context, taps):
    padded = jnp.concatenate([context, values], axis=0)
    num_tokens = values.shape[0]
    result = padded[0:num_tokens] * taps[0].astype(jnp.float32)
    for tap_index in range(1, taps.shape[0]):
        result = result + padded[tap_index : tap_index + num_tokens] * taps[tap_index].astype(
            jnp.float32
        )
    return jax.nn.silu(result)


def run_scan(x_act, b_act, c_act, step_dt, decay_rates, skip_gain, start_state):
    tokens = x_act.shape[0]
    num_heads = x_act.shape[1]
    num_groups = b_act.shape[1]
    per_group = num_heads // num_groups
    blocks = tokens // Q
    x_blocks = x_act.reshape(blocks, Q, num_groups, per_group, HD)
    b_blocks = b_act.reshape(blocks, Q, num_groups, N)
    c_blocks = c_act.reshape(blocks, Q, num_groups, N)
    log_decay = (
        (-step_dt * decay_rates[:, None])
        .reshape(num_groups, per_group, blocks, Q)
        .transpose(2, 0, 1, 3)
    )
    dt_blocks = step_dt.reshape(num_groups, per_group, blocks, Q).transpose(2, 0, 1, 3)
    lower_tri = jnp.arange(Q)[:, None] >= jnp.arange(Q)[None, :]
    skip_shaped = skip_gain.reshape(num_groups, per_group)[:, :, None]

    def advance(current, pieces):
        x_block, b_block, c_block, log_block, dt_block = pieces
        cumulative = jnp.cumsum(log_block, axis=-1)
        log_gaps = cumulative[..., :, None] - cumulative[..., None, :]
        within = jnp.where(lower_tri, jnp.exp(jnp.where(lower_tri, log_gaps, 0.0)), 0.0)
        scores = jnp.einsum("tgn,sgn->gts", c_block, b_block, precision=EXACT_DOT)
        mixing = scores[:, None] * within * dt_block[:, :, None, :]
        inner_out = jnp.einsum("gkts,sgkp->tgkp", mixing, x_block, precision=EXACT_DOT)
        carried = jnp.einsum("tgn,gkpn->tgkp", c_block, current, precision=EXACT_DOT)
        carried = carried * jnp.exp(cumulative).transpose(2, 0, 1)[..., None]
        output = inner_out + carried + skip_shaped * x_block
        weights = jnp.exp(cumulative[..., -1:] - cumulative) * dt_block
        updated = current * jnp.exp(cumulative[..., -1])[..., None, None]
        updated = updated + jnp.einsum(
            "gks,sgkp,sgn->gkpn", weights, x_block, b_block, precision=EXACT_DOT
        )
        return (updated, output)

    last_state, outputs = lax.scan(
        jax.checkpoint(advance),
        start_state.reshape(num_groups, per_group, HD, N),
        (x_blocks, b_blocks, c_blocks, log_decay, dt_blocks),
    )
    return (outputs.reshape(tokens, num_heads * HD), last_state.reshape(num_heads, HD, N))


def block_forward(x_feat, b_feat, c_feat, dt_raw, left_x, left_b, left_c, start_state, params):
    conv_x, conv_b, conv_c, decay_rates, dt_offset, skip_gain = params
    num_heads = decay_rates.shape[0]
    num_groups = conv_b.shape[1] // N
    x_act = causal_conv(x_feat, left_x, conv_x).reshape(-1, num_heads, HD)
    b_act = causal_conv(b_feat, left_b, conv_b).reshape(-1, num_groups, N)
    c_act = causal_conv(c_feat, left_c, conv_c).reshape(-1, num_groups, N)
    step_dt = jax.nn.softplus(dt_raw + dt_offset[:, None])
    return run_scan(x_act, b_act, c_act, step_dt, decay_rates, skip_gain, start_state)


def block_grads(xa, ba, ca, step, rate, skip, S0, G, lam):
    T = xa.shape[0]
    tri = jnp.arange(T)[:, None] >= jnp.arange(T)[None, :]
    cum = jnp.cumsum(-step * rate[:, :, None], axis=-1)
    gaps = cum[..., :, None] - cum[..., None, :]
    within = jnp.where(tri, jnp.exp(jnp.where(tri, gaps, 0.0)), 0.0)
    scores = jnp.einsum("tgn,sgn->gts", ca, ba, precision=EXACT_DOT)
    score_w = scores[:, None] * within
    mixing = score_w * step[:, :, None, :]
    d_mix = jnp.einsum("tgkp,sgkp->gkts", G, xa, precision=EXACT_DOT)
    dx = jnp.einsum("gkts,tgkp->sgkp", mixing, G, precision=EXACT_DOT) + skip[None, :, :, None] * G
    d_sw = d_mix * within
    d_scores = jnp.sum(d_sw * step[:, :, None, :], axis=1)
    dc = jnp.einsum("gts,sgn->tgn", d_scores, ba, precision=EXACT_DOT)
    db = jnp.einsum("gts,tgn->sgn", d_scores, ca, precision=EXACT_DOT)
    grow = jnp.exp(cum)
    g_grow = G * grow.transpose(2, 0, 1)[..., None]
    carried = jnp.einsum("tgn,gkpn->tgkp", ca, S0, precision=EXACT_DOT)
    dc = dc + jnp.einsum("tgkp,gkpn->tgn", g_grow, S0, precision=EXACT_DOT)
    d_cum = jnp.sum(g_grow * carried, axis=-1).transpose(1, 2, 0)
    q_mat = d_mix * score_w
    d_step = jnp.sum(q_mat, axis=-2)
    p_mat = q_mat * step[:, :, None, :]
    d_cum = d_cum + jnp.sum(p_mat, axis=-1) - jnp.sum(p_mat, axis=-2)
    if lam is not None:
        to_end = jnp.exp(cum[..., -1:] - cum)
        push = to_end * step
        lam_b = jnp.einsum("gkpn,sgn->sgkp", lam, ba, precision=EXACT_DOT)
        dx = dx + push.transpose(2, 0, 1)[..., None] * lam_b
        db = db + jnp.einsum("gkpn,sgkp,gks->sgn", lam, xa, push, precision=EXACT_DOT)
        q_end = jnp.sum(xa * lam_b, axis=-1).transpose(1, 2, 0)
        d_step = d_step + to_end * q_end
        wq = push * q_end
        end_total = jnp.sum(wq, axis=-1) + jnp.exp(cum[..., -1]) * jnp.sum(lam * S0, axis=(-2, -1))
        d_cum = d_cum - wq
        d_cum = d_cum.at[..., -1].add(end_total)
    d_log = jnp.flip(jnp.cumsum(jnp.flip(d_cum, -1), axis=-1), -1)
    d_step = d_step - rate[:, :, None] * d_log
    return dx, db, dc, d_step


def _dot(a, b, dims):
    return lax.dot_general(a, b, (dims, ((), ())), precision=EXACT_DOT, preferred_element_type=jnp.float32)


def _grad_kernel(with_end, per_group_pairs, x_ref, g_ref, b_ref, c_ref, crow_ref, ccol_ref, srow_ref, lane_ref,
                 s0_ref, lam_ref, dx_ref, dstep_ref, dcum_ref, qend_ref, dsc_ref, dcc_ref, dbe_ref):
    step_id = pl.program_id(0)
    x = x_ref[...]
    g = g_ref[...]
    bb = b_ref[...]
    cc = c_ref[...]
    t_len = x.shape[0]
    tri = lax.broadcasted_iota(jnp.int32, (t_len, t_len), 0) >= lax.broadcasted_iota(jnp.int32, (t_len, t_len), 1)
    lane = lax.broadcasted_iota(jnp.int32, (1, 2 * HD), 1)
    ones = jnp.ones((8, t_len), jnp.float32)
    scores = _dot(cc, bb, ((1,), (1,)))
    s0 = s0_ref[0]
    carried = _dot(cc, s0, ((1,), (1,)))
    grow_l = lane_ref[0, 0]
    push_l = lane_ref[0, 1]
    g_grow = g * grow_l
    dcc = _dot(g_grow, s0, ((1,), (0,)))
    gc = g_grow * carried
    dx = jnp.zeros_like(x)
    dsc = jnp.zeros((t_len, t_len), jnp.float32)
    if with_end:
        lam = lam_ref[0]
        lam_b = _dot(bb, lam, ((1,), (1,)))
        dx = dx + push_l * lam_b
        dbe = _dot(push_l * x, lam, ((1,), (0,)))
        xl = x * lam_b
    for h in range(2):
        mask = ((lane >= h * HD) & (lane < (h + 1) * HD)).astype(jnp.float32)
        gm = g * mask
        crow = crow_ref[0, h : h + 1, :]
        ccol = ccol_ref[0, :, h : h + 1]
        srow = srow_ref[0, h : h + 1, :]
        within = jnp.where(tri, jnp.exp(jnp.where(tri, ccol - crow, 0.0)), 0.0)
        score_w = scores * within
        mixing = score_w * srow
        d_mix = _dot(gm, x, ((1,), (1,)))
        dx = dx + _dot(mixing, gm, ((0,), (0,)))
        d_sw = d_mix * within
        dsc = dsc + d_sw * srow
        q_mat = d_mix * score_w
        p_mat = q_mat * srow
        mask8 = jnp.broadcast_to(mask, (8, 2 * HD))
        d_cum = _dot(ones, p_mat, ((1,), (1,)))[0:1] - jnp.sum(p_mat, axis=0, keepdims=True)
        d_cum = d_cum + _dot(mask8, gc, ((1,), (1,)))[0:1]
        dstep_ref[0, h : h + 1, :] = jnp.sum(q_mat, axis=0, keepdims=True)
        dcum_ref[0, h : h + 1, :] = d_cum
        if with_end:
            qend_ref[0, h : h + 1, :] = _dot(mask8, xl, ((1,), (1,)))[0:1]
        else:
            qend_ref[0, h : h + 1, :] = jnp.zeros((1, t_len), jnp.float32)
    dx_ref[...] = dx
    first = step_id % per_group_pairs == 0

    @pl.when(first)
    def _():
        dsc_ref[0] = dsc
        dcc_ref[...] = dcc
        dbe_ref[...] = dbe if with_end else jnp.zeros_like(dcc)

    @pl.when(jnp.logical_not(first))
    def _():
        dsc_ref[0] += dsc
        dcc_ref[...] += dcc
        if with_end:
            dbe_ref[...] += dbe


def block_grads_kernel(xa, ba, ca, step, rate, skip, S0, G, lam):
    T, ng, nk, P = xa.shape
    nh = ng * nk
    pairs = nh // 2
    per_group_pairs = nk // 2
    cum = jnp.cumsum(-step * rate[:, :, None], axis=-1).reshape(pairs, 2, T)
    steps = step.reshape(pairs, 2, T)
    ccol = jnp.swapaxes(cum, 1, 2)
    grow = jnp.exp(cum)
    to_end = jnp.exp(cum[..., -1:] - cum)
    push = to_end * steps

    def lanes(v):
        return jnp.repeat(jnp.swapaxes(v, 1, 2), P, axis=2)

    lane_w = jnp.stack([lanes(grow), lanes(push)], axis=1)
    s0 = S0.reshape(pairs, 2 * P, N)
    lm = (lam if lam is not None else S0).reshape(pairs, 2 * P, N)
    x2 = xa.reshape(T, nh * P)
    g2 = G.reshape(T, nh * P)
    b2 = ba.reshape(T, ng * N)
    c2 = ca.reshape(T, ng * N)
    row_spec = pl.BlockSpec((1, 2, T), lambda j: (j, 0, 0))
    lane_spec = pl.BlockSpec((T, 2 * P), lambda j: (0, j))
    grp_spec = pl.BlockSpec((T, N), lambda j: (0, j // per_group_pairs))
    outs = pl.pallas_call(
        functools.partial(_grad_kernel, lam is not None, per_group_pairs),
        grid=(pairs,),
        in_specs=[
            lane_spec, lane_spec, grp_spec, grp_spec, row_spec,
            pl.BlockSpec((1, T, 2), lambda j: (j, 0, 0)), row_spec,
            pl.BlockSpec((1, 2, T, 2 * P), lambda j: (j, 0, 0, 0)),
            pl.BlockSpec((1, 2 * P, N), lambda j: (j, 0, 0)),
            pl.BlockSpec((1, 2 * P, N), lambda j: (j, 0, 0)),
        ],
        out_specs=[
            lane_spec, row_spec, row_spec, row_spec,
            pl.BlockSpec((1, T, T), lambda j: (j // per_group_pairs, 0, 0)),
            grp_spec, grp_spec,
        ],
        out_shape=[
            jax.ShapeDtypeStruct((T, nh * P), jnp.float32),
            jax.ShapeDtypeStruct((pairs, 2, T), jnp.float32),
            jax.ShapeDtypeStruct((pairs, 2, T), jnp.float32),
            jax.ShapeDtypeStruct((pairs, 2, T), jnp.float32),
            jax.ShapeDtypeStruct((ng, T, T), jnp.float32),
            jax.ShapeDtypeStruct((T, ng * N), jnp.float32),
            jax.ShapeDtypeStruct((T, ng * N), jnp.float32),
        ],
    )(x2, g2, b2, c2, cum, ccol, steps, lane_w, s0, lm)
    dx2, d_direct, d_cum, q_end, d_scores, dcc, dbe = outs
    dx = dx2.reshape(T, ng, nk, P) + skip[None, :, :, None] * G
    dc = jnp.einsum("gts,sgn->tgn", d_scores, ba, precision=EXACT_DOT) + dcc.reshape(T, ng, N)
    db = jnp.einsum("gts,tgn->sgn", d_scores, ca, precision=EXACT_DOT)
    d_direct = d_direct.reshape(ng, nk, T)
    d_cum = d_cum.reshape(ng, nk, T)
    cum = cum.reshape(ng, nk, T)
    if lam is not None:
        db = db + dbe.reshape(T, ng, N)
        q_end = q_end.reshape(ng, nk, T)
        to_end = to_end.reshape(ng, nk, T)
        push = push.reshape(ng, nk, T)
        d_direct = d_direct + to_end * q_end
        wq = push * q_end
        end_total = jnp.sum(wq, axis=-1) + jnp.exp(cum[..., -1]) * jnp.sum(lam * S0, axis=(-2, -1))
        d_cum = d_cum - wq
        d_cum = d_cum.at[..., -1].add(end_total)
    d_log = jnp.flip(jnp.cumsum(jnp.flip(d_cum, -1), axis=-1), -1)
    d_step = d_direct - rate[:, :, None] * d_log
    return dx, db, dc, d_step


def shards(
    prefix_x,
    prefix_b,
    prefix_c,
    prefix_dt,
    prefix_grad,
    suffix_x,
    suffix_b,
    suffix_c,
    suffix_dt,
    suffix_grad,
    lengths,
    loss_mask,
    advantage,
    conv_x,
    conv_b,
    conv_c,
    decay_rate,
    dt_bias,
    skip,
):
    num_ways = lax.axis_size("suf")
    my_index = lax.axis_index("suf")
    num_heads = decay_rate.shape[0]
    num_groups = conv_b.shape[1] // N
    per_group = num_heads // num_groups
    margin = KW - 1
    prompt_len = prefix_x.shape[0]
    width_x = prefix_x.shape[1]
    width_b = prefix_b.shape[1]
    rate = decay_rate.reshape(num_groups, per_group)
    gain = skip.reshape(num_groups, per_group)

    def split_tokens(tokens):
        return (
            tokens[:, :width_x],
            tokens[:, width_x : width_x + width_b],
            tokens[:, width_x + width_b :],
        )

    def convs(ux, ub, uc, cx, cb, cc):
        return (
            causal_conv(ux, cx, conv_x),
            causal_conv(ub, cb, conv_b),
            causal_conv(uc, cc, conv_c),
        )

    def softplus_of(raw):
        return jax.nn.softplus(raw + dt_bias[:, None])

    prompt_step, step_pullback = jax.vjp(softplus_of, prefix_dt)
    cumulative = jnp.cumsum(-prompt_step * decay_rate[:, None], axis=1)
    total_log = cumulative[:, -1]
    tails = jnp.concatenate(
        [prefix_x[-margin:], prefix_b[-margin:], prefix_c[-margin:]], axis=1
    ).astype(jnp.float32)
    tail_size = tails.size
    own_pack = jnp.concatenate([tails.reshape(-1), total_log])
    received = [own_pack] + [
        lax.ppermute(own_pack, "suf", [(j, (j + shift) % num_ways) for j in range(num_ways)])
        for shift in range(1, num_ways)
    ]
    every = jnp.take(
        jnp.stack(received), (my_index - jnp.arange(num_ways)) % num_ways, axis=0
    )
    every_tails = every[:, :tail_size].reshape((num_ways,) + tails.shape)
    every_log = every[:, tail_size:]
    behind = lax.dynamic_index_in_dim(every_tails, jnp.maximum(my_index - 1, 0), 0, False)
    behind = jnp.where(my_index > 0, behind, 0.0)
    left_x, left_b, left_c = split_tokens(behind)
    ctx_x, ctx_b, ctx_c = split_tokens(every_tails[num_ways - 1])

    acts, prompt_conv_pullback = jax.vjp(
        convs,
        prefix_x.astype(jnp.float32),
        prefix_b.astype(jnp.float32),
        prefix_c.astype(jnp.float32),
        left_x,
        left_b,
        left_c,
    )
    x_act = acts[0].reshape(prompt_len, num_groups, per_group, HD)
    b_act = acts[1].reshape(prompt_len, num_groups, N)
    c_act = acts[2].reshape(prompt_len, num_groups, N)
    prompt_cot = prefix_grad.astype(jnp.float32).reshape(prompt_len, num_groups, per_group, HD)
    push_weight = (jnp.exp(total_log[:, None] - cumulative) * prompt_step).reshape(
        num_groups, per_group, prompt_len
    )
    own_state = jnp.einsum("gkt,tgkp,tgn->gkpn", push_weight, x_act, b_act, precision=EXACT_DOT)
    pull_weight = jnp.exp(cumulative).reshape(num_groups, per_group, prompt_len)
    own_adjoint = jnp.einsum(
        "gkt,tgkp,tgn->gkpn", pull_weight, prompt_cot, c_act, precision=EXACT_DOT
    )
    positions = jnp.arange(suffix_x.shape[1])[None, :]
    weight = (
        advantage[:, None]
        * loss_mask.astype(jnp.float32)
        * (positions < lengths[:, None]).astype(jnp.float32)
    )

    def suffix_parts(x_one, b_one, c_one, dt_one, grad_one, weight_one):
        suffix_len = x_one.shape[0]
        step_one, one_step_pullback = jax.vjp(softplus_of, dt_one)
        s_acts, conv_pullback = jax.vjp(convs, x_one, b_one, c_one, ctx_x, ctx_b, ctx_c)
        sx = s_acts[0].reshape(suffix_len, num_groups, per_group, HD)
        sb = s_acts[1].reshape(suffix_len, num_groups, N)
        sc = s_acts[2].reshape(suffix_len, num_groups, N)
        cot = (weight_one[:, None] * grad_one).reshape(suffix_len, num_groups, per_group, HD)
        step_g = step_one.reshape(num_groups, per_group, suffix_len)
        return one_step_pullback, conv_pullback, sx, sb, sc, cot, step_g

    def suffix_front(*items):
        unused_a, unused_b, sx, sb, sc, cot, step_g = suffix_parts(*items)
        grow = jnp.exp(jnp.cumsum(-step_g * rate[:, :, None], axis=-1))
        return jnp.einsum("gkt,tgkp,tgn->gkpn", grow, cot, sc, precision=EXACT_DOT)

    def suffix_back(end_state, *items):
        one_step_pullback, conv_pullback, sx, sb, sc, cot, step_g = suffix_parts(*items)
        suffix_len = sx.shape[0]
        dx, db, dc, d_step = block_grads_kernel(sx, sb, sc, step_g, rate, gain, end_state, cot, None)
        conv_grads = conv_pullback(
            (dx.reshape(suffix_len, -1), db.reshape(suffix_len, -1), dc.reshape(suffix_len, -1))
        )
        d_dt = one_step_pullback(d_step.reshape(num_heads, suffix_len))[0]
        return conv_grads, d_dt

    suffix_items = (
        suffix_x.astype(jnp.float32),
        suffix_b.astype(jnp.float32),
        suffix_c.astype(jnp.float32),
        suffix_dt,
        suffix_grad.astype(jnp.float32),
        weight,
    )
    adjoints = jax.vmap(suffix_front, in_axes=(0, 0, 0, 1, 0, 0))(*suffix_items)
    core = my_index % 2
    chip = my_index // 2
    num_chips = num_ways // 2
    own_triple = jnp.stack([own_state, own_adjoint, jnp.sum(adjoints, axis=0)])
    partner_triple = lax.ppermute(own_triple, "suf", [(j, j ^ 1) for j in range(num_ways)])
    even = jnp.where(core == 0, own_triple, partner_triple)
    odd = jnp.where(core == 0, partner_triple, own_triple)
    block_decay = jnp.exp(every_log).reshape(num_ways, num_groups, per_group, 1, 1)
    decay_even = lax.dynamic_index_in_dim(block_decay, 2 * chip, 0, False)
    decay_odd = lax.dynamic_index_in_dim(block_decay, 2 * chip + 1, 0, False)
    chip_log = every_log.reshape(num_chips, 2, num_heads).sum(axis=1)
    later_log = jnp.sum(jnp.where((jnp.arange(num_chips) >= chip)[:, None], chip_log, 0.0), axis=0)
    chip_state = decay_odd * even[0] + odd[0]
    chip_adjoint = even[1] + decay_even * odd[1]
    chip_suffix = even[2] + odd[2]
    chip_later = chip_adjoint + jnp.exp(later_log).reshape(num_groups, per_group, 1, 1) * chip_suffix
    got_state = [chip_state]
    got_other = [chip_suffix]
    for shift in range(1, num_chips):
        wraps = chip + shift >= num_chips
        outgoing = jnp.where(core == 0, chip_state, jnp.where(wraps, chip_later, chip_suffix))
        route = [
            (2 * c + k, 2 * ((c + shift) % num_chips) + k) for c in range(num_chips) for k in range(2)
        ]
        incoming = lax.ppermute(outgoing, "suf", route)
        shared = lax.ppermute(incoming, "suf", [(j, j ^ 1) for j in range(num_ways)])
        got_state.append(jnp.where(core == 0, incoming, shared))
        got_other.append(jnp.where(core == 0, shared, incoming))
    order = (chip - jnp.arange(num_chips)) % num_chips
    chip_states = jnp.take(jnp.stack(got_state), order, axis=0)
    chip_others = jnp.take(jnp.stack(got_other), order, axis=0)
    chip_decay = jnp.exp(chip_log).reshape(num_chips, num_groups, per_group, 1, 1)
    running = jnp.zeros_like(own_state)
    chip_start = running
    for c in range(num_chips):
        chip_start = jnp.where(chip == c, running, chip_start)
        running = chip_decay[c] * running + chip_states[c]
    prompt_end_late = running
    running = jnp.sum(
        jnp.where((jnp.arange(num_chips) <= chip).reshape(num_chips, 1, 1, 1, 1), chip_others, 0.0),
        axis=0,
    )
    chip_end_grad = running
    for c in reversed(range(num_chips)):
        chip_end_grad = jnp.where(chip == c, running, chip_end_grad)
        running = chip_others[c] + chip_decay[c] * running
    start_state = jnp.where(core == 0, chip_start, decay_even * chip_start + even[0])
    end_grad = jnp.where(core == 0, odd[1] + decay_odd * chip_end_grad, chip_end_grad)
    conv_grads, suffix_ddt = jax.vmap(
        suffix_back, in_axes=(None, 0, 0, 0, 1, 0, 0), out_axes=(0, 1)
    )(prompt_end_late, *suffix_items)
    step_g = prompt_step.reshape(num_groups, per_group, prompt_len)
    dx, db, dc, d_step = block_grads_kernel(
        x_act, b_act, c_act, step_g, rate, gain, start_state, prompt_cot, end_grad
    )
    prompt_grads = prompt_conv_pullback(
        (dx.reshape(prompt_len, -1), db.reshape(prompt_len, -1), dc.reshape(prompt_len, -1))
    )
    prefix_ddt = step_pullback(d_step.reshape(num_heads, prompt_len))[0]
    left_grads = jnp.concatenate([prompt_grads[3], prompt_grads[4], prompt_grads[5]], axis=1)
    from_right = from_behind(left_grads, "suf", -1)
    ctx_grads = jnp.concatenate(
        [jnp.sum(conv_grads[3], axis=0), jnp.sum(conv_grads[4], axis=0), jnp.sum(conv_grads[5], axis=0)],
        axis=1,
    )
    from_suffix = ctx_grads
    for sender in range(num_ways - 1):
        from_suffix = from_suffix + lax.ppermute(ctx_grads, "suf", [(sender, num_ways - 1)])
    last_device = my_index == num_ways - 1
    tail_add = split_tokens(from_right + jnp.where(last_device, from_suffix, 0.0))

    def finish(grad_full, extra):
        return grad_full.at[-margin:].add(extra).astype(jnp.bfloat16)

    return (
        finish(prompt_grads[0], tail_add[0]),
        finish(prompt_grads[1], tail_add[1]),
        finish(prompt_grads[2], tail_add[2]),
        prefix_ddt,
        conv_grads[0].astype(jnp.bfloat16),
        conv_grads[1].astype(jnp.bfloat16),
        conv_grads[2].astype(jnp.bfloat16),
        suffix_ddt,
    )


def solution(mesh):
    return jax.shard_map(
        shards,
        mesh=mesh,
        in_specs=(
            P(("grp", "suf"), "head"),
            P(("grp", "suf"), "head"),
            P(("grp", "suf"), "head"),
            P("head", ("grp", "suf")),
            P(("grp", "suf"), "head"),
            P(("grp", "suf"), None, "head"),
            P(("grp", "suf"), None, "head"),
            P(("grp", "suf"), None, "head"),
            P("head", ("grp", "suf"), None),
            P(("grp", "suf"), None, "head"),
            P(("grp", "suf")),
            P(("grp", "suf"), None),
            P(("grp", "suf")),
            P(None, "head"),
            P(None, "head"),
            P(None, "head"),
            P("head"),
            P("head"),
            P("head"),
        ),
        out_specs=(
            P(("grp", "suf"), "head"),
            P(("grp", "suf"), "head"),
            P(("grp", "suf"), "head"),
            P("head", ("grp", "suf")),
            P(("grp", "suf"), None, "head"),
            P(("grp", "suf"), None, "head"),
            P(("grp", "suf"), None, "head"),
            P("head", ("grp", "suf"), None),
        ),
        check_vma=False,
    )
```

```python
import functools

import jax
import jax.numpy as jnp
from jax import lax
from jax.experimental import pallas as pl
from jax.sharding import PartitionSpec as P

HD = 64
N = 128
KW = 4
Q = 128


EXACT_DOT = lax.Precision.HIGHEST


def from_behind(block, axis, distance):
    devices = range(lax.axis_size(axis))
    route = [(i - distance, i) for i in devices if i - distance in devices]
    return lax.ppermute(block, axis, route)


def prefix(shard, axis, combine, identity, reverse):
    length, here = (lax.axis_size(axis), lax.axis_index(axis))
    everything = jax.tree.map(lambda part: lax.all_gather(part, axis), shard)
    start = jax.tree.map(
        lambda part, zero: jnp.broadcast_to(jnp.asarray(zero, part.dtype), part.shape),
        shard,
        identity,
    )

    def lap(k, before):
        at = length - 1 - k if reverse else k
        reached = at > here if reverse else at < here
        new = combine(before, jax.tree.map(lambda part: part[at], everything))
        return jax.tree.map(lambda a, b: jnp.where(reached, a, b), new, before)

    return lax.fori_loop(0, length, lap, start)


def spread(block, axis, holder):
    block = jnp.where(lax.axis_index(axis) == holder, block, jnp.zeros_like(block))
    return lax.psum(block, axis)


def causal_conv(values, context, taps):
    padded = jnp.concatenate([context, values], axis=0)
    num_tokens = values.shape[0]
    result = padded[0:num_tokens] * taps[0].astype(jnp.float32)
    for tap_index in range(1, taps.shape[0]):
        result = result + padded[tap_index : tap_index + num_tokens] * taps[tap_index].astype(
            jnp.float32
        )
    return jax.nn.silu(result)


def run_scan(x_act, b_act, c_act, step_dt, decay_rates, skip_gain, start_state):
    tokens = x_act.shape[0]
    num_heads = x_act.shape[1]
    num_groups = b_act.shape[1]
    per_group = num_heads // num_groups
    blocks = tokens // Q
    x_blocks = x_act.reshape(blocks, Q, num_groups, per_group, HD)
    b_blocks = b_act.reshape(blocks, Q, num_groups, N)
    c_blocks = c_act.reshape(blocks, Q, num_groups, N)
    log_decay = (
        (-step_dt * decay_rates[:, None])
        .reshape(num_groups, per_group, blocks, Q)
        .transpose(2, 0, 1, 3)
    )
    dt_blocks = step_dt.reshape(num_groups, per_group, blocks, Q).transpose(2, 0, 1, 3)
    lower_tri = jnp.arange(Q)[:, None] >= jnp.arange(Q)[None, :]
    skip_shaped = skip_gain.reshape(num_groups, per_group)[:, :, None]

    def advance(current, pieces):
        x_block, b_block, c_block, log_block, dt_block = pieces
        cumulative = jnp.cumsum(log_block, axis=-1)
        log_gaps = cumulative[..., :, None] - cumulative[..., None, :]
        within = jnp.where(lower_tri, jnp.exp(jnp.where(lower_tri, log_gaps, 0.0)), 0.0)
        scores = jnp.einsum("tgn,sgn->gts", c_block, b_block, precision=EXACT_DOT)
        mixing = scores[:, None] * within * dt_block[:, :, None, :]
        inner_out = jnp.einsum("gkts,sgkp->tgkp", mixing, x_block, precision=EXACT_DOT)
        carried = jnp.einsum("tgn,gkpn->tgkp", c_block, current, precision=EXACT_DOT)
        carried = carried * jnp.exp(cumulative).transpose(2, 0, 1)[..., None]
        output = inner_out + carried + skip_shaped * x_block
        weights = jnp.exp(cumulative[..., -1:] - cumulative) * dt_block
        updated = current * jnp.exp(cumulative[..., -1])[..., None, None]
        updated = updated + jnp.einsum(
            "gks,sgkp,sgn->gkpn", weights, x_block, b_block, precision=EXACT_DOT
        )
        return (updated, output)

    last_state, outputs = lax.scan(
        jax.checkpoint(advance),
        start_state.reshape(num_groups, per_group, HD, N),
        (x_blocks, b_blocks, c_blocks, log_decay, dt_blocks),
    )
    return (outputs.reshape(tokens, num_heads * HD), last_state.reshape(num_heads, HD, N))


def block_forward(x_feat, b_feat, c_feat, dt_raw, left_x, left_b, left_c, start_state, params):
    conv_x, conv_b, conv_c, decay_rates, dt_offset, skip_gain = params
    num_heads = decay_rates.shape[0]
    num_groups = conv_b.shape[1] // N
    x_act = causal_conv(x_feat, left_x, conv_x).reshape(-1, num_heads, HD)
    b_act = causal_conv(b_feat, left_b, conv_b).reshape(-1, num_groups, N)
    c_act = causal_conv(c_feat, left_c, conv_c).reshape(-1, num_groups, N)
    step_dt = jax.nn.softplus(dt_raw + dt_offset[:, None])
    return run_scan(x_act, b_act, c_act, step_dt, decay_rates, skip_gain, start_state)


def _dot(a, b, dims):
    return lax.dot_general(a, b, (dims, ((), ())), precision=EXACT_DOT, preferred_element_type=jnp.float32)


def _grad_kernel(per_group_pairs, x_ref, g_ref, b_ref, c_ref, crow_ref, ccol_ref, srow_ref,
                 dx_ref, dstep_ref, dcum_ref, dsc_ref):
    step_id = pl.program_id(0)
    x = x_ref[...]
    g = g_ref[...]
    t_len = x.shape[0]
    tri = lax.broadcasted_iota(jnp.int32, (t_len, t_len), 0) >= lax.broadcasted_iota(jnp.int32, (t_len, t_len), 1)
    lane = lax.broadcasted_iota(jnp.int32, (1, 2 * HD), 1)
    ones = jnp.ones((8, t_len), jnp.float32)
    scores = _dot(c_ref[...], b_ref[...], ((1,), (1,)))
    dx = jnp.zeros_like(x)
    dsc = jnp.zeros((t_len, t_len), jnp.float32)
    for h in range(2):
        mask = ((lane >= h * HD) & (lane < (h + 1) * HD)).astype(jnp.float32)
        gm = g * mask
        crow = crow_ref[0, h : h + 1, :]
        ccol = ccol_ref[0, :, h : h + 1]
        srow = srow_ref[0, h : h + 1, :]
        within = jnp.where(tri, jnp.exp(jnp.where(tri, ccol - crow, 0.0)), 0.0)
        score_w = scores * within
        d_mix = _dot(gm, x, ((1,), (1,)))
        dx = dx + _dot(score_w * srow, gm, ((0,), (0,)))
        dsc = dsc + d_mix * within * srow
        q_mat = d_mix * score_w
        p_mat = q_mat * srow
        dstep_ref[0, h : h + 1, :] = jnp.sum(q_mat, axis=0, keepdims=True)
        dcum_ref[0, h : h + 1, :] = _dot(ones, p_mat, ((1,), (1,)))[0:1] - jnp.sum(
            p_mat, axis=0, keepdims=True
        )
    dx_ref[...] = dx
    first = step_id % per_group_pairs == 0

    @pl.when(first)
    def _():
        dsc_ref[0] = dsc

    @pl.when(jnp.logical_not(first))
    def _():
        dsc_ref[0] += dsc


def block_inner(xa, ba, ca, step, rate, G):
    T, ng, nk, P = xa.shape
    nh = ng * nk
    pairs = nh // 2
    per_group_pairs = nk // 2
    cum = jnp.cumsum(-step * rate[:, :, None], axis=-1)
    cum_pairs = cum.reshape(pairs, 2, T)
    row_spec = pl.BlockSpec((1, 2, T), lambda j: (j, 0, 0))
    lane_spec = pl.BlockSpec((T, 2 * P), lambda j: (0, j))
    grp_spec = pl.BlockSpec((T, N), lambda j: (0, j // per_group_pairs))
    dx2, d_direct, d_cum, d_scores = pl.pallas_call(
        functools.partial(_grad_kernel, per_group_pairs),
        grid=(pairs,),
        in_specs=[
            lane_spec, lane_spec, grp_spec, grp_spec, row_spec,
            pl.BlockSpec((1, T, 2), lambda j: (j, 0, 0)), row_spec,
        ],
        out_specs=[
            lane_spec, row_spec, row_spec,
            pl.BlockSpec((1, T, T), lambda j: (j // per_group_pairs, 0, 0)),
        ],
        out_shape=[
            jax.ShapeDtypeStruct((T, nh * P), jnp.float32),
            jax.ShapeDtypeStruct((pairs, 2, T), jnp.float32),
            jax.ShapeDtypeStruct((pairs, 2, T), jnp.float32),
            jax.ShapeDtypeStruct((ng, T, T), jnp.float32),
        ],
    )(
        xa.reshape(T, nh * P),
        G.reshape(T, nh * P),
        ba.reshape(T, ng * N),
        ca.reshape(T, ng * N),
        cum_pairs,
        jnp.swapaxes(cum_pairs, 1, 2),
        step.reshape(pairs, 2, T),
    )
    return (
        dx2.reshape(T, ng, nk, P),
        d_direct.reshape(ng, nk, T),
        d_cum.reshape(ng, nk, T),
        d_scores,
        cum,
    )


def block_outer(inner, xa, ba, ca, step, rate, skip, S0, G, lam):
    dx, d_step, d_cum, d_scores, cum = inner
    dx = dx + skip[None, :, :, None] * G
    dc = jnp.einsum("gts,sgn->tgn", d_scores, ba, precision=EXACT_DOT)
    db = jnp.einsum("gts,tgn->sgn", d_scores, ca, precision=EXACT_DOT)
    grow = jnp.exp(cum)
    g_grow = G * grow.transpose(2, 0, 1)[..., None]
    carried = jnp.einsum("tgn,gkpn->tgkp", ca, S0, precision=EXACT_DOT)
    dc = dc + jnp.einsum("tgkp,gkpn->tgn", g_grow, S0, precision=EXACT_DOT)
    d_cum = d_cum + jnp.sum(g_grow * carried, axis=-1).transpose(1, 2, 0)
    if lam is not None:
        to_end = jnp.exp(cum[..., -1:] - cum)
        push = to_end * step
        lam_b = jnp.einsum("gkpn,sgn->sgkp", lam, ba, precision=EXACT_DOT)
        dx = dx + push.transpose(2, 0, 1)[..., None] * lam_b
        db = db + jnp.einsum("gkpn,sgkp,gks->sgn", lam, xa, push, precision=EXACT_DOT)
        q_end = jnp.sum(xa * lam_b, axis=-1).transpose(1, 2, 0)
        d_step = d_step + to_end * q_end
        wq = push * q_end
        end_total = jnp.sum(wq, axis=-1) + jnp.exp(cum[..., -1]) * jnp.sum(lam * S0, axis=(-2, -1))
        d_cum = d_cum - wq
        d_cum = d_cum.at[..., -1].add(end_total)
    d_log = jnp.flip(jnp.cumsum(jnp.flip(d_cum, -1), axis=-1), -1)
    d_step = d_step - rate[:, :, None] * d_log
    return dx, db, dc, d_step


def shards(
    prefix_x,
    prefix_b,
    prefix_c,
    prefix_dt,
    prefix_grad,
    suffix_x,
    suffix_b,
    suffix_c,
    suffix_dt,
    suffix_grad,
    lengths,
    loss_mask,
    advantage,
    conv_x,
    conv_b,
    conv_c,
    decay_rate,
    dt_bias,
    skip,
):
    num_ways = lax.axis_size("suf")
    my_index = lax.axis_index("suf")
    num_heads = decay_rate.shape[0]
    num_groups = conv_b.shape[1] // N
    per_group = num_heads // num_groups
    margin = KW - 1
    prompt_len = prefix_x.shape[0]
    width_x = prefix_x.shape[1]
    width_b = prefix_b.shape[1]
    rate = decay_rate.reshape(num_groups, per_group)
    gain = skip.reshape(num_groups, per_group)

    def split_tokens(tokens):
        return (
            tokens[:, :width_x],
            tokens[:, width_x : width_x + width_b],
            tokens[:, width_x + width_b :],
        )

    def convs(ux, ub, uc, cx, cb, cc):
        return (
            causal_conv(ux, cx, conv_x),
            causal_conv(ub, cb, conv_b),
            causal_conv(uc, cc, conv_c),
        )

    def softplus_of(raw):
        return jax.nn.softplus(raw + dt_bias[:, None])

    prompt_step, step_pullback = jax.vjp(softplus_of, prefix_dt)
    cumulative = jnp.cumsum(-prompt_step * decay_rate[:, None], axis=1)
    total_log = cumulative[:, -1]
    tails = jnp.concatenate(
        [prefix_x[-margin:], prefix_b[-margin:], prefix_c[-margin:]], axis=1
    ).astype(jnp.float32)
    tail_size = tails.size
    own_pack = jnp.concatenate([tails.reshape(-1), total_log])
    received = [own_pack] + [
        lax.ppermute(own_pack, "suf", [(j, (j + shift) % num_ways) for j in range(num_ways)])
        for shift in range(1, num_ways)
    ]
    every = jnp.take(
        jnp.stack(received), (my_index - jnp.arange(num_ways)) % num_ways, axis=0
    )
    every_tails = every[:, :tail_size].reshape((num_ways,) + tails.shape)
    every_log = every[:, tail_size:]
    behind = lax.dynamic_index_in_dim(every_tails, jnp.maximum(my_index - 1, 0), 0, False)
    behind = jnp.where(my_index > 0, behind, 0.0)
    left_x, left_b, left_c = split_tokens(behind)
    ctx_x, ctx_b, ctx_c = split_tokens(every_tails[num_ways - 1])

    acts, prompt_conv_pullback = jax.vjp(
        convs,
        prefix_x.astype(jnp.float32),
        prefix_b.astype(jnp.float32),
        prefix_c.astype(jnp.float32),
        left_x,
        left_b,
        left_c,
    )
    x_act = acts[0].reshape(prompt_len, num_groups, per_group, HD)
    b_act = acts[1].reshape(prompt_len, num_groups, N)
    c_act = acts[2].reshape(prompt_len, num_groups, N)
    prompt_cot = prefix_grad.astype(jnp.float32).reshape(prompt_len, num_groups, per_group, HD)
    push_weight = (jnp.exp(total_log[:, None] - cumulative) * prompt_step).reshape(
        num_groups, per_group, prompt_len
    )
    own_state = jnp.einsum("gkt,tgkp,tgn->gkpn", push_weight, x_act, b_act, precision=EXACT_DOT)
    pull_weight = jnp.exp(cumulative).reshape(num_groups, per_group, prompt_len)
    own_adjoint = jnp.einsum(
        "gkt,tgkp,tgn->gkpn", pull_weight, prompt_cot, c_act, precision=EXACT_DOT
    )
    positions = jnp.arange(suffix_x.shape[1])[None, :]
    weight = (
        advantage[:, None]
        * loss_mask.astype(jnp.float32)
        * (positions < lengths[:, None]).astype(jnp.float32)
    )

    def suffix_parts(x_one, b_one, c_one, dt_one, grad_one, weight_one):
        suffix_len = x_one.shape[0]
        step_one, one_step_pullback = jax.vjp(softplus_of, dt_one)
        s_acts, conv_pullback = jax.vjp(convs, x_one, b_one, c_one, ctx_x, ctx_b, ctx_c)
        sx = s_acts[0].reshape(suffix_len, num_groups, per_group, HD)
        sb = s_acts[1].reshape(suffix_len, num_groups, N)
        sc = s_acts[2].reshape(suffix_len, num_groups, N)
        cot = (weight_one[:, None] * grad_one).reshape(suffix_len, num_groups, per_group, HD)
        step_g = step_one.reshape(num_groups, per_group, suffix_len)
        return one_step_pullback, conv_pullback, sx, sb, sc, cot, step_g

    def suffix_front(*items):
        unused_a, unused_b, sx, sb, sc, cot, step_g = suffix_parts(*items)
        grow = jnp.exp(jnp.cumsum(-step_g * rate[:, :, None], axis=-1))
        adjoint = jnp.einsum("gkt,tgkp,tgn->gkpn", grow, cot, sc, precision=EXACT_DOT)
        return adjoint, block_inner(sx, sb, sc, step_g, rate, cot)

    def suffix_back(end_state, inner, *items):
        one_step_pullback, conv_pullback, sx, sb, sc, cot, step_g = suffix_parts(*items)
        suffix_len = sx.shape[0]
        dx, db, dc, d_step = block_outer(inner, sx, sb, sc, step_g, rate, gain, end_state, cot, None)
        conv_grads = conv_pullback(
            (dx.reshape(suffix_len, -1), db.reshape(suffix_len, -1), dc.reshape(suffix_len, -1))
        )
        d_dt = one_step_pullback(d_step.reshape(num_heads, suffix_len))[0]
        return conv_grads, d_dt

    suffix_items = (
        suffix_x.astype(jnp.float32),
        suffix_b.astype(jnp.float32),
        suffix_c.astype(jnp.float32),
        suffix_dt,
        suffix_grad.astype(jnp.float32),
        weight,
    )
    adjoints, suffix_inner = jax.vmap(suffix_front, in_axes=(0, 0, 0, 1, 0, 0))(*suffix_items)
    step_g = prompt_step.reshape(num_groups, per_group, prompt_len)
    prompt_inner = block_inner(x_act, b_act, c_act, step_g, rate, prompt_cot)
    core = my_index % 2
    chip = my_index // 2
    num_chips = num_ways // 2
    own_triple = jnp.stack([own_state, own_adjoint, jnp.sum(adjoints, axis=0)])
    partner_triple = lax.ppermute(own_triple, "suf", [(j, j ^ 1) for j in range(num_ways)])
    even = jnp.where(core == 0, own_triple, partner_triple)
    odd = jnp.where(core == 0, partner_triple, own_triple)
    block_decay = jnp.exp(every_log).reshape(num_ways, num_groups, per_group, 1, 1)
    decay_even = lax.dynamic_index_in_dim(block_decay, 2 * chip, 0, False)
    decay_odd = lax.dynamic_index_in_dim(block_decay, 2 * chip + 1, 0, False)
    chip_log = every_log.reshape(num_chips, 2, num_heads).sum(axis=1)
    later_log = jnp.sum(jnp.where((jnp.arange(num_chips) >= chip)[:, None], chip_log, 0.0), axis=0)
    chip_state = decay_odd * even[0] + odd[0]
    chip_adjoint = even[1] + decay_even * odd[1]
    chip_suffix = even[2] + odd[2]
    chip_later = chip_adjoint + jnp.exp(later_log).reshape(num_groups, per_group, 1, 1) * chip_suffix
    got_state = [chip_state]
    got_other = [chip_suffix]
    for shift in range(1, num_chips):
        wraps = chip + shift >= num_chips
        outgoing = jnp.where(core == 0, chip_state, jnp.where(wraps, chip_later, chip_suffix))
        route = [
            (2 * c + k, 2 * ((c + shift) % num_chips) + k) for c in range(num_chips) for k in range(2)
        ]
        incoming = lax.ppermute(outgoing, "suf", route)
        shared = lax.ppermute(incoming, "suf", [(j, j ^ 1) for j in range(num_ways)])
        got_state.append(jnp.where(core == 0, incoming, shared))
        got_other.append(jnp.where(core == 0, shared, incoming))
    order = (chip - jnp.arange(num_chips)) % num_chips
    chip_states = jnp.take(jnp.stack(got_state), order, axis=0)
    chip_others = jnp.take(jnp.stack(got_other), order, axis=0)
    chip_decay = jnp.exp(chip_log).reshape(num_chips, num_groups, per_group, 1, 1)
    running = jnp.zeros_like(own_state)
    chip_start = running
    for c in range(num_chips):
        chip_start = jnp.where(chip == c, running, chip_start)
        running = chip_decay[c] * running + chip_states[c]
    prompt_end_late = running
    running = jnp.sum(
        jnp.where((jnp.arange(num_chips) <= chip).reshape(num_chips, 1, 1, 1, 1), chip_others, 0.0),
        axis=0,
    )
    chip_end_grad = running
    for c in reversed(range(num_chips)):
        chip_end_grad = jnp.where(chip == c, running, chip_end_grad)
        running = chip_others[c] + chip_decay[c] * running
    start_state = jnp.where(core == 0, chip_start, decay_even * chip_start + even[0])
    end_grad = jnp.where(core == 0, odd[1] + decay_odd * chip_end_grad, chip_end_grad)
    conv_grads, suffix_ddt = jax.vmap(
        suffix_back, in_axes=(None, 0, 0, 0, 0, 1, 0, 0), out_axes=(0, 1)
    )(prompt_end_late, suffix_inner, *suffix_items)
    dx, db, dc, d_step = block_outer(
        prompt_inner, x_act, b_act, c_act, step_g, rate, gain, start_state, prompt_cot, end_grad
    )
    prompt_grads = prompt_conv_pullback(
        (dx.reshape(prompt_len, -1), db.reshape(prompt_len, -1), dc.reshape(prompt_len, -1))
    )
    prefix_ddt = step_pullback(d_step.reshape(num_heads, prompt_len))[0]
    left_grads = jnp.concatenate([prompt_grads[3], prompt_grads[4], prompt_grads[5]], axis=1)
    from_right = from_behind(left_grads, "suf", -1)
    ctx_grads = jnp.concatenate(
        [jnp.sum(conv_grads[3], axis=0), jnp.sum(conv_grads[4], axis=0), jnp.sum(conv_grads[5], axis=0)],
        axis=1,
    )
    from_suffix = ctx_grads
    for sender in range(num_ways - 1):
        from_suffix = from_suffix + lax.ppermute(ctx_grads, "suf", [(sender, num_ways - 1)])
    last_device = my_index == num_ways - 1
    tail_add = split_tokens(from_right + jnp.where(last_device, from_suffix, 0.0))

    def finish(grad_full, extra):
        return grad_full.at[-margin:].add(extra).astype(jnp.bfloat16)

    return (
        finish(prompt_grads[0], tail_add[0]),
        finish(prompt_grads[1], tail_add[1]),
        finish(prompt_grads[2], tail_add[2]),
        prefix_ddt,
        conv_grads[0].astype(jnp.bfloat16),
        conv_grads[1].astype(jnp.bfloat16),
        conv_grads[2].astype(jnp.bfloat16),
        suffix_ddt,
    )


def solution(mesh):
    return jax.shard_map(
        shards,
        mesh=mesh,
        in_specs=(
            P(("grp", "suf"), "head"),
            P(("grp", "suf"), "head"),
            P(("grp", "suf"), "head"),
            P("head", ("grp", "suf")),
            P(("grp", "suf"), "head"),
            P(("grp", "suf"), None, "head"),
            P(("grp", "suf"), None, "head"),
            P(("grp", "suf"), None, "head"),
            P("head", ("grp", "suf"), None),
            P(("grp", "suf"), None, "head"),
            P(("grp", "suf")),
            P(("grp", "suf"), None),
            P(("grp", "suf")),
            P(None, "head"),
            P(None, "head"),
            P(None, "head"),
            P("head"),
            P("head"),
            P("head"),
        ),
        out_specs=(
            P(("grp", "suf"), "head"),
            P(("grp", "suf"), "head"),
            P(("grp", "suf"), "head"),
            P("head", ("grp", "suf")),
            P(("grp", "suf"), None, "head"),
            P(("grp", "suf"), None, "head"),
            P(("grp", "suf"), None, "head"),
            P("head", ("grp", "suf"), None),
        ),
        check_vma=False,
    )
```

```python
import functools

import jax
import jax.numpy as jnp
from jax import lax
from jax.experimental import pallas as pl
from jax.sharding import PartitionSpec as P

HD = 64
N = 128
KW = 4
Q = 128


EXACT_DOT = lax.Precision.HIGHEST


def from_behind(block, axis, distance):
    devices = range(lax.axis_size(axis))
    route = [(i - distance, i) for i in devices if i - distance in devices]
    return lax.ppermute(block, axis, route)


def prefix(shard, axis, combine, identity, reverse):
    length, here = (lax.axis_size(axis), lax.axis_index(axis))
    everything = jax.tree.map(lambda part: lax.all_gather(part, axis), shard)
    start = jax.tree.map(
        lambda part, zero: jnp.broadcast_to(jnp.asarray(zero, part.dtype), part.shape),
        shard,
        identity,
    )

    def lap(k, before):
        at = length - 1 - k if reverse else k
        reached = at > here if reverse else at < here
        new = combine(before, jax.tree.map(lambda part: part[at], everything))
        return jax.tree.map(lambda a, b: jnp.where(reached, a, b), new, before)

    return lax.fori_loop(0, length, lap, start)


def spread(block, axis, holder):
    block = jnp.where(lax.axis_index(axis) == holder, block, jnp.zeros_like(block))
    return lax.psum(block, axis)


def causal_conv(values, context, taps):
    padded = jnp.concatenate([context, values], axis=0)
    num_tokens = values.shape[0]
    result = padded[0:num_tokens] * taps[0].astype(jnp.float32)
    for tap_index in range(1, taps.shape[0]):
        result = result + padded[tap_index : tap_index + num_tokens] * taps[tap_index].astype(
            jnp.float32
        )
    return jax.nn.silu(result)


def run_scan(x_act, b_act, c_act, step_dt, decay_rates, skip_gain, start_state):
    tokens = x_act.shape[0]
    num_heads = x_act.shape[1]
    num_groups = b_act.shape[1]
    per_group = num_heads // num_groups
    blocks = tokens // Q
    x_blocks = x_act.reshape(blocks, Q, num_groups, per_group, HD)
    b_blocks = b_act.reshape(blocks, Q, num_groups, N)
    c_blocks = c_act.reshape(blocks, Q, num_groups, N)
    log_decay = (
        (-step_dt * decay_rates[:, None])
        .reshape(num_groups, per_group, blocks, Q)
        .transpose(2, 0, 1, 3)
    )
    dt_blocks = step_dt.reshape(num_groups, per_group, blocks, Q).transpose(2, 0, 1, 3)
    lower_tri = jnp.arange(Q)[:, None] >= jnp.arange(Q)[None, :]
    skip_shaped = skip_gain.reshape(num_groups, per_group)[:, :, None]

    def advance(current, pieces):
        x_block, b_block, c_block, log_block, dt_block = pieces
        cumulative = jnp.cumsum(log_block, axis=-1)
        log_gaps = cumulative[..., :, None] - cumulative[..., None, :]
        within = jnp.where(lower_tri, jnp.exp(jnp.where(lower_tri, log_gaps, 0.0)), 0.0)
        scores = jnp.einsum("tgn,sgn->gts", c_block, b_block, precision=EXACT_DOT)
        mixing = scores[:, None] * within * dt_block[:, :, None, :]
        inner_out = jnp.einsum("gkts,sgkp->tgkp", mixing, x_block, precision=EXACT_DOT)
        carried = jnp.einsum("tgn,gkpn->tgkp", c_block, current, precision=EXACT_DOT)
        carried = carried * jnp.exp(cumulative).transpose(2, 0, 1)[..., None]
        output = inner_out + carried + skip_shaped * x_block
        weights = jnp.exp(cumulative[..., -1:] - cumulative) * dt_block
        updated = current * jnp.exp(cumulative[..., -1])[..., None, None]
        updated = updated + jnp.einsum(
            "gks,sgkp,sgn->gkpn", weights, x_block, b_block, precision=EXACT_DOT
        )
        return (updated, output)

    last_state, outputs = lax.scan(
        jax.checkpoint(advance),
        start_state.reshape(num_groups, per_group, HD, N),
        (x_blocks, b_blocks, c_blocks, log_decay, dt_blocks),
    )
    return (outputs.reshape(tokens, num_heads * HD), last_state.reshape(num_heads, HD, N))


def block_forward(x_feat, b_feat, c_feat, dt_raw, left_x, left_b, left_c, start_state, params):
    conv_x, conv_b, conv_c, decay_rates, dt_offset, skip_gain = params
    num_heads = decay_rates.shape[0]
    num_groups = conv_b.shape[1] // N
    x_act = causal_conv(x_feat, left_x, conv_x).reshape(-1, num_heads, HD)
    b_act = causal_conv(b_feat, left_b, conv_b).reshape(-1, num_groups, N)
    c_act = causal_conv(c_feat, left_c, conv_c).reshape(-1, num_groups, N)
    step_dt = jax.nn.softplus(dt_raw + dt_offset[:, None])
    return run_scan(x_act, b_act, c_act, step_dt, decay_rates, skip_gain, start_state)


def _dot(a, b, dims):
    return lax.dot_general(a, b, (dims, ((), ())), precision=EXACT_DOT, preferred_element_type=jnp.float32)


def _grad_kernel(per_group_pairs, x_ref, g_ref, b_ref, c_ref, crow_ref, ccol_ref, srow_ref,
                 dx_ref, dstep_ref, dcum_ref, dsc_ref):
    step_id = pl.program_id(0)
    x = x_ref[...]
    g = g_ref[...]
    t_len = x.shape[0]
    tri = lax.broadcasted_iota(jnp.int32, (t_len, t_len), 0) >= lax.broadcasted_iota(jnp.int32, (t_len, t_len), 1)
    lane = lax.broadcasted_iota(jnp.int32, (1, 2 * HD), 1)
    ones = jnp.ones((8, t_len), jnp.float32)
    scores = _dot(c_ref[...], b_ref[...], ((1,), (1,)))
    dx = jnp.zeros_like(x)
    dsc = jnp.zeros((t_len, t_len), jnp.float32)
    for h in range(2):
        mask = ((lane >= h * HD) & (lane < (h + 1) * HD)).astype(jnp.float32)
        gm = g * mask
        crow = crow_ref[0, h : h + 1, :]
        ccol = ccol_ref[0, :, h : h + 1]
        srow = srow_ref[0, h : h + 1, :]
        within = jnp.where(tri, jnp.exp(jnp.where(tri, ccol - crow, 0.0)), 0.0)
        score_w = scores * within
        d_mix = _dot(gm, x, ((1,), (1,)))
        dx = dx + _dot(score_w * srow, gm, ((0,), (0,)))
        dsc = dsc + d_mix * within * srow
        q_mat = d_mix * score_w
        p_mat = q_mat * srow
        dstep_ref[0, h : h + 1, :] = jnp.sum(q_mat, axis=0, keepdims=True)
        dcum_ref[0, h : h + 1, :] = _dot(ones, p_mat, ((1,), (1,)))[0:1] - jnp.sum(
            p_mat, axis=0, keepdims=True
        )
    dx_ref[...] = dx
    first = step_id % per_group_pairs == 0

    @pl.when(first)
    def _():
        dsc_ref[0] = dsc

    @pl.when(jnp.logical_not(first))
    def _():
        dsc_ref[0] += dsc


def block_inner(xa, ba, ca, step, rate, G):
    T, ng, nk, P = xa.shape
    nh = ng * nk
    pairs = nh // 2
    per_group_pairs = nk // 2
    cum = jnp.cumsum(-step * rate[:, :, None], axis=-1)
    cum_pairs = cum.reshape(pairs, 2, T)
    row_spec = pl.BlockSpec((1, 2, T), lambda j: (j, 0, 0))
    lane_spec = pl.BlockSpec((T, 2 * P), lambda j: (0, j))
    grp_spec = pl.BlockSpec((T, N), lambda j: (0, j // per_group_pairs))
    dx2, d_direct, d_cum, d_scores = pl.pallas_call(
        functools.partial(_grad_kernel, per_group_pairs),
        grid=(pairs,),
        in_specs=[
            lane_spec, lane_spec, grp_spec, grp_spec, row_spec,
            pl.BlockSpec((1, T, 2), lambda j: (j, 0, 0)), row_spec,
        ],
        out_specs=[
            lane_spec, row_spec, row_spec,
            pl.BlockSpec((1, T, T), lambda j: (j // per_group_pairs, 0, 0)),
        ],
        out_shape=[
            jax.ShapeDtypeStruct((T, nh * P), jnp.float32),
            jax.ShapeDtypeStruct((pairs, 2, T), jnp.float32),
            jax.ShapeDtypeStruct((pairs, 2, T), jnp.float32),
            jax.ShapeDtypeStruct((ng, T, T), jnp.float32),
        ],
    )(
        xa.reshape(T, nh * P),
        G.reshape(T, nh * P),
        ba.reshape(T, ng * N),
        ca.reshape(T, ng * N),
        cum_pairs,
        jnp.swapaxes(cum_pairs, 1, 2),
        step.reshape(pairs, 2, T),
    )
    return (
        dx2.reshape(T, ng, nk, P),
        d_direct.reshape(ng, nk, T),
        d_cum.reshape(ng, nk, T),
        d_scores,
        cum,
    )


def block_outer(inner, xa, ba, ca, step, rate, skip, S0, G, lam):
    dx, d_step, d_cum, d_scores, cum = inner
    dx = dx + skip[None, :, :, None] * G
    dc = jnp.einsum("gts,sgn->tgn", d_scores, ba, precision=EXACT_DOT)
    db = jnp.einsum("gts,tgn->sgn", d_scores, ca, precision=EXACT_DOT)
    grow = jnp.exp(cum)
    g_grow = G * grow.transpose(2, 0, 1)[..., None]
    carried = jnp.einsum("tgn,gkpn->tgkp", ca, S0, precision=EXACT_DOT)
    dc = dc + jnp.einsum("tgkp,gkpn->tgn", g_grow, S0, precision=EXACT_DOT)
    d_cum = d_cum + jnp.sum(g_grow * carried, axis=-1).transpose(1, 2, 0)
    if lam is not None:
        to_end = jnp.exp(cum[..., -1:] - cum)
        push = to_end * step
        lam_b = jnp.einsum("gkpn,sgn->sgkp", lam, ba, precision=EXACT_DOT)
        dx = dx + push.transpose(2, 0, 1)[..., None] * lam_b
        db = db + jnp.einsum("gkpn,sgkp,gks->sgn", lam, xa, push, precision=EXACT_DOT)
        q_end = jnp.sum(xa * lam_b, axis=-1).transpose(1, 2, 0)
        d_step = d_step + to_end * q_end
        wq = push * q_end
        end_total = jnp.sum(wq, axis=-1) + jnp.exp(cum[..., -1]) * jnp.sum(lam * S0, axis=(-2, -1))
        d_cum = d_cum - wq
        d_cum = d_cum.at[..., -1].add(end_total)
    d_log = jnp.flip(jnp.cumsum(jnp.flip(d_cum, -1), axis=-1), -1)
    d_step = d_step - rate[:, :, None] * d_log
    return dx, db, dc, d_step


def shards(
    prefix_x,
    prefix_b,
    prefix_c,
    prefix_dt,
    prefix_grad,
    suffix_x,
    suffix_b,
    suffix_c,
    suffix_dt,
    suffix_grad,
    lengths,
    loss_mask,
    advantage,
    conv_x,
    conv_b,
    conv_c,
    decay_rate,
    dt_bias,
    skip,
):
    num_ways = lax.axis_size("suf")
    my_index = lax.axis_index("suf")
    num_heads = decay_rate.shape[0]
    num_groups = conv_b.shape[1] // N
    per_group = num_heads // num_groups
    margin = KW - 1
    prompt_len = prefix_x.shape[0]
    width_x = prefix_x.shape[1]
    width_b = prefix_b.shape[1]
    rate = decay_rate.reshape(num_groups, per_group)
    gain = skip.reshape(num_groups, per_group)

    def split_tokens(tokens):
        return (
            tokens[:, :width_x],
            tokens[:, width_x : width_x + width_b],
            tokens[:, width_x + width_b :],
        )

    def convs(ux, ub, uc, cx, cb, cc):
        return (
            causal_conv(ux, cx, conv_x),
            causal_conv(ub, cb, conv_b),
            causal_conv(uc, cc, conv_c),
        )

    def softplus_of(raw):
        return jax.nn.softplus(raw + dt_bias[:, None])

    prompt_step, step_pullback = jax.vjp(softplus_of, prefix_dt)
    cumulative = jnp.cumsum(-prompt_step * decay_rate[:, None], axis=1)
    total_log = cumulative[:, -1]
    tails = jnp.concatenate(
        [prefix_x[-margin:], prefix_b[-margin:], prefix_c[-margin:]], axis=1
    ).astype(jnp.float32)
    tail_size = tails.size
    own_pack = jnp.concatenate([tails.reshape(-1), total_log])
    received = [own_pack] + [
        lax.ppermute(own_pack, "suf", [(j, (j + shift) % num_ways) for j in range(num_ways)])
        for shift in range(1, num_ways)
    ]
    every = jnp.take(
        jnp.stack(received), (my_index - jnp.arange(num_ways)) % num_ways, axis=0
    )
    every_tails = every[:, :tail_size].reshape((num_ways,) + tails.shape)
    every_log = every[:, tail_size:]
    behind = lax.dynamic_index_in_dim(every_tails, jnp.maximum(my_index - 1, 0), 0, False)
    behind = jnp.where(my_index > 0, behind, 0.0)
    left_x, left_b, left_c = split_tokens(behind)
    ctx_x, ctx_b, ctx_c = split_tokens(every_tails[num_ways - 1])

    acts, prompt_conv_pullback = jax.vjp(
        convs,
        prefix_x.astype(jnp.float32),
        prefix_b.astype(jnp.float32),
        prefix_c.astype(jnp.float32),
        left_x,
        left_b,
        left_c,
    )
    x_act = acts[0].reshape(prompt_len, num_groups, per_group, HD)
    b_act = acts[1].reshape(prompt_len, num_groups, N)
    c_act = acts[2].reshape(prompt_len, num_groups, N)
    prompt_cot = prefix_grad.astype(jnp.float32).reshape(prompt_len, num_groups, per_group, HD)
    push_weight = (jnp.exp(total_log[:, None] - cumulative) * prompt_step).reshape(
        num_groups, per_group, prompt_len
    )
    own_state = jnp.einsum("gkt,tgkp,tgn->gkpn", push_weight, x_act, b_act, precision=EXACT_DOT)
    pull_weight = jnp.exp(cumulative).reshape(num_groups, per_group, prompt_len)
    own_adjoint = jnp.einsum(
        "gkt,tgkp,tgn->gkpn", pull_weight, prompt_cot, c_act, precision=EXACT_DOT
    )
    positions = jnp.arange(suffix_x.shape[1])[None, :]
    weight = (
        advantage[:, None]
        * loss_mask.astype(jnp.float32)
        * (positions < lengths[:, None]).astype(jnp.float32)
    )

    def suffix_parts(x_one, b_one, c_one, dt_one, grad_one, weight_one):
        suffix_len = x_one.shape[0]
        step_one, one_step_pullback = jax.vjp(softplus_of, dt_one)
        s_acts, conv_pullback = jax.vjp(convs, x_one, b_one, c_one, ctx_x, ctx_b, ctx_c)
        sx = s_acts[0].reshape(suffix_len, num_groups, per_group, HD)
        sb = s_acts[1].reshape(suffix_len, num_groups, N)
        sc = s_acts[2].reshape(suffix_len, num_groups, N)
        cot = (weight_one[:, None] * grad_one).reshape(suffix_len, num_groups, per_group, HD)
        step_g = step_one.reshape(num_groups, per_group, suffix_len)
        return one_step_pullback, conv_pullback, sx, sb, sc, cot, step_g

    def suffix_front(*items):
        unused_a, unused_b, sx, sb, sc, cot, step_g = suffix_parts(*items)
        grow = jnp.exp(jnp.cumsum(-step_g * rate[:, :, None], axis=-1))
        adjoint = jnp.einsum("gkt,tgkp,tgn->gkpn", grow, cot, sc, precision=EXACT_DOT)
        return adjoint, block_inner(sx, sb, sc, step_g, rate, cot)

    def suffix_back(end_state, inner, *items):
        one_step_pullback, conv_pullback, sx, sb, sc, cot, step_g = suffix_parts(*items)
        suffix_len = sx.shape[0]
        dx, db, dc, d_step = block_outer(inner, sx, sb, sc, step_g, rate, gain, end_state, cot, None)
        conv_grads = conv_pullback(
            (dx.reshape(suffix_len, -1), db.reshape(suffix_len, -1), dc.reshape(suffix_len, -1))
        )
        d_dt = one_step_pullback(d_step.reshape(num_heads, suffix_len))[0]
        return conv_grads, d_dt

    suffix_items = (
        suffix_x.astype(jnp.float32),
        suffix_b.astype(jnp.float32),
        suffix_c.astype(jnp.float32),
        suffix_dt,
        suffix_grad.astype(jnp.float32),
        weight,
    )
    adjoints, suffix_inner = jax.vmap(suffix_front, in_axes=(0, 0, 0, 1, 0, 0))(*suffix_items)
    step_g = prompt_step.reshape(num_groups, per_group, prompt_len)
    prompt_inner = block_inner(x_act, b_act, c_act, step_g, rate, prompt_cot)
    core = my_index % 2
    chip = my_index // 2
    num_chips = num_ways // 2
    own_triple = jnp.stack([own_state, own_adjoint, jnp.sum(adjoints, axis=0)])
    partner_triple = lax.ppermute(own_triple, "suf", [(j, j ^ 1) for j in range(num_ways)])
    even = jnp.where(core == 0, own_triple, partner_triple)
    odd = jnp.where(core == 0, partner_triple, own_triple)
    block_decay = jnp.exp(every_log).reshape(num_ways, num_groups, per_group, 1, 1)
    decay_even = lax.dynamic_index_in_dim(block_decay, 2 * chip, 0, False)
    decay_odd = lax.dynamic_index_in_dim(block_decay, 2 * chip + 1, 0, False)
    chip_log = every_log.reshape(num_chips, 2, num_heads).sum(axis=1)
    later_log = jnp.sum(jnp.where((jnp.arange(num_chips) >= chip)[:, None], chip_log, 0.0), axis=0)
    chip_state = decay_odd * even[0] + odd[0]
    chip_adjoint = even[1] + decay_even * odd[1]
    chip_suffix = even[2] + odd[2]
    chip_later = chip_adjoint + jnp.exp(later_log).reshape(num_groups, per_group, 1, 1) * chip_suffix
    got_state = [chip_state]
    got_other = [chip_suffix]
    for shift in range(1, num_chips):
        wraps = chip + shift >= num_chips
        outgoing = jnp.where(core == 0, chip_state, jnp.where(wraps, chip_later, chip_suffix))
        route = [
            (2 * c + k, 2 * ((c + shift) % num_chips) + k) for c in range(num_chips) for k in range(2)
        ]
        incoming = lax.ppermute(outgoing, "suf", route)
        shared = lax.ppermute(incoming, "suf", [(j, j ^ 1) for j in range(num_ways)])
        got_state.append(jnp.where(core == 0, incoming, shared))
        got_other.append(jnp.where(core == 0, shared, incoming))
    def chip_ordered(got):
        ordered = []
        for c in range(num_chips):
            distance = (chip - c) % num_chips
            value = got[0]
            for shift in range(1, num_chips):
                value = jnp.where(distance == shift, got[shift], value)
            ordered.append(value)
        return ordered

    chip_states = chip_ordered(got_state)
    chip_others = chip_ordered(got_other)
    chip_decay = jnp.exp(chip_log).reshape(num_chips, num_groups, per_group, 1, 1)
    running = jnp.zeros_like(own_state)
    chip_start = running
    for c in range(num_chips):
        chip_start = jnp.where(chip == c, running, chip_start)
        running = chip_decay[c] * running + chip_states[c]
    prompt_end_late = running
    running = jnp.zeros_like(own_state)
    for c in range(num_chips):
        running = running + jnp.where(c <= chip, chip_others[c], 0.0)
    chip_end_grad = running
    for c in reversed(range(num_chips)):
        chip_end_grad = jnp.where(chip == c, running, chip_end_grad)
        running = chip_others[c] + chip_decay[c] * running
    start_state = jnp.where(core == 0, chip_start, decay_even * chip_start + even[0])
    end_grad = jnp.where(core == 0, odd[1] + decay_odd * chip_end_grad, chip_end_grad)
    conv_grads, suffix_ddt = jax.vmap(
        suffix_back, in_axes=(None, 0, 0, 0, 0, 1, 0, 0), out_axes=(0, 1)
    )(prompt_end_late, suffix_inner, *suffix_items)
    dx, db, dc, d_step = block_outer(
        prompt_inner, x_act, b_act, c_act, step_g, rate, gain, start_state, prompt_cot, end_grad
    )
    prompt_grads = prompt_conv_pullback(
        (dx.reshape(prompt_len, -1), db.reshape(prompt_len, -1), dc.reshape(prompt_len, -1))
    )
    prefix_ddt = step_pullback(d_step.reshape(num_heads, prompt_len))[0]
    left_grads = jnp.concatenate([prompt_grads[3], prompt_grads[4], prompt_grads[5]], axis=1)
    from_right = from_behind(left_grads, "suf", -1)
    ctx_grads = jnp.concatenate(
        [jnp.sum(conv_grads[3], axis=0), jnp.sum(conv_grads[4], axis=0), jnp.sum(conv_grads[5], axis=0)],
        axis=1,
    )
    from_suffix = ctx_grads
    for sender in range(num_ways - 1):
        from_suffix = from_suffix + lax.ppermute(ctx_grads, "suf", [(sender, num_ways - 1)])
    last_device = my_index == num_ways - 1
    tail_add = split_tokens(from_right + jnp.where(last_device, from_suffix, 0.0))

    def finish(grad_full, extra):
        placed = jnp.pad(extra, ((grad_full.shape[0] - margin, 0), (0, 0)))
        return (grad_full + placed).astype(jnp.bfloat16)

    return (
        finish(prompt_grads[0], tail_add[0]),
        finish(prompt_grads[1], tail_add[1]),
        finish(prompt_grads[2], tail_add[2]),
        prefix_ddt,
        conv_grads[0].astype(jnp.bfloat16),
        conv_grads[1].astype(jnp.bfloat16),
        conv_grads[2].astype(jnp.bfloat16),
        suffix_ddt,
    )


def solution(mesh):
    return jax.shard_map(
        shards,
        mesh=mesh,
        in_specs=(
            P(("grp", "suf"), "head"),
            P(("grp", "suf"), "head"),
            P(("grp", "suf"), "head"),
            P("head", ("grp", "suf")),
            P(("grp", "suf"), "head"),
            P(("grp", "suf"), None, "head"),
            P(("grp", "suf"), None, "head"),
            P(("grp", "suf"), None, "head"),
            P("head", ("grp", "suf"), None),
            P(("grp", "suf"), None, "head"),
            P(("grp", "suf")),
            P(("grp", "suf"), None),
            P(("grp", "suf")),
            P(None, "head"),
            P(None, "head"),
            P(None, "head"),
            P("head"),
            P("head"),
            P("head"),
        ),
        out_specs=(
            P(("grp", "suf"), "head"),
            P(("grp", "suf"), "head"),
            P(("grp", "suf"), "head"),
            P("head", ("grp", "suf")),
            P(("grp", "suf"), None, "head"),
            P(("grp", "suf"), None, "head"),
            P(("grp", "suf"), None, "head"),
            P("head", ("grp", "suf"), None),
        ),
        check_vma=False,
    )
```

```python
import functools

import jax
import jax.numpy as jnp
from jax import lax
from jax.experimental import pallas as pl
from jax.sharding import PartitionSpec as P


HD = 64
N = 128
KW = 4


EXACT_DOT = lax.Precision.HIGHEST


def from_behind(block, axis, distance):
    devices = range(lax.axis_size(axis))
    route = [(i - distance, i) for i in devices if i - distance in devices]
    return lax.ppermute(block, axis, route)


def causal_conv(values, context, taps):
    padded = jnp.concatenate([context, values], axis=0)
    num_tokens = values.shape[0]
    result = padded[0:num_tokens] * taps[0].astype(jnp.float32)
    for tap_index in range(1, taps.shape[0]):
        result = result + padded[tap_index : tap_index + num_tokens] * taps[tap_index].astype(
            jnp.float32
        )
    return jax.nn.silu(result)


def _dot(a, b, dims):
    return lax.dot_general(a, b, (dims, ((), ())), precision=EXACT_DOT, preferred_element_type=jnp.float32)


def _grad_kernel(per_group_pairs, x_ref, g_ref, b_ref, c_ref, crow_ref, ccol_ref, srow_ref,
                 dx_ref, dstep_ref, dcum_ref, dsc_ref):
    step_id = pl.program_id(0)
    x = x_ref[...]
    g = g_ref[...]
    t_len = x.shape[0]
    tri = lax.broadcasted_iota(jnp.int32, (t_len, t_len), 0) >= lax.broadcasted_iota(jnp.int32, (t_len, t_len), 1)
    lane = lax.broadcasted_iota(jnp.int32, (1, 2 * HD), 1)
    ones = jnp.ones((8, t_len), jnp.float32)
    scores = _dot(c_ref[...], b_ref[...], ((1,), (1,)))
    dx = jnp.zeros_like(x)
    dsc = jnp.zeros((t_len, t_len), jnp.float32)
    for h in range(2):
        mask = ((lane >= h * HD) & (lane < (h + 1) * HD)).astype(jnp.float32)
        gm = g * mask
        crow = crow_ref[0, h : h + 1, :]
        ccol = ccol_ref[0, :, h : h + 1]
        srow = srow_ref[0, h : h + 1, :]
        within = jnp.where(tri, jnp.exp(jnp.where(tri, ccol - crow, 0.0)), 0.0)
        score_w = scores * within
        d_mix = _dot(gm, x, ((1,), (1,)))
        dx = dx + _dot(score_w * srow, gm, ((0,), (0,)))
        dsc = dsc + d_mix * within * srow
        q_mat = d_mix * score_w
        p_mat = q_mat * srow
        dstep_ref[0, h : h + 1, :] = jnp.sum(q_mat, axis=0, keepdims=True)
        dcum_ref[0, h : h + 1, :] = _dot(ones, p_mat, ((1,), (1,)))[0:1] - jnp.sum(
            p_mat, axis=0, keepdims=True
        )
    dx_ref[...] = dx
    first = step_id % per_group_pairs == 0

    @pl.when(first)
    def _():
        dsc_ref[0] = dsc

    @pl.when(jnp.logical_not(first))
    def _():
        dsc_ref[0] += dsc


def block_inner(xa, ba, ca, step, rate, G):
    T, ng, nk, P = xa.shape
    nh = ng * nk
    pairs = nh // 2
    per_group_pairs = nk // 2
    cum = jnp.cumsum(-step * rate[:, :, None], axis=-1)
    cum_pairs = cum.reshape(pairs, 2, T)
    row_spec = pl.BlockSpec((1, 2, T), lambda j: (j, 0, 0))
    lane_spec = pl.BlockSpec((T, 2 * P), lambda j: (0, j))
    grp_spec = pl.BlockSpec((T, N), lambda j: (0, j // per_group_pairs))
    dx2, d_direct, d_cum, d_scores = pl.pallas_call(
        functools.partial(_grad_kernel, per_group_pairs),
        grid=(pairs,),
        in_specs=[
            lane_spec, lane_spec, grp_spec, grp_spec, row_spec,
            pl.BlockSpec((1, T, 2), lambda j: (j, 0, 0)), row_spec,
        ],
        out_specs=[
            lane_spec, row_spec, row_spec,
            pl.BlockSpec((1, T, T), lambda j: (j // per_group_pairs, 0, 0)),
        ],
        out_shape=[
            jax.ShapeDtypeStruct((T, nh * P), jnp.float32),
            jax.ShapeDtypeStruct((pairs, 2, T), jnp.float32),
            jax.ShapeDtypeStruct((pairs, 2, T), jnp.float32),
            jax.ShapeDtypeStruct((ng, T, T), jnp.float32),
        ],
    )(
        xa.reshape(T, nh * P),
        G.reshape(T, nh * P),
        ba.reshape(T, ng * N),
        ca.reshape(T, ng * N),
        cum_pairs,
        jnp.swapaxes(cum_pairs, 1, 2),
        step.reshape(pairs, 2, T),
    )
    return (
        dx2.reshape(T, ng, nk, P),
        d_direct.reshape(ng, nk, T),
        d_cum.reshape(ng, nk, T),
        d_scores,
        cum,
    )


def block_outer(inner, xa, ba, ca, step, rate, skip, S0, G, lam):
    dx, d_step, d_cum, d_scores, cum = inner
    dx = dx + skip[None, :, :, None] * G
    dc = jnp.einsum("gts,sgn->tgn", d_scores, ba, precision=EXACT_DOT)
    db = jnp.einsum("gts,tgn->sgn", d_scores, ca, precision=EXACT_DOT)
    grow = jnp.exp(cum)
    g_grow = G * grow.transpose(2, 0, 1)[..., None]
    carried = jnp.einsum("tgn,gkpn->tgkp", ca, S0, precision=EXACT_DOT)
    dc = dc + jnp.einsum("tgkp,gkpn->tgn", g_grow, S0, precision=EXACT_DOT)
    d_cum = d_cum + jnp.sum(g_grow * carried, axis=-1).transpose(1, 2, 0)
    if lam is not None:
        to_end = jnp.exp(cum[..., -1:] - cum)
        push = to_end * step
        lam_b = jnp.einsum("gkpn,sgn->sgkp", lam, ba, precision=EXACT_DOT)
        dx = dx + push.transpose(2, 0, 1)[..., None] * lam_b
        db = db + jnp.einsum("gkpn,sgkp,gks->sgn", lam, xa, push, precision=EXACT_DOT)
        q_end = jnp.sum(xa * lam_b, axis=-1).transpose(1, 2, 0)
        d_step = d_step + to_end * q_end
        wq = push * q_end
        end_total = jnp.sum(wq, axis=-1) + jnp.exp(cum[..., -1]) * jnp.sum(lam * S0, axis=(-2, -1))
        d_cum = d_cum - wq
        d_cum = d_cum.at[..., -1].add(end_total)
    d_log = jnp.flip(jnp.cumsum(jnp.flip(d_cum, -1), axis=-1), -1)
    d_step = d_step - rate[:, :, None] * d_log
    return dx, db, dc, d_step


def shards(
    prefix_x,
    prefix_b,
    prefix_c,
    prefix_dt,
    prefix_grad,
    suffix_x,
    suffix_b,
    suffix_c,
    suffix_dt,
    suffix_grad,
    lengths,
    loss_mask,
    advantage,
    conv_x,
    conv_b,
    conv_c,
    decay_rate,
    dt_bias,
    skip,
):
    num_ways = lax.axis_size("suf")
    my_index = lax.axis_index("suf")
    num_heads = decay_rate.shape[0]
    num_groups = conv_b.shape[1] // N
    per_group = num_heads // num_groups
    margin = KW - 1
    prompt_len = prefix_x.shape[0]
    width_x = prefix_x.shape[1]
    width_b = prefix_b.shape[1]
    rate = decay_rate.reshape(num_groups, per_group)
    gain = skip.reshape(num_groups, per_group)

    def split_tokens(tokens):
        return (
            tokens[:, :width_x],
            tokens[:, width_x : width_x + width_b],
            tokens[:, width_x + width_b :],
        )

    def convs(ux, ub, uc, cx, cb, cc):
        return (
            causal_conv(ux, cx, conv_x),
            causal_conv(ub, cb, conv_b),
            causal_conv(uc, cc, conv_c),
        )

    def softplus_of(raw):
        return jax.nn.softplus(raw + dt_bias[:, None])

    prompt_step, step_pullback = jax.vjp(softplus_of, prefix_dt)
    cumulative = jnp.cumsum(-prompt_step * decay_rate[:, None], axis=1)
    total_log = cumulative[:, -1]
    tails = jnp.concatenate(
        [prefix_x[-margin:], prefix_b[-margin:], prefix_c[-margin:]], axis=1
    ).astype(jnp.float32)
    tail_size = tails.size
    own_pack = jnp.concatenate([tails.reshape(-1), total_log])
    received = [own_pack] + [
        lax.ppermute(own_pack, "suf", [(j, (j + shift) % num_ways) for j in range(num_ways)])
        for shift in range(1, num_ways)
    ]
    every = jnp.take(
        jnp.stack(received), (my_index - jnp.arange(num_ways)) % num_ways, axis=0
    )
    every_tails = every[:, :tail_size].reshape((num_ways,) + tails.shape)
    every_log = every[:, tail_size:]
    behind = lax.dynamic_index_in_dim(every_tails, jnp.maximum(my_index - 1, 0), 0, False)
    behind = jnp.where(my_index > 0, behind, 0.0)
    left_x, left_b, left_c = split_tokens(behind)
    ctx_x, ctx_b, ctx_c = split_tokens(every_tails[num_ways - 1])

    acts, prompt_conv_pullback = jax.vjp(
        convs,
        prefix_x.astype(jnp.float32),
        prefix_b.astype(jnp.float32),
        prefix_c.astype(jnp.float32),
        left_x,
        left_b,
        left_c,
    )
    x_act = acts[0].reshape(prompt_len, num_groups, per_group, HD)
    b_act = acts[1].reshape(prompt_len, num_groups, N)
    c_act = acts[2].reshape(prompt_len, num_groups, N)
    prompt_cot = prefix_grad.astype(jnp.float32).reshape(prompt_len, num_groups, per_group, HD)
    push_weight = (jnp.exp(total_log[:, None] - cumulative) * prompt_step).reshape(
        num_groups, per_group, prompt_len
    )
    own_state = jnp.einsum("gkt,tgkp,tgn->gkpn", push_weight, x_act, b_act, precision=EXACT_DOT)
    pull_weight = jnp.exp(cumulative).reshape(num_groups, per_group, prompt_len)
    own_adjoint = jnp.einsum(
        "gkt,tgkp,tgn->gkpn", pull_weight, prompt_cot, c_act, precision=EXACT_DOT
    )
    positions = jnp.arange(suffix_x.shape[1])[None, :]
    weight = (
        advantage[:, None]
        * loss_mask.astype(jnp.float32)
        * (positions < lengths[:, None]).astype(jnp.float32)
    )

    def suffix_parts(x_one, b_one, c_one, dt_one, grad_one, weight_one):
        suffix_len = x_one.shape[0]
        step_one, one_step_pullback = jax.vjp(softplus_of, dt_one)
        s_acts, conv_pullback = jax.vjp(convs, x_one, b_one, c_one, ctx_x, ctx_b, ctx_c)
        sx = s_acts[0].reshape(suffix_len, num_groups, per_group, HD)
        sb = s_acts[1].reshape(suffix_len, num_groups, N)
        sc = s_acts[2].reshape(suffix_len, num_groups, N)
        cot = (weight_one[:, None] * grad_one).reshape(suffix_len, num_groups, per_group, HD)
        step_g = step_one.reshape(num_groups, per_group, suffix_len)
        return one_step_pullback, conv_pullback, sx, sb, sc, cot, step_g

    def suffix_front(*items):
        _, _, sx, sb, sc, cot, step_g = suffix_parts(*items)
        grow = jnp.exp(jnp.cumsum(-step_g * rate[:, :, None], axis=-1))
        adjoint = jnp.einsum("gkt,tgkp,tgn->gkpn", grow, cot, sc, precision=EXACT_DOT)
        inner = block_inner(sx, sb, sc, step_g, rate, cot)
        return adjoint, inner

    def suffix_back(end_state, inner, *items):
        one_step_pullback, conv_pullback, sx, sb, sc, cot, step_g = suffix_parts(*items)
        suffix_len = sx.shape[0]
        dx, db, dc, d_step = block_outer(inner, sx, sb, sc, step_g, rate, gain, end_state, cot, None)
        conv_grads = conv_pullback(
            (dx.reshape(suffix_len, -1), db.reshape(suffix_len, -1), dc.reshape(suffix_len, -1))
        )
        d_dt = one_step_pullback(d_step.reshape(num_heads, suffix_len))[0]
        return conv_grads, d_dt

    suffix_items = (
        suffix_x.astype(jnp.float32),
        suffix_b.astype(jnp.float32),
        suffix_c.astype(jnp.float32),
        suffix_dt,
        suffix_grad.astype(jnp.float32),
        weight,
    )
    adjoints, suffix_inner = jax.vmap(suffix_front, in_axes=(0, 0, 0, 1, 0, 0))(*suffix_items)
    step_g = prompt_step.reshape(num_groups, per_group, prompt_len)
    prompt_inner = block_inner(x_act, b_act, c_act, step_g, rate, prompt_cot)
    core = my_index % 2
    chip = my_index // 2
    num_chips = num_ways // 2
    own_triple = jnp.stack([own_state, own_adjoint, jnp.sum(adjoints, axis=0)])
    partner_triple = lax.ppermute(own_triple, "suf", [(j, j ^ 1) for j in range(num_ways)])
    even = jnp.where(core == 0, own_triple, partner_triple)
    odd = jnp.where(core == 0, partner_triple, own_triple)
    block_decay = jnp.exp(every_log).reshape(num_ways, num_groups, per_group, 1, 1)
    decay_even = lax.dynamic_index_in_dim(block_decay, 2 * chip, 0, False)
    decay_odd = lax.dynamic_index_in_dim(block_decay, 2 * chip + 1, 0, False)
    chip_log = every_log.reshape(num_chips, 2, num_heads).sum(axis=1)
    later_log = jnp.sum(jnp.where((jnp.arange(num_chips) >= chip)[:, None], chip_log, 0.0), axis=0)
    chip_state = decay_odd * even[0] + odd[0]
    chip_adjoint = even[1] + decay_even * odd[1]
    chip_suffix = even[2] + odd[2]
    chip_later = chip_adjoint + jnp.exp(later_log).reshape(num_groups, per_group, 1, 1) * chip_suffix
    got_state = [chip_state]
    got_other = [chip_suffix]
    for shift in range(1, num_chips):
        wraps = chip + shift >= num_chips
        outgoing = jnp.where(core == 0, chip_state, jnp.where(wraps, chip_later, chip_suffix))
        route = [
            (2 * c + k, 2 * ((c + shift) % num_chips) + k) for c in range(num_chips) for k in range(2)
        ]
        incoming = lax.ppermute(outgoing, "suf", route)
        shared = lax.ppermute(incoming, "suf", [(j, j ^ 1) for j in range(num_ways)])
        got_state.append(jnp.where(core == 0, incoming, shared))
        got_other.append(jnp.where(core == 0, shared, incoming))

    def chip_ordered(got):
        ordered = []
        for c in range(num_chips):
            distance = (chip - c) % num_chips
            value = got[0]
            for shift in range(1, num_chips):
                value = jnp.where(distance == shift, got[shift], value)
            ordered.append(value)
        return ordered

    chip_states = chip_ordered(got_state)
    chip_others = chip_ordered(got_other)
    chip_decay = jnp.exp(chip_log).reshape(num_chips, num_groups, per_group, 1, 1)
    running = jnp.zeros_like(own_state)
    chip_start = running
    for c in range(num_chips):
        chip_start = jnp.where(chip == c, running, chip_start)
        running = chip_decay[c] * running + chip_states[c]
    prompt_end_late = running
    running = jnp.zeros_like(own_state)
    for c in range(num_chips):
        running = running + jnp.where(c <= chip, chip_others[c], 0.0)
    chip_end_grad = running
    for c in reversed(range(num_chips)):
        chip_end_grad = jnp.where(chip == c, running, chip_end_grad)
        running = chip_others[c] + chip_decay[c] * running
    start_state = jnp.where(core == 0, chip_start, decay_even * chip_start + even[0])
    end_grad = jnp.where(core == 0, odd[1] + decay_odd * chip_end_grad, chip_end_grad)
    conv_grads, suffix_ddt = jax.vmap(
        suffix_back, in_axes=(None, 0, 0, 0, 0, 1, 0, 0), out_axes=(0, 1)
    )(prompt_end_late, suffix_inner, *suffix_items)
    dx, db, dc, d_step = block_outer(
        prompt_inner, x_act, b_act, c_act, step_g, rate, gain, start_state, prompt_cot, end_grad
    )
    prompt_grads = prompt_conv_pullback(
        (dx.reshape(prompt_len, -1), db.reshape(prompt_len, -1), dc.reshape(prompt_len, -1))
    )
    prefix_ddt = step_pullback(d_step.reshape(num_heads, prompt_len))[0]
    left_grads = jnp.concatenate([prompt_grads[3], prompt_grads[4], prompt_grads[5]], axis=1)
    from_right = from_behind(left_grads, "suf", -1)
    ctx_grads = jnp.concatenate(
        [jnp.sum(conv_grads[3], axis=0), jnp.sum(conv_grads[4], axis=0), jnp.sum(conv_grads[5], axis=0)],
        axis=1,
    )
    from_suffix = ctx_grads
    for sender in range(num_ways - 1):
        from_suffix = from_suffix + lax.ppermute(ctx_grads, "suf", [(sender, num_ways - 1)])
    last_device = my_index == num_ways - 1
    tail_add = split_tokens(from_right + jnp.where(last_device, from_suffix, 0.0))

    def finish(grad_full, extra):
        placed = jnp.pad(extra, ((grad_full.shape[0] - margin, 0), (0, 0)))
        return (grad_full + placed).astype(jnp.bfloat16)

    return (
        finish(prompt_grads[0], tail_add[0]),
        finish(prompt_grads[1], tail_add[1]),
        finish(prompt_grads[2], tail_add[2]),
        prefix_ddt,
        conv_grads[0].astype(jnp.bfloat16),
        conv_grads[1].astype(jnp.bfloat16),
        conv_grads[2].astype(jnp.bfloat16),
        suffix_ddt,
    )


def solution(mesh):
    return jax.shard_map(
        shards,
        mesh=mesh,
        in_specs=(
            P(("grp", "suf"), "head"),
            P(("grp", "suf"), "head"),
            P(("grp", "suf"), "head"),
            P("head", ("grp", "suf")),
            P(("grp", "suf"), "head"),
            P(("grp", "suf"), None, "head"),
            P(("grp", "suf"), None, "head"),
            P(("grp", "suf"), None, "head"),
            P("head", ("grp", "suf"), None),
            P(("grp", "suf"), None, "head"),
            P(("grp", "suf")),
            P(("grp", "suf"), None),
            P(("grp", "suf")),
            P(None, "head"),
            P(None, "head"),
            P(None, "head"),
            P("head"),
            P("head"),
            P("head"),
        ),
        out_specs=(
            P(("grp", "suf"), "head"),
            P(("grp", "suf"), "head"),
            P(("grp", "suf"), "head"),
            P("head", ("grp", "suf")),
            P(("grp", "suf"), None, "head"),
            P(("grp", "suf"), None, "head"),
            P(("grp", "suf"), None, "head"),
            P("head", ("grp", "suf"), None),
        ),
        check_vma=False,
    )
```

```python
import functools

import jax
import jax.numpy as jnp
from jax import lax
from jax.experimental import pallas as pl
from jax.experimental.pallas import tpu as pltpu
from jax.sharding import PartitionSpec as P


HD = 64
N = 128
KW = 4


EXACT_DOT = lax.Precision.HIGHEST


def from_behind(block, axis, distance):
    devices = range(lax.axis_size(axis))
    route = [(i - distance, i) for i in devices if i - distance in devices]
    return lax.ppermute(block, axis, route)


def causal_conv(values, context, taps):
    padded = jnp.concatenate([context, values], axis=0)
    num_tokens = values.shape[0]
    result = padded[0:num_tokens] * taps[0].astype(jnp.float32)
    for tap_index in range(1, taps.shape[0]):
        result = result + padded[tap_index : tap_index + num_tokens] * taps[tap_index].astype(
            jnp.float32
        )
    return jax.nn.silu(result)


def _dot(a, b, dims):
    return lax.dot_general(a, b, (dims, ((), ())), precision=EXACT_DOT, preferred_element_type=jnp.float32)


def _grad_kernel(steps_per_group, x_ref, g_ref, b_ref, c_ref, crow_ref, srow_ref, skip_ref,
                 dx_ref, dstep_ref, dcum_ref, dc_ref, db_ref, dsc_ref):
    step_id = pl.program_id(0)
    bb = b_ref[...]
    cc = c_ref[...]
    t_len = bb.shape[0]
    lanes = 2 * HD
    tri = lax.broadcasted_iota(jnp.int32, (t_len, t_len), 0) >= lax.broadcasted_iota(jnp.int32, (t_len, t_len), 1)
    lane = lax.broadcasted_iota(jnp.int32, (1, lanes), 1)
    ones = jnp.ones((8, t_len), jnp.float32)
    scores = _dot(cc, bb, ((1,), (1,)))
    dsc = jnp.zeros((t_len, t_len), jnp.float32)
    for pair in range(dx_ref.shape[1] // lanes):
        cols = slice(pair * lanes, (pair + 1) * lanes)
        x = x_ref[:, cols]
        g = g_ref[:, cols]
        dx = skip_ref[:, cols] * g
        for h in range(2):
            head = 2 * pair + h
            mask = ((lane >= h * HD) & (lane < (h + 1) * HD)).astype(jnp.float32)
            gm = g * mask
            crow = crow_ref[head : head + 1, :]
            srow = srow_ref[head : head + 1, :]
            ccol = jnp.transpose(jnp.broadcast_to(crow, (t_len, t_len)))
            within = jnp.where(tri, jnp.exp(jnp.where(tri, ccol - crow, 0.0)), 0.0)
            score_w = scores * within
            d_mix = _dot(gm, x, ((1,), (1,)))
            dx = dx + _dot(score_w * srow, gm, ((0,), (0,)))
            dsc = dsc + d_mix * within * srow
            q_mat = d_mix * score_w
            p_mat = q_mat * srow
            dstep_ref[head : head + 1, :] = jnp.sum(q_mat, axis=0, keepdims=True)
            dcum_ref[head : head + 1, :] = _dot(ones, p_mat, ((1,), (1,)))[0:1] - jnp.sum(
                p_mat, axis=0, keepdims=True
            )
        dx_ref[:, cols] = dx
    within_group = step_id % steps_per_group

    @pl.when(within_group == 0)
    def _():
        dsc_ref[...] = dsc

    @pl.when(within_group != 0)
    def _():
        dsc_ref[...] += dsc

    @pl.when(within_group == steps_per_group - 1)
    def _():
        total = dsc_ref[...]
        dc_ref[...] = _dot(total, bb, ((1,), (0,)))
        db_ref[...] = _dot(total, cc, ((0,), (0,)))


def block_inner(xa, ba, ca, step, rate, skip, G):
    T, ng, nk, P = xa.shape
    nh = ng * nk
    heads_per_step = 8
    steps_per_group = nk // heads_per_step
    cum = jnp.cumsum(-step * rate[:, :, None], axis=-1)
    row_spec = pl.BlockSpec((heads_per_step, T), lambda j: (j, 0))
    lane_spec = pl.BlockSpec((T, heads_per_step * P), lambda j: (0, j))
    grp_spec = pl.BlockSpec((T, N), lambda j: (0, j // steps_per_group))
    dx2, d_direct, d_cum, dc, db = pl.pallas_call(
        functools.partial(_grad_kernel, steps_per_group),
        grid=(nh // heads_per_step,),
        in_specs=[
            lane_spec, lane_spec, grp_spec, grp_spec, row_spec, row_spec,
            pl.BlockSpec((1, heads_per_step * P), lambda j: (0, j)),
        ],
        out_specs=[lane_spec, row_spec, row_spec, grp_spec, grp_spec],
        out_shape=[
            jax.ShapeDtypeStruct((T, nh * P), jnp.float32),
            jax.ShapeDtypeStruct((nh, T), jnp.float32),
            jax.ShapeDtypeStruct((nh, T), jnp.float32),
            jax.ShapeDtypeStruct((T, ng * N), jnp.float32),
            jax.ShapeDtypeStruct((T, ng * N), jnp.float32),
        ],
        scratch_shapes=[pltpu.VMEM((T, T), jnp.float32)],
    )(
        xa.reshape(T, nh * P),
        G.reshape(T, nh * P),
        ba.reshape(T, ng * N),
        ca.reshape(T, ng * N),
        cum.reshape(nh, T),
        step.reshape(nh, T),
        jnp.repeat(skip.reshape(1, nh), P, axis=1),
    )
    return (
        dx2.reshape(T, ng, nk, P),
        d_direct.reshape(ng, nk, T),
        d_cum.reshape(ng, nk, T),
        dc.reshape(T, ng, N),
        db.reshape(T, ng, N),
        cum,
    )


def block_outer(inner, xa, ba, ca, step, rate, S0, G, lam):
    dx, d_step, d_cum, dc, db, cum = inner
    grow = jnp.exp(cum)
    g_grow = G * grow.transpose(2, 0, 1)[..., None]
    carried = jnp.einsum("tgn,gkpn->tgkp", ca, S0, precision=EXACT_DOT)
    dc = dc + jnp.einsum("tgkp,gkpn->tgn", g_grow, S0, precision=EXACT_DOT)
    d_cum = d_cum + jnp.sum(g_grow * carried, axis=-1).transpose(1, 2, 0)
    if lam is not None:
        to_end = jnp.exp(cum[..., -1:] - cum)
        push = to_end * step
        lam_b = jnp.einsum("gkpn,sgn->sgkp", lam, ba, precision=EXACT_DOT)
        dx = dx + push.transpose(2, 0, 1)[..., None] * lam_b
        db = db + jnp.einsum("gkpn,sgkp,gks->sgn", lam, xa, push, precision=EXACT_DOT)
        q_end = jnp.sum(xa * lam_b, axis=-1).transpose(1, 2, 0)
        d_step = d_step + to_end * q_end
        wq = push * q_end
        end_total = jnp.sum(wq, axis=-1) + jnp.exp(cum[..., -1]) * jnp.sum(lam * S0, axis=(-2, -1))
        d_cum = d_cum - wq
        d_cum = d_cum.at[..., -1].add(end_total)
    d_log = jnp.flip(jnp.cumsum(jnp.flip(d_cum, -1), axis=-1), -1)
    d_step = d_step - rate[:, :, None] * d_log
    return dx, db, dc, d_step


def shards(
    prefix_x,
    prefix_b,
    prefix_c,
    prefix_dt,
    prefix_grad,
    suffix_x,
    suffix_b,
    suffix_c,
    suffix_dt,
    suffix_grad,
    lengths,
    loss_mask,
    advantage,
    conv_x,
    conv_b,
    conv_c,
    decay_rate,
    dt_bias,
    skip,
):
    num_ways = lax.axis_size("suf")
    my_index = lax.axis_index("suf")
    num_heads = decay_rate.shape[0]
    num_groups = conv_b.shape[1] // N
    per_group = num_heads // num_groups
    margin = KW - 1
    prompt_len = prefix_x.shape[0]
    width_x = prefix_x.shape[1]
    width_b = prefix_b.shape[1]
    rate = decay_rate.reshape(num_groups, per_group)
    gain = skip.reshape(num_groups, per_group)

    def split_tokens(tokens):
        return (
            tokens[:, :width_x],
            tokens[:, width_x : width_x + width_b],
            tokens[:, width_x + width_b :],
        )

    def convs(ux, ub, uc, cx, cb, cc):
        return (
            causal_conv(ux, cx, conv_x),
            causal_conv(ub, cb, conv_b),
            causal_conv(uc, cc, conv_c),
        )

    def softplus_of(raw):
        return jax.nn.softplus(raw + dt_bias[:, None])

    prompt_step, step_pullback = jax.vjp(softplus_of, prefix_dt)
    cumulative = jnp.cumsum(-prompt_step * decay_rate[:, None], axis=1)
    total_log = cumulative[:, -1]
    tails = jnp.concatenate(
        [prefix_x[-margin:], prefix_b[-margin:], prefix_c[-margin:]], axis=1
    ).astype(jnp.float32)
    tail_size = tails.size
    own_pack = jnp.concatenate([tails.reshape(-1), total_log])
    received = [own_pack] + [
        lax.ppermute(own_pack, "suf", [(j, (j + shift) % num_ways) for j in range(num_ways)])
        for shift in range(1, num_ways)
    ]
    every = jnp.take(
        jnp.stack(received), (my_index - jnp.arange(num_ways)) % num_ways, axis=0
    )
    every_tails = every[:, :tail_size].reshape((num_ways,) + tails.shape)
    every_log = every[:, tail_size:]
    behind = lax.dynamic_index_in_dim(every_tails, jnp.maximum(my_index - 1, 0), 0, False)
    behind = jnp.where(my_index > 0, behind, 0.0)
    left_x, left_b, left_c = split_tokens(behind)
    ctx_x, ctx_b, ctx_c = split_tokens(every_tails[num_ways - 1])

    acts, prompt_conv_pullback = jax.vjp(
        convs,
        prefix_x.astype(jnp.float32),
        prefix_b.astype(jnp.float32),
        prefix_c.astype(jnp.float32),
        left_x,
        left_b,
        left_c,
    )
    x_act = acts[0].reshape(prompt_len, num_groups, per_group, HD)
    b_act = acts[1].reshape(prompt_len, num_groups, N)
    c_act = acts[2].reshape(prompt_len, num_groups, N)
    prompt_cot = prefix_grad.astype(jnp.float32).reshape(prompt_len, num_groups, per_group, HD)
    push_weight = (jnp.exp(total_log[:, None] - cumulative) * prompt_step).reshape(
        num_groups, per_group, prompt_len
    )
    own_state = jnp.einsum("gkt,tgkp,tgn->gkpn", push_weight, x_act, b_act, precision=EXACT_DOT)
    pull_weight = jnp.exp(cumulative).reshape(num_groups, per_group, prompt_len)
    own_adjoint = jnp.einsum(
        "gkt,tgkp,tgn->gkpn", pull_weight, prompt_cot, c_act, precision=EXACT_DOT
    )
    positions = jnp.arange(suffix_x.shape[1])[None, :]
    weight = (
        advantage[:, None]
        * loss_mask.astype(jnp.float32)
        * (positions < lengths[:, None]).astype(jnp.float32)
    )

    def suffix_parts(x_one, b_one, c_one, dt_one, grad_one, weight_one):
        suffix_len = x_one.shape[0]
        step_one, one_step_pullback = jax.vjp(softplus_of, dt_one)
        s_acts, conv_pullback = jax.vjp(convs, x_one, b_one, c_one, ctx_x, ctx_b, ctx_c)
        sx = s_acts[0].reshape(suffix_len, num_groups, per_group, HD)
        sb = s_acts[1].reshape(suffix_len, num_groups, N)
        sc = s_acts[2].reshape(suffix_len, num_groups, N)
        cot = (weight_one[:, None] * grad_one).reshape(suffix_len, num_groups, per_group, HD)
        step_g = step_one.reshape(num_groups, per_group, suffix_len)
        return one_step_pullback, conv_pullback, sx, sb, sc, cot, step_g

    def suffix_front(*items):
        _, _, sx, sb, sc, cot, step_g = suffix_parts(*items)
        grow = jnp.exp(jnp.cumsum(-step_g * rate[:, :, None], axis=-1))
        adjoint = jnp.einsum("gkt,tgkp,tgn->gkpn", grow, cot, sc, precision=EXACT_DOT)
        inner = block_inner(sx, sb, sc, step_g, rate, gain, cot)
        return adjoint, inner

    def suffix_back(end_state, inner, *items):
        one_step_pullback, conv_pullback, sx, sb, sc, cot, step_g = suffix_parts(*items)
        suffix_len = sx.shape[0]
        dx, db, dc, d_step = block_outer(inner, sx, sb, sc, step_g, rate, end_state, cot, None)
        conv_grads = conv_pullback(
            (dx.reshape(suffix_len, -1), db.reshape(suffix_len, -1), dc.reshape(suffix_len, -1))
        )
        d_dt = one_step_pullback(d_step.reshape(num_heads, suffix_len))[0]
        return conv_grads, d_dt

    suffix_items = (
        suffix_x.astype(jnp.float32),
        suffix_b.astype(jnp.float32),
        suffix_c.astype(jnp.float32),
        suffix_dt,
        suffix_grad.astype(jnp.float32),
        weight,
    )
    adjoints, suffix_inner = jax.vmap(suffix_front, in_axes=(0, 0, 0, 1, 0, 0))(*suffix_items)
    step_g = prompt_step.reshape(num_groups, per_group, prompt_len)
    prompt_inner = block_inner(x_act, b_act, c_act, step_g, rate, gain, prompt_cot)
    core = my_index % 2
    chip = my_index // 2
    num_chips = num_ways // 2
    own_triple = jnp.stack([own_state, own_adjoint, jnp.sum(adjoints, axis=0)])
    partner_triple = lax.ppermute(own_triple, "suf", [(j, j ^ 1) for j in range(num_ways)])
    even = jnp.where(core == 0, own_triple, partner_triple)
    odd = jnp.where(core == 0, partner_triple, own_triple)
    block_decay = jnp.exp(every_log).reshape(num_ways, num_groups, per_group, 1, 1)
    decay_even = lax.dynamic_index_in_dim(block_decay, 2 * chip, 0, False)
    decay_odd = lax.dynamic_index_in_dim(block_decay, 2 * chip + 1, 0, False)
    chip_log = every_log.reshape(num_chips, 2, num_heads).sum(axis=1)
    later_log = jnp.sum(jnp.where((jnp.arange(num_chips) >= chip)[:, None], chip_log, 0.0), axis=0)
    chip_state = decay_odd * even[0] + odd[0]
    chip_adjoint = even[1] + decay_even * odd[1]
    chip_suffix = even[2] + odd[2]
    chip_later = chip_adjoint + jnp.exp(later_log).reshape(num_groups, per_group, 1, 1) * chip_suffix
    got_state = [chip_state]
    got_other = [chip_suffix]
    for shift in range(1, num_chips):
        wraps = chip + shift >= num_chips
        outgoing = jnp.where(core == 0, chip_state, jnp.where(wraps, chip_later, chip_suffix))
        route = [
            (2 * c + k, 2 * ((c + shift) % num_chips) + k) for c in range(num_chips) for k in range(2)
        ]
        incoming = lax.ppermute(outgoing, "suf", route)
        shared = lax.ppermute(incoming, "suf", [(j, j ^ 1) for j in range(num_ways)])
        got_state.append(jnp.where(core == 0, incoming, shared))
        got_other.append(jnp.where(core == 0, shared, incoming))

    def chip_ordered(got):
        ordered = []
        for c in range(num_chips):
            distance = (chip - c) % num_chips
            value = got[0]
            for shift in range(1, num_chips):
                value = jnp.where(distance == shift, got[shift], value)
            ordered.append(value)
        return ordered

    chip_states = chip_ordered(got_state)
    chip_others = chip_ordered(got_other)
    chip_decay = jnp.exp(chip_log).reshape(num_chips, num_groups, per_group, 1, 1)
    running = jnp.zeros_like(own_state)
    chip_start = running
    for c in range(num_chips):
        chip_start = jnp.where(chip == c, running, chip_start)
        running = chip_decay[c] * running + chip_states[c]
    prompt_end_late = running
    running = jnp.zeros_like(own_state)
    for c in range(num_chips):
        running = running + jnp.where(c <= chip, chip_others[c], 0.0)
    chip_end_grad = running
    for c in reversed(range(num_chips)):
        chip_end_grad = jnp.where(chip == c, running, chip_end_grad)
        running = chip_others[c] + chip_decay[c] * running
    start_state = jnp.where(core == 0, chip_start, decay_even * chip_start + even[0])
    end_grad = jnp.where(core == 0, odd[1] + decay_odd * chip_end_grad, chip_end_grad)
    conv_grads, suffix_ddt = jax.vmap(
        suffix_back, in_axes=(None, 0, 0, 0, 0, 1, 0, 0), out_axes=(0, 1)
    )(prompt_end_late, suffix_inner, *suffix_items)
    dx, db, dc, d_step = block_outer(
        prompt_inner, x_act, b_act, c_act, step_g, rate, start_state, prompt_cot, end_grad
    )
    prompt_grads = prompt_conv_pullback(
        (dx.reshape(prompt_len, -1), db.reshape(prompt_len, -1), dc.reshape(prompt_len, -1))
    )
    prefix_ddt = step_pullback(d_step.reshape(num_heads, prompt_len))[0]
    left_grads = jnp.concatenate([prompt_grads[3], prompt_grads[4], prompt_grads[5]], axis=1)
    from_right = from_behind(left_grads, "suf", -1)
    ctx_grads = jnp.concatenate(
        [jnp.sum(conv_grads[3], axis=0), jnp.sum(conv_grads[4], axis=0), jnp.sum(conv_grads[5], axis=0)],
        axis=1,
    )
    from_suffix = ctx_grads
    for sender in range(num_ways - 1):
        from_suffix = from_suffix + lax.ppermute(ctx_grads, "suf", [(sender, num_ways - 1)])
    last_device = my_index == num_ways - 1
    tail_add = split_tokens(from_right + jnp.where(last_device, from_suffix, 0.0))

    def finish(grad_full, extra):
        placed = jnp.pad(extra, ((grad_full.shape[0] - margin, 0), (0, 0)))
        return (grad_full + placed).astype(jnp.bfloat16)

    return (
        finish(prompt_grads[0], tail_add[0]),
        finish(prompt_grads[1], tail_add[1]),
        finish(prompt_grads[2], tail_add[2]),
        prefix_ddt,
        conv_grads[0].astype(jnp.bfloat16),
        conv_grads[1].astype(jnp.bfloat16),
        conv_grads[2].astype(jnp.bfloat16),
        suffix_ddt,
    )


def solution(mesh):
    return jax.shard_map(
        shards,
        mesh=mesh,
        in_specs=(
            P(("grp", "suf"), "head"),
            P(("grp", "suf"), "head"),
            P(("grp", "suf"), "head"),
            P("head", ("grp", "suf")),
            P(("grp", "suf"), "head"),
            P(("grp", "suf"), None, "head"),
            P(("grp", "suf"), None, "head"),
            P(("grp", "suf"), None, "head"),
            P("head", ("grp", "suf"), None),
            P(("grp", "suf"), None, "head"),
            P(("grp", "suf")),
            P(("grp", "suf"), None),
            P(("grp", "suf")),
            P(None, "head"),
            P(None, "head"),
            P(None, "head"),
            P("head"),
            P("head"),
            P("head"),
        ),
        out_specs=(
            P(("grp", "suf"), "head"),
            P(("grp", "suf"), "head"),
            P(("grp", "suf"), "head"),
            P("head", ("grp", "suf")),
            P(("grp", "suf"), None, "head"),
            P(("grp", "suf"), None, "head"),
            P(("grp", "suf"), None, "head"),
            P("head", ("grp", "suf"), None),
        ),
        check_vma=False,
    )
```

```python
import functools

import jax
import jax.numpy as jnp
from jax import lax
from jax.experimental import pallas as pl
from jax.experimental.pallas import tpu as pltpu
from jax.sharding import PartitionSpec as P


HD = 64
N = 128
KW = 4


EXACT_DOT = lax.Precision.HIGHEST


def from_behind(block, axis, distance):
    devices = range(lax.axis_size(axis))
    route = [(i - distance, i) for i in devices if i - distance in devices]
    return lax.ppermute(block, axis, route)


def conv_pre(values, context, taps):
    padded = jnp.concatenate([context, values], axis=0)
    num_tokens = values.shape[0]
    result = padded[0:num_tokens] * taps[0].astype(jnp.float32)
    for tap_index in range(1, taps.shape[0]):
        result = result + padded[tap_index : tap_index + num_tokens] * taps[tap_index].astype(
            jnp.float32
        )
    return result


@jax.custom_vjp
def causal_conv(values, context, taps):
    return jax.nn.silu(conv_pre(values, context, taps))


def _conv_forward(values, context, taps):
    pre = conv_pre(values, context, taps)
    return jax.nn.silu(pre), (pre, taps)


def _conv_backward(saved, d_act):
    pre, taps = saved
    gate = jax.nn.sigmoid(pre)
    d_pre = d_act * (gate + pre * (gate * (1.0 - gate)))
    weights = taps.astype(jnp.float32)
    margin = taps.shape[0] - 1
    d_values = d_pre * weights[margin]
    for tap_index in range(margin):
        shift = margin - tap_index
        d_values = d_values + jnp.pad(d_pre[shift:], ((0, shift), (0, 0))) * weights[tap_index]
    d_context = jnp.stack(
        [
            sum(weights[tap_index] * d_pre[row - tap_index] for tap_index in range(row + 1))
            for row in range(margin)
        ]
    )
    return d_values, d_context, jnp.zeros_like(taps)


causal_conv.defvjp(_conv_forward, _conv_backward)


def _dot(a, b, dims):
    return lax.dot_general(a, b, (dims, ((), ())), precision=EXACT_DOT, preferred_element_type=jnp.float32)


def _grad_kernel(steps_per_group, x_ref, g_ref, b_ref, c_ref, crow_ref, srow_ref, skip_ref,
                 dx_ref, dstep_ref, dcum_ref, dc_ref, db_ref, dsc_ref):
    step_id = pl.program_id(0)
    bb = b_ref[...]
    cc = c_ref[...]
    t_len = bb.shape[0]
    lanes = 2 * HD
    tri = lax.broadcasted_iota(jnp.int32, (t_len, t_len), 0) >= lax.broadcasted_iota(jnp.int32, (t_len, t_len), 1)
    lane = lax.broadcasted_iota(jnp.int32, (1, lanes), 1)
    ones = jnp.ones((8, t_len), jnp.float32)
    scores = _dot(cc, bb, ((1,), (1,)))
    dsc = jnp.zeros((t_len, t_len), jnp.float32)
    for pair in range(dx_ref.shape[1] // lanes):
        cols = slice(pair * lanes, (pair + 1) * lanes)
        x = x_ref[:, cols]
        g = g_ref[:, cols]
        dx = skip_ref[:, cols] * g
        for h in range(2):
            head = 2 * pair + h
            mask = ((lane >= h * HD) & (lane < (h + 1) * HD)).astype(jnp.float32)
            gm = g * mask
            crow = crow_ref[head : head + 1, :]
            srow = srow_ref[head : head + 1, :]
            ccol = jnp.transpose(jnp.broadcast_to(crow, (t_len, t_len)))
            within = jnp.where(tri, jnp.exp(jnp.where(tri, ccol - crow, 0.0)), 0.0)
            score_w = scores * within
            d_mix = _dot(gm, x, ((1,), (1,)))
            dx = dx + _dot(score_w * srow, gm, ((0,), (0,)))
            dsc = dsc + d_mix * within * srow
            q_mat = d_mix * score_w
            p_mat = q_mat * srow
            dstep_ref[head : head + 1, :] = jnp.sum(q_mat, axis=0, keepdims=True)
            dcum_ref[head : head + 1, :] = _dot(ones, p_mat, ((1,), (1,)))[0:1] - jnp.sum(
                p_mat, axis=0, keepdims=True
            )
        dx_ref[:, cols] = dx
    within_group = step_id % steps_per_group

    @pl.when(within_group == 0)
    def _():
        dsc_ref[...] = dsc

    @pl.when(within_group != 0)
    def _():
        dsc_ref[...] += dsc

    @pl.when(within_group == steps_per_group - 1)
    def _():
        total = dsc_ref[...]
        dc_ref[...] = _dot(total, bb, ((1,), (0,)))
        db_ref[...] = _dot(total, cc, ((0,), (0,)))


def block_inner(xa, ba, ca, step, rate, skip, G):
    T, ng, nk, P = xa.shape
    nh = ng * nk
    heads_per_step = 8
    steps_per_group = nk // heads_per_step
    cum = jnp.cumsum(-step * rate[:, :, None], axis=-1)
    row_spec = pl.BlockSpec((heads_per_step, T), lambda j: (j, 0))
    lane_spec = pl.BlockSpec((T, heads_per_step * P), lambda j: (0, j))
    grp_spec = pl.BlockSpec((T, N), lambda j: (0, j // steps_per_group))
    dx2, d_direct, d_cum, dc, db = pl.pallas_call(
        functools.partial(_grad_kernel, steps_per_group),
        grid=(nh // heads_per_step,),
        in_specs=[
            lane_spec, lane_spec, grp_spec, grp_spec, row_spec, row_spec,
            pl.BlockSpec((1, heads_per_step * P), lambda j: (0, j)),
        ],
        out_specs=[lane_spec, row_spec, row_spec, grp_spec, grp_spec],
        out_shape=[
            jax.ShapeDtypeStruct((T, nh * P), jnp.float32),
            jax.ShapeDtypeStruct((nh, T), jnp.float32),
            jax.ShapeDtypeStruct((nh, T), jnp.float32),
            jax.ShapeDtypeStruct((T, ng * N), jnp.float32),
            jax.ShapeDtypeStruct((T, ng * N), jnp.float32),
        ],
        scratch_shapes=[pltpu.VMEM((T, T), jnp.float32)],
    )(
        xa.reshape(T, nh * P),
        G.reshape(T, nh * P),
        ba.reshape(T, ng * N),
        ca.reshape(T, ng * N),
        cum.reshape(nh, T),
        step.reshape(nh, T),
        jnp.repeat(skip.reshape(1, nh), P, axis=1),
    )
    return (
        dx2.reshape(T, ng, nk, P),
        d_direct.reshape(ng, nk, T),
        d_cum.reshape(ng, nk, T),
        dc.reshape(T, ng, N),
        db.reshape(T, ng, N),
        cum,
    )


def block_outer(inner, xa, ba, ca, step, rate, S0, G, lam):
    dx, d_step, d_cum, dc, db, cum = inner
    grow = jnp.exp(cum)
    g_grow = G * grow.transpose(2, 0, 1)[..., None]
    carried = jnp.einsum("tgn,gkpn->tgkp", ca, S0, precision=EXACT_DOT)
    dc = dc + jnp.einsum("tgkp,gkpn->tgn", g_grow, S0, precision=EXACT_DOT)
    d_cum = d_cum + jnp.sum(g_grow * carried, axis=-1).transpose(1, 2, 0)
    if lam is not None:
        to_end = jnp.exp(cum[..., -1:] - cum)
        push = to_end * step
        lam_b = jnp.einsum("gkpn,sgn->sgkp", lam, ba, precision=EXACT_DOT)
        dx = dx + push.transpose(2, 0, 1)[..., None] * lam_b
        db = db + jnp.einsum("gkpn,sgkp,gks->sgn", lam, xa, push, precision=EXACT_DOT)
        q_end = jnp.sum(xa * lam_b, axis=-1).transpose(1, 2, 0)
        d_step = d_step + to_end * q_end
        wq = push * q_end
        end_total = jnp.sum(wq, axis=-1) + jnp.exp(cum[..., -1]) * jnp.sum(lam * S0, axis=(-2, -1))
        d_cum = d_cum - wq
        d_cum = d_cum.at[..., -1].add(end_total)
    d_log = jnp.flip(jnp.cumsum(jnp.flip(d_cum, -1), axis=-1), -1)
    d_step = d_step - rate[:, :, None] * d_log
    return dx, db, dc, d_step


def shards(
    prefix_x,
    prefix_b,
    prefix_c,
    prefix_dt,
    prefix_grad,
    suffix_x,
    suffix_b,
    suffix_c,
    suffix_dt,
    suffix_grad,
    lengths,
    loss_mask,
    advantage,
    conv_x,
    conv_b,
    conv_c,
    decay_rate,
    dt_bias,
    skip,
):
    num_ways = lax.axis_size("suf")
    my_index = lax.axis_index("suf")
    num_heads = decay_rate.shape[0]
    num_groups = conv_b.shape[1] // N
    per_group = num_heads // num_groups
    margin = KW - 1
    prompt_len = prefix_x.shape[0]
    width_x = prefix_x.shape[1]
    width_b = prefix_b.shape[1]
    rate = decay_rate.reshape(num_groups, per_group)
    gain = skip.reshape(num_groups, per_group)

    def split_tokens(tokens):
        return (
            tokens[:, :width_x],
            tokens[:, width_x : width_x + width_b],
            tokens[:, width_x + width_b :],
        )

    def convs(ux, ub, uc, cx, cb, cc):
        return (
            causal_conv(ux, cx, conv_x),
            causal_conv(ub, cb, conv_b),
            causal_conv(uc, cc, conv_c),
        )

    def softplus_of(raw):
        return jax.nn.softplus(raw + dt_bias[:, None])

    prompt_step, step_pullback = jax.vjp(softplus_of, prefix_dt)
    cumulative = jnp.cumsum(-prompt_step * decay_rate[:, None], axis=1)
    total_log = cumulative[:, -1]
    tails = jnp.concatenate(
        [prefix_x[-margin:], prefix_b[-margin:], prefix_c[-margin:]], axis=1
    ).astype(jnp.float32)
    tail_size = tails.size
    own_pack = jnp.concatenate([tails.reshape(-1), total_log])
    received = [own_pack] + [
        lax.ppermute(own_pack, "suf", [(j, (j + shift) % num_ways) for j in range(num_ways)])
        for shift in range(1, num_ways)
    ]
    every = jnp.take(
        jnp.stack(received), (my_index - jnp.arange(num_ways)) % num_ways, axis=0
    )
    every_tails = every[:, :tail_size].reshape((num_ways,) + tails.shape)
    every_log = every[:, tail_size:]
    behind = lax.dynamic_index_in_dim(every_tails, jnp.maximum(my_index - 1, 0), 0, False)
    behind = jnp.where(my_index > 0, behind, 0.0)
    left_x, left_b, left_c = split_tokens(behind)
    ctx_x, ctx_b, ctx_c = split_tokens(every_tails[num_ways - 1])

    acts, prompt_conv_pullback = jax.vjp(
        convs,
        prefix_x.astype(jnp.float32),
        prefix_b.astype(jnp.float32),
        prefix_c.astype(jnp.float32),
        left_x,
        left_b,
        left_c,
    )
    x_act = acts[0].reshape(prompt_len, num_groups, per_group, HD)
    b_act = acts[1].reshape(prompt_len, num_groups, N)
    c_act = acts[2].reshape(prompt_len, num_groups, N)
    prompt_cot = prefix_grad.astype(jnp.float32).reshape(prompt_len, num_groups, per_group, HD)
    push_weight = (jnp.exp(total_log[:, None] - cumulative) * prompt_step).reshape(
        num_groups, per_group, prompt_len
    )
    own_state = jnp.einsum("gkt,tgkp,tgn->gkpn", push_weight, x_act, b_act, precision=EXACT_DOT)
    pull_weight = jnp.exp(cumulative).reshape(num_groups, per_group, prompt_len)
    own_adjoint = jnp.einsum(
        "gkt,tgkp,tgn->gkpn", pull_weight, prompt_cot, c_act, precision=EXACT_DOT
    )
    positions = jnp.arange(suffix_x.shape[1])[None, :]
    weight = (
        advantage[:, None]
        * loss_mask.astype(jnp.float32)
        * (positions < lengths[:, None]).astype(jnp.float32)
    )

    def suffix_parts(x_one, b_one, c_one, dt_one, grad_one, weight_one):
        suffix_len = x_one.shape[0]
        step_one, one_step_pullback = jax.vjp(softplus_of, dt_one)
        s_acts, conv_pullback = jax.vjp(convs, x_one, b_one, c_one, ctx_x, ctx_b, ctx_c)
        sx = s_acts[0].reshape(suffix_len, num_groups, per_group, HD)
        sb = s_acts[1].reshape(suffix_len, num_groups, N)
        sc = s_acts[2].reshape(suffix_len, num_groups, N)
        cot = (weight_one[:, None] * grad_one).reshape(suffix_len, num_groups, per_group, HD)
        step_g = step_one.reshape(num_groups, per_group, suffix_len)
        return one_step_pullback, conv_pullback, sx, sb, sc, cot, step_g

    def suffix_front(*items):
        _, _, sx, sb, sc, cot, step_g = suffix_parts(*items)
        grow = jnp.exp(jnp.cumsum(-step_g * rate[:, :, None], axis=-1))
        adjoint = jnp.einsum("gkt,tgkp,tgn->gkpn", grow, cot, sc, precision=EXACT_DOT)
        inner = block_inner(sx, sb, sc, step_g, rate, gain, cot)
        return adjoint, inner

    def suffix_back(end_state, inner, *items):
        one_step_pullback, conv_pullback, sx, sb, sc, cot, step_g = suffix_parts(*items)
        suffix_len = sx.shape[0]
        dx, db, dc, d_step = block_outer(inner, sx, sb, sc, step_g, rate, end_state, cot, None)
        conv_grads = conv_pullback(
            (dx.reshape(suffix_len, -1), db.reshape(suffix_len, -1), dc.reshape(suffix_len, -1))
        )
        d_dt = one_step_pullback(d_step.reshape(num_heads, suffix_len))[0]
        return conv_grads, d_dt

    suffix_items = (
        suffix_x.astype(jnp.float32),
        suffix_b.astype(jnp.float32),
        suffix_c.astype(jnp.float32),
        suffix_dt,
        suffix_grad.astype(jnp.float32),
        weight,
    )
    adjoints, suffix_inner = jax.vmap(suffix_front, in_axes=(0, 0, 0, 1, 0, 0))(*suffix_items)
    step_g = prompt_step.reshape(num_groups, per_group, prompt_len)
    prompt_inner = block_inner(x_act, b_act, c_act, step_g, rate, gain, prompt_cot)
    core = my_index % 2
    chip = my_index // 2
    num_chips = num_ways // 2
    own_triple = jnp.stack([own_state, own_adjoint, jnp.sum(adjoints, axis=0)])
    partner_triple = lax.ppermute(own_triple, "suf", [(j, j ^ 1) for j in range(num_ways)])
    even = jnp.where(core == 0, own_triple, partner_triple)
    odd = jnp.where(core == 0, partner_triple, own_triple)
    block_decay = jnp.exp(every_log).reshape(num_ways, num_groups, per_group, 1, 1)
    decay_even = lax.dynamic_index_in_dim(block_decay, 2 * chip, 0, False)
    decay_odd = lax.dynamic_index_in_dim(block_decay, 2 * chip + 1, 0, False)
    chip_log = every_log.reshape(num_chips, 2, num_heads).sum(axis=1)
    later_log = jnp.sum(jnp.where((jnp.arange(num_chips) >= chip)[:, None], chip_log, 0.0), axis=0)
    chip_state = decay_odd * even[0] + odd[0]
    chip_adjoint = even[1] + decay_even * odd[1]
    chip_suffix = even[2] + odd[2]
    chip_later = chip_adjoint + jnp.exp(later_log).reshape(num_groups, per_group, 1, 1) * chip_suffix
    got_state = [chip_state]
    got_other = [chip_suffix]
    for shift in range(1, num_chips):
        wraps = chip + shift >= num_chips
        outgoing = jnp.where(core == 0, chip_state, jnp.where(wraps, chip_later, chip_suffix))
        route = [
            (2 * c + k, 2 * ((c + shift) % num_chips) + k) for c in range(num_chips) for k in range(2)
        ]
        incoming = lax.ppermute(outgoing, "suf", route)
        shared = lax.ppermute(incoming, "suf", [(j, j ^ 1) for j in range(num_ways)])
        got_state.append(jnp.where(core == 0, incoming, shared))
        got_other.append(jnp.where(core == 0, shared, incoming))

    def chip_ordered(got):
        ordered = []
        for c in range(num_chips):
            distance = (chip - c) % num_chips
            value = got[0]
            for shift in range(1, num_chips):
                value = jnp.where(distance == shift, got[shift], value)
            ordered.append(value)
        return ordered

    chip_states = chip_ordered(got_state)
    chip_others = chip_ordered(got_other)
    chip_decay = jnp.exp(chip_log).reshape(num_chips, num_groups, per_group, 1, 1)
    running = jnp.zeros_like(own_state)
    chip_start = running
    for c in range(num_chips):
        chip_start = jnp.where(chip == c, running, chip_start)
        running = chip_decay[c] * running + chip_states[c]
    prompt_end_late = running
    running = jnp.zeros_like(own_state)
    for c in range(num_chips):
        running = running + jnp.where(c <= chip, chip_others[c], 0.0)
    chip_end_grad = running
    for c in reversed(range(num_chips)):
        chip_end_grad = jnp.where(chip == c, running, chip_end_grad)
        running = chip_others[c] + chip_decay[c] * running
    start_state = jnp.where(core == 0, chip_start, decay_even * chip_start + even[0])
    end_grad = jnp.where(core == 0, odd[1] + decay_odd * chip_end_grad, chip_end_grad)
    conv_grads, suffix_ddt = jax.vmap(
        suffix_back, in_axes=(None, 0, 0, 0, 0, 1, 0, 0), out_axes=(0, 1)
    )(prompt_end_late, suffix_inner, *suffix_items)
    dx, db, dc, d_step = block_outer(
        prompt_inner, x_act, b_act, c_act, step_g, rate, start_state, prompt_cot, end_grad
    )
    prompt_grads = prompt_conv_pullback(
        (dx.reshape(prompt_len, -1), db.reshape(prompt_len, -1), dc.reshape(prompt_len, -1))
    )
    prefix_ddt = step_pullback(d_step.reshape(num_heads, prompt_len))[0]
    left_grads = jnp.concatenate([prompt_grads[3], prompt_grads[4], prompt_grads[5]], axis=1)
    from_right = from_behind(left_grads, "suf", -1)
    ctx_grads = jnp.concatenate(
        [jnp.sum(conv_grads[3], axis=0), jnp.sum(conv_grads[4], axis=0), jnp.sum(conv_grads[5], axis=0)],
        axis=1,
    )
    from_suffix = ctx_grads
    for sender in range(num_ways - 1):
        from_suffix = from_suffix + lax.ppermute(ctx_grads, "suf", [(sender, num_ways - 1)])
    last_device = my_index == num_ways - 1
    tail_add = split_tokens(from_right + jnp.where(last_device, from_suffix, 0.0))

    def finish(grad_full, extra):
        placed = jnp.pad(extra, ((grad_full.shape[0] - margin, 0), (0, 0)))
        return (grad_full + placed).astype(jnp.bfloat16)

    return (
        finish(prompt_grads[0], tail_add[0]),
        finish(prompt_grads[1], tail_add[1]),
        finish(prompt_grads[2], tail_add[2]),
        prefix_ddt,
        conv_grads[0].astype(jnp.bfloat16),
        conv_grads[1].astype(jnp.bfloat16),
        conv_grads[2].astype(jnp.bfloat16),
        suffix_ddt,
    )


def solution(mesh):
    return jax.shard_map(
        shards,
        mesh=mesh,
        in_specs=(
            P(("grp", "suf"), "head"),
            P(("grp", "suf"), "head"),
            P(("grp", "suf"), "head"),
            P("head", ("grp", "suf")),
            P(("grp", "suf"), "head"),
            P(("grp", "suf"), None, "head"),
            P(("grp", "suf"), None, "head"),
            P(("grp", "suf"), None, "head"),
            P("head", ("grp", "suf"), None),
            P(("grp", "suf"), None, "head"),
            P(("grp", "suf")),
            P(("grp", "suf"), None),
            P(("grp", "suf")),
            P(None, "head"),
            P(None, "head"),
            P(None, "head"),
            P("head"),
            P("head"),
            P("head"),
        ),
        out_specs=(
            P(("grp", "suf"), "head"),
            P(("grp", "suf"), "head"),
            P(("grp", "suf"), "head"),
            P("head", ("grp", "suf")),
            P(("grp", "suf"), None, "head"),
            P(("grp", "suf"), None, "head"),
            P(("grp", "suf"), None, "head"),
            P("head", ("grp", "suf"), None),
        ),
        check_vma=False,
    )
```

```python
import functools

import jax
import jax.numpy as jnp
from jax import lax
from jax.experimental import pallas as pl
from jax.experimental.pallas import tpu as pltpu
from jax.sharding import PartitionSpec as P


HD = 64
N = 128
KW = 4


EXACT_DOT = lax.Precision.HIGHEST


def causal_conv(values, context, taps):
    padded = jnp.concatenate([context, values], axis=0)
    num_tokens = values.shape[0]
    result = padded[0:num_tokens] * taps[0].astype(jnp.float32)
    for tap_index in range(1, taps.shape[0]):
        result = result + padded[tap_index : tap_index + num_tokens] * taps[tap_index].astype(
            jnp.float32
        )
    return jax.nn.silu(result)


def _dot(a, b, dims):
    return lax.dot_general(a, b, (dims, ((), ())), precision=EXACT_DOT, preferred_element_type=jnp.float32)


def _grad_kernel(steps_per_group, x_ref, g_ref, b_ref, c_ref, crow_ref, srow_ref, skip_ref,
                 dx_ref, dstep_ref, dcum_ref, dc_ref, db_ref, dsc_ref):
    step_id = pl.program_id(0)
    bb = b_ref[...]
    cc = c_ref[...]
    t_len = bb.shape[0]
    lanes = 2 * HD
    tri = lax.broadcasted_iota(jnp.int32, (t_len, t_len), 0) >= lax.broadcasted_iota(jnp.int32, (t_len, t_len), 1)
    lane = lax.broadcasted_iota(jnp.int32, (1, lanes), 1)
    ones = jnp.ones((8, t_len), jnp.float32)
    scores = _dot(cc, bb, ((1,), (1,)))
    dsc = jnp.zeros((t_len, t_len), jnp.float32)
    for pair in range(dx_ref.shape[1] // lanes):
        cols = slice(pair * lanes, (pair + 1) * lanes)
        x = x_ref[:, cols]
        g = g_ref[:, cols]
        dx = skip_ref[:, cols] * g
        for h in range(2):
            head = 2 * pair + h
            mask = ((lane >= h * HD) & (lane < (h + 1) * HD)).astype(jnp.float32)
            gm = g * mask
            crow = crow_ref[head : head + 1, :]
            srow = srow_ref[head : head + 1, :]
            ccol = jnp.transpose(jnp.broadcast_to(crow, (t_len, t_len)))
            within = jnp.where(tri, jnp.exp(jnp.where(tri, ccol - crow, 0.0)), 0.0)
            score_w = scores * within
            d_mix = _dot(gm, x, ((1,), (1,)))
            dx = dx + _dot(score_w * srow, gm, ((0,), (0,)))
            dsc = dsc + d_mix * within * srow
            q_mat = d_mix * score_w
            p_mat = q_mat * srow
            dstep_ref[head : head + 1, :] = jnp.sum(q_mat, axis=0, keepdims=True)
            dcum_ref[head : head + 1, :] = _dot(ones, p_mat, ((1,), (1,)))[0:1] - jnp.sum(
                p_mat, axis=0, keepdims=True
            )
        dx_ref[:, cols] = dx
    within_group = step_id % steps_per_group

    @pl.when(within_group == 0)
    def _():
        dsc_ref[...] = dsc

    @pl.when(within_group != 0)
    def _():
        dsc_ref[...] += dsc

    @pl.when(within_group == steps_per_group - 1)
    def _():
        total = dsc_ref[...]
        dc_ref[...] = _dot(total, bb, ((1,), (0,)))
        db_ref[...] = _dot(total, cc, ((0,), (0,)))


def block_inner(xa, ba, ca, step, rate, skip, G):
    T, ng, nk, P = xa.shape
    nh = ng * nk
    heads_per_step = 8
    steps_per_group = nk // heads_per_step
    cum = jnp.cumsum(-step * rate[:, :, None], axis=-1)
    row_spec = pl.BlockSpec((heads_per_step, T), lambda j: (j, 0))
    lane_spec = pl.BlockSpec((T, heads_per_step * P), lambda j: (0, j))
    grp_spec = pl.BlockSpec((T, N), lambda j: (0, j // steps_per_group))
    dx2, d_direct, d_cum, dc, db = pl.pallas_call(
        functools.partial(_grad_kernel, steps_per_group),
        grid=(nh // heads_per_step,),
        in_specs=[
            lane_spec, lane_spec, grp_spec, grp_spec, row_spec, row_spec,
            pl.BlockSpec((1, heads_per_step * P), lambda j: (0, j)),
        ],
        out_specs=[lane_spec, row_spec, row_spec, grp_spec, grp_spec],
        out_shape=[
            jax.ShapeDtypeStruct((T, nh * P), jnp.float32),
            jax.ShapeDtypeStruct((nh, T), jnp.float32),
            jax.ShapeDtypeStruct((nh, T), jnp.float32),
            jax.ShapeDtypeStruct((T, ng * N), jnp.float32),
            jax.ShapeDtypeStruct((T, ng * N), jnp.float32),
        ],
        scratch_shapes=[pltpu.VMEM((T, T), jnp.float32)],
    )(
        xa.reshape(T, nh * P),
        G.reshape(T, nh * P),
        ba.reshape(T, ng * N),
        ca.reshape(T, ng * N),
        cum.reshape(nh, T),
        step.reshape(nh, T),
        jnp.repeat(skip.reshape(1, nh), P, axis=1),
    )
    return (
        dx2.reshape(T, ng, nk, P),
        d_direct.reshape(ng, nk, T),
        d_cum.reshape(ng, nk, T),
        dc.reshape(T, ng, N),
        db.reshape(T, ng, N),
        cum,
    )


def block_outer(inner, xa, ba, ca, step, rate, S0, G, lam):
    dx, d_step, d_cum, dc, db, cum = inner
    grow = jnp.exp(cum)
    g_grow = G * grow.transpose(2, 0, 1)[..., None]
    carried = jnp.einsum("tgn,gkpn->tgkp", ca, S0, precision=EXACT_DOT)
    dc = dc + jnp.einsum("tgkp,gkpn->tgn", g_grow, S0, precision=EXACT_DOT)
    d_cum = d_cum + jnp.sum(g_grow * carried, axis=-1).transpose(1, 2, 0)
    if lam is not None:
        to_end = jnp.exp(cum[..., -1:] - cum)
        push = to_end * step
        lam_b = jnp.einsum("gkpn,sgn->sgkp", lam, ba, precision=EXACT_DOT)
        dx = dx + push.transpose(2, 0, 1)[..., None] * lam_b
        db = db + jnp.einsum("gkpn,sgkp,gks->sgn", lam, xa, push, precision=EXACT_DOT)
        q_end = jnp.sum(xa * lam_b, axis=-1).transpose(1, 2, 0)
        d_step = d_step + to_end * q_end
        wq = push * q_end
        end_total = jnp.sum(wq, axis=-1) + jnp.exp(cum[..., -1]) * jnp.sum(lam * S0, axis=(-2, -1))
        d_cum = d_cum - wq
        d_cum = d_cum.at[..., -1].add(end_total)
    d_log = jnp.flip(jnp.cumsum(jnp.flip(d_cum, -1), axis=-1), -1)
    d_step = d_step - rate[:, :, None] * d_log
    return dx, db, dc, d_step


def shards(
    prefix_x,
    prefix_b,
    prefix_c,
    prefix_dt,
    prefix_grad,
    suffix_x,
    suffix_b,
    suffix_c,
    suffix_dt,
    suffix_grad,
    lengths,
    loss_mask,
    advantage,
    conv_x,
    conv_b,
    conv_c,
    decay_rate,
    dt_bias,
    skip,
):
    num_ways = lax.axis_size("suf")
    my_index = lax.axis_index("suf")
    num_heads = decay_rate.shape[0]
    num_groups = conv_b.shape[1] // N
    per_group = num_heads // num_groups
    margin = KW - 1
    prompt_len = prefix_x.shape[0]
    width_x = prefix_x.shape[1]
    width_b = prefix_b.shape[1]
    rate = decay_rate.reshape(num_groups, per_group)
    gain = skip.reshape(num_groups, per_group)

    def split_tokens(tokens):
        return (
            tokens[:, :width_x],
            tokens[:, width_x : width_x + width_b],
            tokens[:, width_x + width_b :],
        )

    def convs(ux, ub, uc, cx, cb, cc):
        return (
            causal_conv(ux, cx, conv_x),
            causal_conv(ub, cb, conv_b),
            causal_conv(uc, cc, conv_c),
        )

    def softplus_of(raw):
        return jax.nn.softplus(raw + dt_bias[:, None])

    prompt_step, step_pullback = jax.vjp(softplus_of, prefix_dt)
    cumulative = jnp.cumsum(-prompt_step * decay_rate[:, None], axis=1)
    total_log = cumulative[:, -1]
    tails = jnp.concatenate(
        [prefix_x[-margin:], prefix_b[-margin:], prefix_c[-margin:]], axis=1
    ).astype(jnp.float32)
    tail_size = tails.size
    own_pack = jnp.concatenate([tails.reshape(-1), total_log])
    received = [own_pack] + [
        lax.ppermute(own_pack, "suf", [(j, (j + shift) % num_ways) for j in range(num_ways)])
        for shift in range(1, num_ways)
    ]
    every = jnp.take(
        jnp.stack(received), (my_index - jnp.arange(num_ways)) % num_ways, axis=0
    )
    every_tails = every[:, :tail_size].reshape((num_ways,) + tails.shape)
    every_log = every[:, tail_size:]
    behind = lax.dynamic_index_in_dim(every_tails, jnp.maximum(my_index - 1, 0), 0, False)
    behind = jnp.where(my_index > 0, behind, 0.0)
    left_x, left_b, left_c = split_tokens(behind)
    ctx_x, ctx_b, ctx_c = split_tokens(every_tails[num_ways - 1])

    acts, prompt_conv_pullback = jax.vjp(
        convs,
        prefix_x.astype(jnp.float32),
        prefix_b.astype(jnp.float32),
        prefix_c.astype(jnp.float32),
        left_x,
        left_b,
        left_c,
    )
    x_act = acts[0].reshape(prompt_len, num_groups, per_group, HD)
    b_act = acts[1].reshape(prompt_len, num_groups, N)
    c_act = acts[2].reshape(prompt_len, num_groups, N)
    prompt_cot = prefix_grad.astype(jnp.float32).reshape(prompt_len, num_groups, per_group, HD)
    push_weight = (jnp.exp(total_log[:, None] - cumulative) * prompt_step).reshape(
        num_groups, per_group, prompt_len
    )
    own_state = jnp.einsum("gkt,tgkp,tgn->gkpn", push_weight, x_act, b_act, precision=EXACT_DOT)
    pull_weight = jnp.exp(cumulative).reshape(num_groups, per_group, prompt_len)
    own_adjoint = jnp.einsum(
        "gkt,tgkp,tgn->gkpn", pull_weight, prompt_cot, c_act, precision=EXACT_DOT
    )
    positions = jnp.arange(suffix_x.shape[1])[None, :]
    weight = (
        advantage[:, None]
        * loss_mask.astype(jnp.float32)
        * (positions < lengths[:, None]).astype(jnp.float32)
    )

    def suffix_parts(x_one, b_one, c_one, dt_one, grad_one, weight_one):
        suffix_len = x_one.shape[0]
        step_one, one_step_pullback = jax.vjp(softplus_of, dt_one)
        s_acts, conv_pullback = jax.vjp(convs, x_one, b_one, c_one, ctx_x, ctx_b, ctx_c)
        sx = s_acts[0].reshape(suffix_len, num_groups, per_group, HD)
        sb = s_acts[1].reshape(suffix_len, num_groups, N)
        sc = s_acts[2].reshape(suffix_len, num_groups, N)
        cot = (weight_one[:, None] * grad_one).reshape(suffix_len, num_groups, per_group, HD)
        step_g = step_one.reshape(num_groups, per_group, suffix_len)
        return one_step_pullback, conv_pullback, sx, sb, sc, cot, step_g

    def suffix_front(*items):
        _, _, sx, sb, sc, cot, step_g = suffix_parts(*items)
        grow = jnp.exp(jnp.cumsum(-step_g * rate[:, :, None], axis=-1))
        adjoint = jnp.einsum("gkt,tgkp,tgn->gkpn", grow, cot, sc, precision=EXACT_DOT)
        inner = block_inner(sx, sb, sc, step_g, rate, gain, cot)
        return adjoint, inner

    def suffix_back(end_state, inner, *items):
        one_step_pullback, conv_pullback, sx, sb, sc, cot, step_g = suffix_parts(*items)
        suffix_len = sx.shape[0]
        dx, db, dc, d_step = block_outer(inner, sx, sb, sc, step_g, rate, end_state, cot, None)
        conv_grads = conv_pullback(
            (dx.reshape(suffix_len, -1), db.reshape(suffix_len, -1), dc.reshape(suffix_len, -1))
        )
        d_dt = one_step_pullback(d_step.reshape(num_heads, suffix_len))[0]
        return conv_grads, d_dt

    suffix_items = (
        suffix_x.astype(jnp.float32),
        suffix_b.astype(jnp.float32),
        suffix_c.astype(jnp.float32),
        suffix_dt,
        suffix_grad.astype(jnp.float32),
        weight,
    )
    adjoints, suffix_inner = jax.vmap(suffix_front, in_axes=(0, 0, 0, 1, 0, 0))(*suffix_items)
    step_g = prompt_step.reshape(num_groups, per_group, prompt_len)
    prompt_inner = block_inner(x_act, b_act, c_act, step_g, rate, gain, prompt_cot)
    core = my_index % 2
    chip = my_index // 2
    num_chips = num_ways // 2
    own_triple = jnp.stack([own_state, own_adjoint, jnp.sum(adjoints, axis=0)])
    partner_triple = lax.ppermute(own_triple, "suf", [(j, j ^ 1) for j in range(num_ways)])
    even = jnp.where(core == 0, own_triple, partner_triple)
    odd = jnp.where(core == 0, partner_triple, own_triple)
    block_decay = jnp.exp(every_log).reshape(num_ways, num_groups, per_group, 1, 1)
    decay_even = lax.dynamic_index_in_dim(block_decay, 2 * chip, 0, False)
    decay_odd = lax.dynamic_index_in_dim(block_decay, 2 * chip + 1, 0, False)
    chip_log = every_log.reshape(num_chips, 2, num_heads).sum(axis=1)
    later_log = jnp.sum(jnp.where((jnp.arange(num_chips) >= chip)[:, None], chip_log, 0.0), axis=0)
    chip_state = decay_odd * even[0] + odd[0]
    chip_adjoint = even[1] + decay_even * odd[1]
    chip_suffix = even[2] + odd[2]
    chip_later = chip_adjoint + jnp.exp(later_log).reshape(num_groups, per_group, 1, 1) * chip_suffix
    got_state = [chip_state]
    got_other = [chip_suffix]
    for shift in range(1, num_chips):
        wraps = chip + shift >= num_chips
        outgoing = jnp.where(core == 0, chip_state, jnp.where(wraps, chip_later, chip_suffix))
        route = [
            (2 * c + k, 2 * ((c + shift) % num_chips) + k) for c in range(num_chips) for k in range(2)
        ]
        incoming = lax.ppermute(outgoing, "suf", route)
        shared = lax.ppermute(incoming, "suf", [(j, j ^ 1) for j in range(num_ways)])
        got_state.append(jnp.where(core == 0, incoming, shared))
        got_other.append(jnp.where(core == 0, shared, incoming))

    def chip_ordered(got):
        ordered = []
        for c in range(num_chips):
            distance = (chip - c) % num_chips
            value = got[0]
            for shift in range(1, num_chips):
                value = jnp.where(distance == shift, got[shift], value)
            ordered.append(value)
        return ordered

    chip_states = chip_ordered(got_state)
    chip_others = chip_ordered(got_other)
    chip_decay = jnp.exp(chip_log).reshape(num_chips, num_groups, per_group, 1, 1)
    running = jnp.zeros_like(own_state)
    chip_start = running
    for c in range(num_chips):
        chip_start = jnp.where(chip == c, running, chip_start)
        running = chip_decay[c] * running + chip_states[c]
    prompt_end_late = running
    running = jnp.zeros_like(own_state)
    for c in range(num_chips):
        running = running + jnp.where(c <= chip, chip_others[c], 0.0)
    chip_end_grad = running
    for c in reversed(range(num_chips)):
        chip_end_grad = jnp.where(chip == c, running, chip_end_grad)
        running = chip_others[c] + chip_decay[c] * running
    start_state = jnp.where(core == 0, chip_start, decay_even * chip_start + even[0])
    end_grad = jnp.where(core == 0, odd[1] + decay_odd * chip_end_grad, chip_end_grad)
    conv_grads, suffix_ddt = jax.vmap(
        suffix_back, in_axes=(None, 0, 0, 0, 0, 1, 0, 0), out_axes=(0, 1)
    )(prompt_end_late, suffix_inner, *suffix_items)
    dx, db, dc, d_step = block_outer(
        prompt_inner, x_act, b_act, c_act, step_g, rate, start_state, prompt_cot, end_grad
    )
    prompt_grads = prompt_conv_pullback(
        (dx.reshape(prompt_len, -1), db.reshape(prompt_len, -1), dc.reshape(prompt_len, -1))
    )
    prefix_ddt = step_pullback(d_step.reshape(num_heads, prompt_len))[0]
    left_grads = jnp.concatenate([prompt_grads[3], prompt_grads[4], prompt_grads[5]], axis=1)
    ctx_grads = jnp.concatenate(
        [jnp.sum(conv_grads[3], axis=0), jnp.sum(conv_grads[4], axis=0), jnp.sum(conv_grads[5], axis=0)],
        axis=1,
    )
    from_right = lax.ppermute(
        jnp.where(my_index == 0, ctx_grads, left_grads),
        "suf",
        [(j, (j - 1) % num_ways) for j in range(num_ways)],
    )
    from_suffix = ctx_grads
    for sender in range(1, num_ways - 1):
        from_suffix = from_suffix + lax.ppermute(ctx_grads, "suf", [(sender, num_ways - 1)])
    last_device = my_index == num_ways - 1
    tail_add = split_tokens(from_right + jnp.where(last_device, from_suffix, 0.0))

    def finish(grad_full, extra):
        placed = jnp.pad(extra, ((grad_full.shape[0] - margin, 0), (0, 0)))
        return (grad_full + placed).astype(jnp.bfloat16)

    return (
        finish(prompt_grads[0], tail_add[0]),
        finish(prompt_grads[1], tail_add[1]),
        finish(prompt_grads[2], tail_add[2]),
        prefix_ddt,
        conv_grads[0].astype(jnp.bfloat16),
        conv_grads[1].astype(jnp.bfloat16),
        conv_grads[2].astype(jnp.bfloat16),
        suffix_ddt,
    )


def solution(mesh):
    return jax.shard_map(
        shards,
        mesh=mesh,
        in_specs=(
            P(("grp", "suf"), "head"),
            P(("grp", "suf"), "head"),
            P(("grp", "suf"), "head"),
            P("head", ("grp", "suf")),
            P(("grp", "suf"), "head"),
            P(("grp", "suf"), None, "head"),
            P(("grp", "suf"), None, "head"),
            P(("grp", "suf"), None, "head"),
            P("head", ("grp", "suf"), None),
            P(("grp", "suf"), None, "head"),
            P(("grp", "suf")),
            P(("grp", "suf"), None),
            P(("grp", "suf")),
            P(None, "head"),
            P(None, "head"),
            P(None, "head"),
            P("head"),
            P("head"),
            P("head"),
        ),
        out_specs=(
            P(("grp", "suf"), "head"),
            P(("grp", "suf"), "head"),
            P(("grp", "suf"), "head"),
            P("head", ("grp", "suf")),
            P(("grp", "suf"), None, "head"),
            P(("grp", "suf"), None, "head"),
            P(("grp", "suf"), None, "head"),
            P("head", ("grp", "suf"), None),
        ),
        check_vma=False,
    )
```

```python
import functools

import jax
import jax.numpy as jnp
from jax import lax
from jax.experimental import pallas as pl
from jax.experimental.pallas import tpu as pltpu
from jax.sharding import PartitionSpec as P


HD = 64
N = 128
KW = 4


EXACT_DOT = lax.Precision.HIGHEST


def from_behind(block, axis, distance):
    devices = range(lax.axis_size(axis))
    route = [(i - distance, i) for i in devices if i - distance in devices]
    return lax.ppermute(block, axis, route)


def causal_conv(values, context, taps):
    padded = jnp.concatenate([context, values], axis=0)
    num_tokens = values.shape[0]
    result = padded[0:num_tokens] * taps[0].astype(jnp.float32)
    for tap_index in range(1, taps.shape[0]):
        result = result + padded[tap_index : tap_index + num_tokens] * taps[tap_index].astype(
            jnp.float32
        )
    return jax.nn.silu(result)


def _dot(a, b, dims):
    return lax.dot_general(a, b, (dims, ((), ())), precision=EXACT_DOT, preferred_element_type=jnp.float32)


def _grad_kernel(steps_per_group, x_ref, g_ref, b_ref, c_ref, crow_ref, srow_ref, skip_ref,
                 dx_ref, dstep_ref, dcum_ref, dc_ref, db_ref, dsc_ref):
    step_id = pl.program_id(0)
    bb = b_ref[...]
    cc = c_ref[...]
    t_len = bb.shape[0]
    lanes = 2 * HD
    tri = lax.broadcasted_iota(jnp.int32, (t_len, t_len), 0) >= lax.broadcasted_iota(jnp.int32, (t_len, t_len), 1)
    lane = lax.broadcasted_iota(jnp.int32, (1, lanes), 1)
    ones = jnp.ones((8, t_len), jnp.float32)
    scores = _dot(cc, bb, ((1,), (1,)))
    dsc = jnp.zeros((t_len, t_len), jnp.float32)
    for pair in range(dx_ref.shape[1] // lanes):
        cols = slice(pair * lanes, (pair + 1) * lanes)
        x = x_ref[:, cols]
        g = g_ref[:, cols]
        dx = skip_ref[:, cols] * g
        for h in range(2):
            head = 2 * pair + h
            mask = ((lane >= h * HD) & (lane < (h + 1) * HD)).astype(jnp.float32)
            gm = g * mask
            crow = crow_ref[head : head + 1, :]
            srow = srow_ref[head : head + 1, :]
            ccol = jnp.transpose(jnp.broadcast_to(crow, (t_len, t_len)))
            within = jnp.where(tri, jnp.exp(jnp.where(tri, ccol - crow, 0.0)), 0.0)
            score_w = scores * within
            d_mix = _dot(gm, x, ((1,), (1,)))
            dx = dx + _dot(score_w * srow, gm, ((0,), (0,)))
            dsc = dsc + d_mix * within * srow
            q_mat = d_mix * score_w
            p_mat = q_mat * srow
            dstep_ref[head : head + 1, :] = jnp.sum(q_mat, axis=0, keepdims=True)
            dcum_ref[head : head + 1, :] = _dot(ones, p_mat, ((1,), (1,)))[0:1] - jnp.sum(
                p_mat, axis=0, keepdims=True
            )
        dx_ref[:, cols] = dx
    within_group = step_id % steps_per_group

    @pl.when(within_group == 0)
    def _():
        dsc_ref[...] = dsc

    @pl.when(within_group != 0)
    def _():
        dsc_ref[...] += dsc

    @pl.when(within_group == steps_per_group - 1)
    def _():
        total = dsc_ref[...]
        dc_ref[...] = _dot(total, bb, ((1,), (0,)))
        db_ref[...] = _dot(total, cc, ((0,), (0,)))


def block_inner(xa, ba, ca, step, rate, skip, G):
    T, ng, nk, P = xa.shape
    nh = ng * nk
    heads_per_step = 8
    steps_per_group = nk // heads_per_step
    cum = jnp.cumsum(-step * rate[:, :, None], axis=-1)
    row_spec = pl.BlockSpec((heads_per_step, T), lambda j: (j, 0))
    lane_spec = pl.BlockSpec((T, heads_per_step * P), lambda j: (0, j))
    grp_spec = pl.BlockSpec((T, N), lambda j: (0, j // steps_per_group))
    dx2, d_direct, d_cum, dc, db = pl.pallas_call(
        functools.partial(_grad_kernel, steps_per_group),
        grid=(nh // heads_per_step,),
        in_specs=[
            lane_spec, lane_spec, grp_spec, grp_spec, row_spec, row_spec,
            pl.BlockSpec((1, heads_per_step * P), lambda j: (0, j)),
        ],
        out_specs=[lane_spec, row_spec, row_spec, grp_spec, grp_spec],
        out_shape=[
            jax.ShapeDtypeStruct((T, nh * P), jnp.float32),
            jax.ShapeDtypeStruct((nh, T), jnp.float32),
            jax.ShapeDtypeStruct((nh, T), jnp.float32),
            jax.ShapeDtypeStruct((T, ng * N), jnp.float32),
            jax.ShapeDtypeStruct((T, ng * N), jnp.float32),
        ],
        scratch_shapes=[pltpu.VMEM((T, T), jnp.float32)],
    )(
        xa.reshape(T, nh * P),
        G.reshape(T, nh * P),
        ba.reshape(T, ng * N),
        ca.reshape(T, ng * N),
        cum.reshape(nh, T),
        step.reshape(nh, T),
        jnp.repeat(skip.reshape(1, nh), P, axis=1),
    )
    return (
        dx2.reshape(T, ng, nk, P),
        d_direct.reshape(ng, nk, T),
        d_cum.reshape(ng, nk, T),
        dc.reshape(T, ng, N),
        db.reshape(T, ng, N),
        cum,
    )


def block_outer(inner, xa, ba, ca, step, rate, S0, G, lam):
    dx, d_step, d_cum, dc, db, cum = inner
    grow = jnp.exp(cum)
    g_grow = G * grow.transpose(2, 0, 1)[..., None]
    carried = jnp.einsum("tgn,gkpn->tgkp", ca, S0, precision=EXACT_DOT)
    dc = dc + jnp.einsum("tgkp,gkpn->tgn", g_grow, S0, precision=EXACT_DOT)
    d_cum = d_cum + jnp.sum(g_grow * carried, axis=-1).transpose(1, 2, 0)
    if lam is not None:
        to_end = jnp.exp(cum[..., -1:] - cum)
        push = to_end * step
        lam_b = jnp.einsum("gkpn,sgn->sgkp", lam, ba, precision=EXACT_DOT)
        dx = dx + push.transpose(2, 0, 1)[..., None] * lam_b
        db = db + jnp.einsum("gkpn,sgkp,gks->sgn", lam, xa, push, precision=EXACT_DOT)
        q_end = jnp.sum(xa * lam_b, axis=-1).transpose(1, 2, 0)
        d_step = d_step + to_end * q_end
        wq = push * q_end
        end_total = jnp.sum(wq, axis=-1) + jnp.exp(cum[..., -1]) * jnp.sum(lam * S0, axis=(-2, -1))
        d_cum = d_cum - wq
        d_cum = d_cum.at[..., -1].add(end_total)
    d_log = jnp.flip(jnp.cumsum(jnp.flip(d_cum, -1), axis=-1), -1)
    d_step = d_step - rate[:, :, None] * d_log
    return dx, db, dc, d_step


def shards(
    prefix_x,
    prefix_b,
    prefix_c,
    prefix_dt,
    prefix_grad,
    suffix_x,
    suffix_b,
    suffix_c,
    suffix_dt,
    suffix_grad,
    lengths,
    loss_mask,
    advantage,
    conv_x,
    conv_b,
    conv_c,
    decay_rate,
    dt_bias,
    skip,
):
    num_ways = lax.axis_size("suf")
    my_index = lax.axis_index("suf")
    num_heads = decay_rate.shape[0]
    num_groups = conv_b.shape[1] // N
    per_group = num_heads // num_groups
    margin = KW - 1
    prompt_len = prefix_x.shape[0]
    width_x = prefix_x.shape[1]
    width_b = prefix_b.shape[1]
    rate = decay_rate.reshape(num_groups, per_group)
    gain = skip.reshape(num_groups, per_group)

    def split_tokens(tokens):
        return (
            tokens[:, :width_x],
            tokens[:, width_x : width_x + width_b],
            tokens[:, width_x + width_b :],
        )

    def convs(ux, ub, uc, cx, cb, cc):
        return (
            causal_conv(ux, cx, conv_x),
            causal_conv(ub, cb, conv_b),
            causal_conv(uc, cc, conv_c),
        )

    def softplus_of(raw):
        return jax.nn.softplus(raw + dt_bias[:, None])

    prompt_step, step_pullback = jax.vjp(softplus_of, prefix_dt)
    cumulative = jnp.cumsum(-prompt_step * decay_rate[:, None], axis=1)
    total_log = cumulative[:, -1]
    tails = jnp.concatenate(
        [prefix_x[-margin:], prefix_b[-margin:], prefix_c[-margin:]], axis=1
    ).astype(jnp.float32)
    tail_size = tails.size
    own_pack = jnp.concatenate([tails.reshape(-1), total_log])
    received = [own_pack] + [
        lax.ppermute(own_pack, "suf", [(j, (j + shift) % num_ways) for j in range(num_ways)])
        for shift in range(1, num_ways)
    ]
    every = jnp.take(
        jnp.stack(received), (my_index - jnp.arange(num_ways)) % num_ways, axis=0
    )
    every_tails = every[:, :tail_size].reshape((num_ways,) + tails.shape)
    every_log = every[:, tail_size:]
    behind = lax.dynamic_index_in_dim(every_tails, jnp.maximum(my_index - 1, 0), 0, False)
    behind = jnp.where(my_index > 0, behind, 0.0)
    left_x, left_b, left_c = split_tokens(behind)
    ctx_x, ctx_b, ctx_c = split_tokens(every_tails[num_ways - 1])

    acts, prompt_conv_pullback = jax.vjp(
        convs,
        prefix_x.astype(jnp.float32),
        prefix_b.astype(jnp.float32),
        prefix_c.astype(jnp.float32),
        left_x,
        left_b,
        left_c,
    )
    x_act = acts[0].reshape(prompt_len, num_groups, per_group, HD)
    b_act = acts[1].reshape(prompt_len, num_groups, N)
    c_act = acts[2].reshape(prompt_len, num_groups, N)
    prompt_cot = prefix_grad.astype(jnp.float32).reshape(prompt_len, num_groups, per_group, HD)
    push_weight = (jnp.exp(total_log[:, None] - cumulative) * prompt_step).reshape(
        num_groups, per_group, prompt_len
    )
    own_state = jnp.einsum("gkt,tgkp,tgn->gkpn", push_weight, x_act, b_act, precision=EXACT_DOT)
    pull_weight = jnp.exp(cumulative).reshape(num_groups, per_group, prompt_len)
    own_adjoint = jnp.einsum(
        "gkt,tgkp,tgn->gkpn", pull_weight, prompt_cot, c_act, precision=EXACT_DOT
    )
    positions = jnp.arange(suffix_x.shape[1])[None, :]
    weight = (
        advantage[:, None]
        * loss_mask.astype(jnp.float32)
        * (positions < lengths[:, None]).astype(jnp.float32)
    )

    def suffix_parts(x_one, b_one, c_one, dt_one, grad_one, weight_one):
        suffix_len = x_one.shape[0]
        step_one, one_step_pullback = jax.vjp(softplus_of, dt_one)
        s_acts, conv_pullback = jax.vjp(convs, x_one, b_one, c_one, ctx_x, ctx_b, ctx_c)
        sx = s_acts[0].reshape(suffix_len, num_groups, per_group, HD)
        sb = s_acts[1].reshape(suffix_len, num_groups, N)
        sc = s_acts[2].reshape(suffix_len, num_groups, N)
        cot = (weight_one[:, None] * grad_one).reshape(suffix_len, num_groups, per_group, HD)
        step_g = step_one.reshape(num_groups, per_group, suffix_len)
        return one_step_pullback, conv_pullback, sx, sb, sc, cot, step_g

    def suffix_front(*items):
        _, _, sx, sb, sc, cot, step_g = suffix_parts(*items)
        grow = jnp.exp(jnp.cumsum(-step_g * rate[:, :, None], axis=-1))
        adjoint = jnp.einsum("gkt,tgkp,tgn->gkpn", grow, cot, sc, precision=EXACT_DOT)
        inner = block_inner(sx, sb, sc, step_g, rate, gain, cot)
        return adjoint, inner

    def suffix_back(end_state, inner, *items):
        one_step_pullback, conv_pullback, sx, sb, sc, cot, step_g = suffix_parts(*items)
        suffix_len = sx.shape[0]
        dx, db, dc, d_step = block_outer(inner, sx, sb, sc, step_g, rate, end_state, cot, None)
        conv_grads = conv_pullback(
            (dx.reshape(suffix_len, -1), db.reshape(suffix_len, -1), dc.reshape(suffix_len, -1))
        )
        d_dt = one_step_pullback(d_step.reshape(num_heads, suffix_len))[0]
        return conv_grads, d_dt

    suffix_items = (
        suffix_x.astype(jnp.float32),
        suffix_b.astype(jnp.float32),
        suffix_c.astype(jnp.float32),
        suffix_dt,
        suffix_grad.astype(jnp.float32),
        weight,
    )
    adjoints, suffix_inner = jax.vmap(suffix_front, in_axes=(0, 0, 0, 1, 0, 0))(*suffix_items)
    step_g = prompt_step.reshape(num_groups, per_group, prompt_len)
    prompt_inner = block_inner(x_act, b_act, c_act, step_g, rate, gain, prompt_cot)
    core = my_index % 2
    chip = my_index // 2
    num_chips = num_ways // 2
    own_triple = jnp.stack([own_state, own_adjoint, jnp.sum(adjoints, axis=0)])
    partner_triple = lax.ppermute(own_triple, "suf", [(j, j ^ 1) for j in range(num_ways)])
    on_even = core == 0
    block_decay = jnp.exp(every_log).reshape(num_ways, num_groups, per_group, 1, 1)
    decay_even = lax.dynamic_index_in_dim(block_decay, 2 * chip, 0, False)
    decay_odd = lax.dynamic_index_in_dim(block_decay, 2 * chip + 1, 0, False)
    chip_log = every_log.reshape(num_chips, 2, num_heads).sum(axis=1)
    later_log = jnp.sum(jnp.where((jnp.arange(num_chips) >= chip)[:, None], chip_log, 0.0), axis=0)
    chip_state = decay_odd * jnp.where(on_even, own_state, partner_triple[0]) + jnp.where(
        on_even, partner_triple[0], own_state
    )
    chip_adjoint = jnp.where(on_even, own_adjoint, partner_triple[1]) + decay_even * jnp.where(
        on_even, partner_triple[1], own_adjoint
    )
    chip_suffix = own_triple[2] + partner_triple[2]
    chip_later = chip_adjoint + jnp.exp(later_log).reshape(num_groups, per_group, 1, 1) * chip_suffix
    got_state = [chip_state]
    got_other = [chip_suffix]
    for shift in range(1, num_chips):
        wraps = chip + shift >= num_chips
        outgoing = jnp.where(core == 0, chip_state, jnp.where(wraps, chip_later, chip_suffix))
        route = [
            (2 * c + k, 2 * ((c + shift) % num_chips) + k) for c in range(num_chips) for k in range(2)
        ]
        incoming = lax.ppermute(outgoing, "suf", route)
        shared = lax.ppermute(incoming, "suf", [(j, j ^ 1) for j in range(num_ways)])
        got_state.append(jnp.where(core == 0, incoming, shared))
        got_other.append(jnp.where(core == 0, shared, incoming))

    def chip_ordered(got):
        ordered = []
        for c in range(num_chips):
            distance = (chip - c) % num_chips
            value = got[0]
            for shift in range(1, num_chips):
                value = jnp.where(distance == shift, got[shift], value)
            ordered.append(value)
        return ordered

    chip_states = chip_ordered(got_state)
    chip_others = chip_ordered(got_other)
    chip_decay = jnp.exp(chip_log).reshape(num_chips, num_groups, per_group, 1, 1)
    running = jnp.zeros_like(own_state)
    chip_start = running
    for c in range(num_chips):
        chip_start = jnp.where(chip == c, running, chip_start)
        running = chip_decay[c] * running + chip_states[c]
    prompt_end_late = running
    running = jnp.zeros_like(own_state)
    for c in range(num_chips):
        running = running + jnp.where(c <= chip, chip_others[c], 0.0)
    chip_end_grad = running
    for c in reversed(range(num_chips)):
        chip_end_grad = jnp.where(chip == c, running, chip_end_grad)
        running = chip_others[c] + chip_decay[c] * running
    start_state = jnp.where(on_even, chip_start, decay_even * chip_start + partner_triple[0])
    end_grad = jnp.where(on_even, partner_triple[1] + decay_odd * chip_end_grad, chip_end_grad)
    conv_grads, suffix_ddt = jax.vmap(
        suffix_back, in_axes=(None, 0, 0, 0, 0, 1, 0, 0), out_axes=(0, 1)
    )(prompt_end_late, suffix_inner, *suffix_items)
    dx, db, dc, d_step = block_outer(
        prompt_inner, x_act, b_act, c_act, step_g, rate, start_state, prompt_cot, end_grad
    )
    prompt_grads = prompt_conv_pullback(
        (dx.reshape(prompt_len, -1), db.reshape(prompt_len, -1), dc.reshape(prompt_len, -1))
    )
    prefix_ddt = step_pullback(d_step.reshape(num_heads, prompt_len))[0]
    left_grads = jnp.concatenate([prompt_grads[3], prompt_grads[4], prompt_grads[5]], axis=1)
    from_right = from_behind(left_grads, "suf", -1)
    ctx_grads = jnp.concatenate(
        [jnp.sum(conv_grads[3], axis=0), jnp.sum(conv_grads[4], axis=0), jnp.sum(conv_grads[5], axis=0)],
        axis=1,
    )
    from_suffix = ctx_grads
    for sender in range(num_ways - 1):
        from_suffix = from_suffix + lax.ppermute(ctx_grads, "suf", [(sender, num_ways - 1)])
    last_device = my_index == num_ways - 1
    tail_add = split_tokens(from_right + jnp.where(last_device, from_suffix, 0.0))

    def finish(grad_full, extra):
        placed = jnp.pad(extra, ((grad_full.shape[0] - margin, 0), (0, 0)))
        return (grad_full + placed).astype(jnp.bfloat16)

    return (
        finish(prompt_grads[0], tail_add[0]),
        finish(prompt_grads[1], tail_add[1]),
        finish(prompt_grads[2], tail_add[2]),
        prefix_ddt,
        conv_grads[0].astype(jnp.bfloat16),
        conv_grads[1].astype(jnp.bfloat16),
        conv_grads[2].astype(jnp.bfloat16),
        suffix_ddt,
    )


def solution(mesh):
    return jax.shard_map(
        shards,
        mesh=mesh,
        in_specs=(
            P(("grp", "suf"), "head"),
            P(("grp", "suf"), "head"),
            P(("grp", "suf"), "head"),
            P("head", ("grp", "suf")),
            P(("grp", "suf"), "head"),
            P(("grp", "suf"), None, "head"),
            P(("grp", "suf"), None, "head"),
            P(("grp", "suf"), None, "head"),
            P("head", ("grp", "suf"), None),
            P(("grp", "suf"), None, "head"),
            P(("grp", "suf")),
            P(("grp", "suf"), None),
            P(("grp", "suf")),
            P(None, "head"),
            P(None, "head"),
            P(None, "head"),
            P("head"),
            P("head"),
            P("head"),
        ),
        out_specs=(
            P(("grp", "suf"), "head"),
            P(("grp", "suf"), "head"),
            P(("grp", "suf"), "head"),
            P("head", ("grp", "suf")),
            P(("grp", "suf"), None, "head"),
            P(("grp", "suf"), None, "head"),
            P(("grp", "suf"), None, "head"),
            P("head", ("grp", "suf"), None),
        ),
        check_vma=False,
    )
```

```python
import functools

import jax
import jax.numpy as jnp
from jax import lax
from jax.experimental import pallas as pl
from jax.experimental.pallas import tpu as pltpu
from jax.sharding import PartitionSpec as P


HD = 64
N = 128
KW = 4


EXACT_DOT = lax.Precision.HIGHEST


def from_behind(block, axis, distance):
    devices = range(lax.axis_size(axis))
    route = [(i - distance, i) for i in devices if i - distance in devices]
    return lax.ppermute(block, axis, route)


def causal_conv(values, context, taps):
    padded = jnp.concatenate([context, values], axis=0)
    num_tokens = values.shape[0]
    result = padded[0:num_tokens] * taps[0].astype(jnp.float32)
    for tap_index in range(1, taps.shape[0]):
        result = result + padded[tap_index : tap_index + num_tokens] * taps[tap_index].astype(
            jnp.float32
        )
    return jax.nn.silu(result)


def _dot(a, b, dims):
    return lax.dot_general(a, b, (dims, ((), ())), precision=EXACT_DOT, preferred_element_type=jnp.float32)


def _grad_kernel(steps_per_group, x_ref, g_ref, b_ref, c_ref, crow_ref, srow_ref, skip_ref,
                 dx_ref, dstep_ref, dcum_ref, dc_ref, db_ref, dsc_ref):
    step_id = pl.program_id(0)
    bb = b_ref[...]
    cc = c_ref[...]
    t_len = bb.shape[0]
    lanes = 2 * HD
    tri = lax.broadcasted_iota(jnp.int32, (t_len, t_len), 0) >= lax.broadcasted_iota(jnp.int32, (t_len, t_len), 1)
    lane = lax.broadcasted_iota(jnp.int32, (1, lanes), 1)
    ones = jnp.ones((8, t_len), jnp.float32)
    scores = _dot(cc, bb, ((1,), (1,)))
    dsc = jnp.zeros((t_len, t_len), jnp.float32)
    for pair in range(dx_ref.shape[1] // lanes):
        cols = slice(pair * lanes, (pair + 1) * lanes)
        x = x_ref[:, cols]
        g = g_ref[:, cols]
        dx = skip_ref[:, cols] * g
        for h in range(2):
            head = 2 * pair + h
            mask = ((lane >= h * HD) & (lane < (h + 1) * HD)).astype(jnp.float32)
            gm = g * mask
            crow = crow_ref[head : head + 1, :]
            srow = srow_ref[head : head + 1, :]
            ccol = jnp.transpose(jnp.broadcast_to(crow, (t_len, t_len)))
            within = jnp.where(tri, jnp.exp(jnp.where(tri, ccol - crow, 0.0)), 0.0)
            score_w = scores * within
            d_mix = _dot(gm, x, ((1,), (1,)))
            dx = dx + _dot(score_w * srow, gm, ((0,), (0,)))
            dsc = dsc + d_mix * within * srow
            q_mat = d_mix * score_w
            p_mat = q_mat * srow
            dstep_ref[head : head + 1, :] = jnp.sum(q_mat, axis=0, keepdims=True)
            dcum_ref[head : head + 1, :] = _dot(ones, p_mat, ((1,), (1,)))[0:1] - jnp.sum(
                p_mat, axis=0, keepdims=True
            )
        dx_ref[:, cols] = dx
    within_group = step_id % steps_per_group

    @pl.when(within_group == 0)
    def _():
        dsc_ref[...] = dsc

    @pl.when(within_group != 0)
    def _():
        dsc_ref[...] += dsc

    @pl.when(within_group == steps_per_group - 1)
    def _():
        total = dsc_ref[...]
        dc_ref[...] = _dot(total, bb, ((1,), (0,)))
        db_ref[...] = _dot(total, cc, ((0,), (0,)))


def block_inner(xa, ba, ca, step, rate, skip, G):
    T, ng, nk, P = xa.shape
    nh = ng * nk
    heads_per_step = 8
    steps_per_group = nk // heads_per_step
    cum = jnp.cumsum(-step * rate[:, :, None], axis=-1)
    row_spec = pl.BlockSpec((heads_per_step, T), lambda j: (j, 0))
    lane_spec = pl.BlockSpec((T, heads_per_step * P), lambda j: (0, j))
    grp_spec = pl.BlockSpec((T, N), lambda j: (0, j // steps_per_group))
    dx2, d_direct, d_cum, dc, db = pl.pallas_call(
        functools.partial(_grad_kernel, steps_per_group),
        grid=(nh // heads_per_step,),
        in_specs=[
            lane_spec, lane_spec, grp_spec, grp_spec, row_spec, row_spec,
            pl.BlockSpec((1, heads_per_step * P), lambda j: (0, j)),
        ],
        out_specs=[lane_spec, row_spec, row_spec, grp_spec, grp_spec],
        out_shape=[
            jax.ShapeDtypeStruct((T, nh * P), jnp.float32),
            jax.ShapeDtypeStruct((nh, T), jnp.float32),
            jax.ShapeDtypeStruct((nh, T), jnp.float32),
            jax.ShapeDtypeStruct((T, ng * N), jnp.float32),
            jax.ShapeDtypeStruct((T, ng * N), jnp.float32),
        ],
        scratch_shapes=[pltpu.VMEM((T, T), jnp.float32)],
    )(
        xa.reshape(T, nh * P),
        G.reshape(T, nh * P),
        ba.reshape(T, ng * N),
        ca.reshape(T, ng * N),
        cum.reshape(nh, T),
        step.reshape(nh, T),
        jnp.repeat(skip.reshape(1, nh), P, axis=1),
    )
    return (
        dx2.reshape(T, ng, nk, P),
        d_direct.reshape(ng, nk, T),
        d_cum.reshape(ng, nk, T),
        dc.reshape(T, ng, N),
        db.reshape(T, ng, N),
        cum,
    )


def block_outer(inner, xa, ba, ca, step, rate, S0, G, lam):
    dx, d_step, d_cum, dc, db, cum = inner
    grow = jnp.exp(cum)
    g_grow = G * grow.transpose(2, 0, 1)[..., None]
    carried = jnp.einsum("tgn,gkpn->tgkp", ca, S0, precision=EXACT_DOT)
    dc = dc + jnp.einsum("tgkp,gkpn->tgn", g_grow, S0, precision=EXACT_DOT)
    d_cum = d_cum + jnp.sum(g_grow * carried, axis=-1).transpose(1, 2, 0)
    if lam is not None:
        to_end = jnp.exp(cum[..., -1:] - cum)
        push = to_end * step
        lam_b = jnp.einsum("gkpn,sgn->sgkp", lam, ba, precision=EXACT_DOT)
        dx = dx + push.transpose(2, 0, 1)[..., None] * lam_b
        db = db + jnp.einsum("gkpn,sgkp,gks->sgn", lam, xa, push, precision=EXACT_DOT)
        q_end = jnp.sum(xa * lam_b, axis=-1).transpose(1, 2, 0)
        d_step = d_step + to_end * q_end
        wq = push * q_end
        end_total = jnp.sum(wq, axis=-1) + jnp.exp(cum[..., -1]) * jnp.sum(
            jnp.einsum("gkpn,n->gkp", lam * S0, jnp.ones((S0.shape[-1],), jnp.float32), precision=EXACT_DOT),
            axis=-1,
        )
        d_cum = d_cum - wq
        d_cum = d_cum.at[..., -1].add(end_total)
    d_log = jnp.flip(jnp.cumsum(jnp.flip(d_cum, -1), axis=-1), -1)
    d_step = d_step - rate[:, :, None] * d_log
    return dx, db, dc, d_step


def shards(
    prefix_x,
    prefix_b,
    prefix_c,
    prefix_dt,
    prefix_grad,
    suffix_x,
    suffix_b,
    suffix_c,
    suffix_dt,
    suffix_grad,
    lengths,
    loss_mask,
    advantage,
    conv_x,
    conv_b,
    conv_c,
    decay_rate,
    dt_bias,
    skip,
):
    num_ways = lax.axis_size("suf")
    my_index = lax.axis_index("suf")
    num_heads = decay_rate.shape[0]
    num_groups = conv_b.shape[1] // N
    per_group = num_heads // num_groups
    margin = KW - 1
    prompt_len = prefix_x.shape[0]
    width_x = prefix_x.shape[1]
    width_b = prefix_b.shape[1]
    rate = decay_rate.reshape(num_groups, per_group)
    gain = skip.reshape(num_groups, per_group)

    def split_tokens(tokens):
        return (
            tokens[:, :width_x],
            tokens[:, width_x : width_x + width_b],
            tokens[:, width_x + width_b :],
        )

    def convs(ux, ub, uc, cx, cb, cc):
        return (
            causal_conv(ux, cx, conv_x),
            causal_conv(ub, cb, conv_b),
            causal_conv(uc, cc, conv_c),
        )

    def softplus_of(raw):
        return jax.nn.softplus(raw + dt_bias[:, None])

    prompt_step, step_pullback = jax.vjp(softplus_of, prefix_dt)
    cumulative = jnp.cumsum(-prompt_step * decay_rate[:, None], axis=1)
    total_log = cumulative[:, -1]
    tails = jnp.concatenate(
        [prefix_x[-margin:], prefix_b[-margin:], prefix_c[-margin:]], axis=1
    ).astype(jnp.float32)
    tail_size = tails.size
    own_pack = jnp.concatenate([tails.reshape(-1), total_log])
    received = [own_pack] + [
        lax.ppermute(own_pack, "suf", [(j, (j + shift) % num_ways) for j in range(num_ways)])
        for shift in range(1, num_ways)
    ]
    every = jnp.take(
        jnp.stack(received), (my_index - jnp.arange(num_ways)) % num_ways, axis=0
    )
    every_tails = every[:, :tail_size].reshape((num_ways,) + tails.shape)
    every_log = every[:, tail_size:]
    behind = lax.dynamic_index_in_dim(every_tails, jnp.maximum(my_index - 1, 0), 0, False)
    behind = jnp.where(my_index > 0, behind, 0.0)
    left_x, left_b, left_c = split_tokens(behind)
    ctx_x, ctx_b, ctx_c = split_tokens(every_tails[num_ways - 1])

    acts, prompt_conv_pullback = jax.vjp(
        convs,
        prefix_x.astype(jnp.float32),
        prefix_b.astype(jnp.float32),
        prefix_c.astype(jnp.float32),
        left_x,
        left_b,
        left_c,
    )
    x_act = acts[0].reshape(prompt_len, num_groups, per_group, HD)
    b_act = acts[1].reshape(prompt_len, num_groups, N)
    c_act = acts[2].reshape(prompt_len, num_groups, N)
    prompt_cot = prefix_grad.astype(jnp.float32).reshape(prompt_len, num_groups, per_group, HD)
    push_weight = (jnp.exp(total_log[:, None] - cumulative) * prompt_step).reshape(
        num_groups, per_group, prompt_len
    )
    own_state = jnp.einsum("gkt,tgkp,tgn->gkpn", push_weight, x_act, b_act, precision=EXACT_DOT)
    pull_weight = jnp.exp(cumulative).reshape(num_groups, per_group, prompt_len)
    own_adjoint = jnp.einsum(
        "gkt,tgkp,tgn->gkpn", pull_weight, prompt_cot, c_act, precision=EXACT_DOT
    )
    positions = jnp.arange(suffix_x.shape[1])[None, :]
    weight = (
        advantage[:, None]
        * loss_mask.astype(jnp.float32)
        * (positions < lengths[:, None]).astype(jnp.float32)
    )

    def suffix_parts(x_one, b_one, c_one, dt_one, grad_one, weight_one):
        suffix_len = x_one.shape[0]
        step_one, one_step_pullback = jax.vjp(softplus_of, dt_one)
        s_acts, conv_pullback = jax.vjp(convs, x_one, b_one, c_one, ctx_x, ctx_b, ctx_c)
        sx = s_acts[0].reshape(suffix_len, num_groups, per_group, HD)
        sb = s_acts[1].reshape(suffix_len, num_groups, N)
        sc = s_acts[2].reshape(suffix_len, num_groups, N)
        cot = (weight_one[:, None] * grad_one).reshape(suffix_len, num_groups, per_group, HD)
        step_g = step_one.reshape(num_groups, per_group, suffix_len)
        return one_step_pullback, conv_pullback, sx, sb, sc, cot, step_g

    def suffix_front(*items):
        _, _, sx, sb, sc, cot, step_g = suffix_parts(*items)
        grow = jnp.exp(jnp.cumsum(-step_g * rate[:, :, None], axis=-1))
        adjoint = jnp.einsum("gkt,tgkp,tgn->gkpn", grow, cot, sc, precision=EXACT_DOT)
        inner = block_inner(sx, sb, sc, step_g, rate, gain, cot)
        return adjoint, inner

    def suffix_back(end_state, inner, *items):
        one_step_pullback, conv_pullback, sx, sb, sc, cot, step_g = suffix_parts(*items)
        suffix_len = sx.shape[0]
        dx, db, dc, d_step = block_outer(inner, sx, sb, sc, step_g, rate, end_state, cot, None)
        conv_grads = conv_pullback(
            (dx.reshape(suffix_len, -1), db.reshape(suffix_len, -1), dc.reshape(suffix_len, -1))
        )
        d_dt = one_step_pullback(d_step.reshape(num_heads, suffix_len))[0]
        return conv_grads, d_dt

    suffix_items = (
        suffix_x.astype(jnp.float32),
        suffix_b.astype(jnp.float32),
        suffix_c.astype(jnp.float32),
        suffix_dt,
        suffix_grad.astype(jnp.float32),
        weight,
    )
    adjoints, suffix_inner = jax.vmap(suffix_front, in_axes=(0, 0, 0, 1, 0, 0))(*suffix_items)
    step_g = prompt_step.reshape(num_groups, per_group, prompt_len)
    prompt_inner = block_inner(x_act, b_act, c_act, step_g, rate, gain, prompt_cot)
    core = my_index % 2
    chip = my_index // 2
    num_chips = num_ways // 2
    own_triple = jnp.stack([own_state, own_adjoint, jnp.sum(adjoints, axis=0)])
    partner_triple = lax.ppermute(own_triple, "suf", [(j, j ^ 1) for j in range(num_ways)])
    even = jnp.where(core == 0, own_triple, partner_triple)
    odd = jnp.where(core == 0, partner_triple, own_triple)
    block_decay = jnp.exp(every_log).reshape(num_ways, num_groups, per_group, 1, 1)
    decay_even = lax.dynamic_index_in_dim(block_decay, 2 * chip, 0, False)
    decay_odd = lax.dynamic_index_in_dim(block_decay, 2 * chip + 1, 0, False)
    chip_log = every_log.reshape(num_chips, 2, num_heads).sum(axis=1)
    later_log = jnp.sum(jnp.where((jnp.arange(num_chips) >= chip)[:, None], chip_log, 0.0), axis=0)
    chip_state = decay_odd * even[0] + odd[0]
    chip_adjoint = even[1] + decay_even * odd[1]
    chip_suffix = even[2] + odd[2]
    chip_later = chip_adjoint + jnp.exp(later_log).reshape(num_groups, per_group, 1, 1) * chip_suffix
    got_state = [chip_state]
    got_other = [chip_suffix]
    for shift in range(1, num_chips):
        wraps = chip + shift >= num_chips
        outgoing = jnp.where(core == 0, chip_state, jnp.where(wraps, chip_later, chip_suffix))
        route = [
            (2 * c + k, 2 * ((c + shift) % num_chips) + k) for c in range(num_chips) for k in range(2)
        ]
        incoming = lax.ppermute(outgoing, "suf", route)
        shared = lax.ppermute(incoming, "suf", [(j, j ^ 1) for j in range(num_ways)])
        got_state.append(jnp.where(core == 0, incoming, shared))
        got_other.append(jnp.where(core == 0, shared, incoming))

    def chip_ordered(got):
        ordered = []
        for c in range(num_chips):
            distance = (chip - c) % num_chips
            value = got[0]
            for shift in range(1, num_chips):
                value = jnp.where(distance == shift, got[shift], value)
            ordered.append(value)
        return ordered

    chip_states = chip_ordered(got_state)
    chip_others = chip_ordered(got_other)
    chip_decay = jnp.exp(chip_log).reshape(num_chips, num_groups, per_group, 1, 1)
    running = jnp.zeros_like(own_state)
    chip_start = running
    for c in range(num_chips):
        chip_start = jnp.where(chip == c, running, chip_start)
        running = chip_decay[c] * running + chip_states[c]
    prompt_end_late = running
    running = jnp.zeros_like(own_state)
    for c in range(num_chips):
        running = running + jnp.where(c <= chip, chip_others[c], 0.0)
    chip_end_grad = running
    for c in reversed(range(num_chips)):
        chip_end_grad = jnp.where(chip == c, running, chip_end_grad)
        running = chip_others[c] + chip_decay[c] * running
    start_state = jnp.where(core == 0, chip_start, decay_even * chip_start + even[0])
    end_grad = jnp.where(core == 0, odd[1] + decay_odd * chip_end_grad, chip_end_grad)
    conv_grads, suffix_ddt = jax.vmap(
        suffix_back, in_axes=(None, 0, 0, 0, 0, 1, 0, 0), out_axes=(0, 1)
    )(prompt_end_late, suffix_inner, *suffix_items)
    dx, db, dc, d_step = block_outer(
        prompt_inner, x_act, b_act, c_act, step_g, rate, start_state, prompt_cot, end_grad
    )
    prompt_grads = prompt_conv_pullback(
        (dx.reshape(prompt_len, -1), db.reshape(prompt_len, -1), dc.reshape(prompt_len, -1))
    )
    prefix_ddt = step_pullback(d_step.reshape(num_heads, prompt_len))[0]
    left_grads = jnp.concatenate([prompt_grads[3], prompt_grads[4], prompt_grads[5]], axis=1)
    from_right = from_behind(left_grads, "suf", -1)
    ctx_grads = jnp.concatenate(
        [jnp.sum(conv_grads[3], axis=0), jnp.sum(conv_grads[4], axis=0), jnp.sum(conv_grads[5], axis=0)],
        axis=1,
    )
    from_suffix = ctx_grads
    for sender in range(num_ways - 1):
        from_suffix = from_suffix + lax.ppermute(ctx_grads, "suf", [(sender, num_ways - 1)])
    last_device = my_index == num_ways - 1
    tail_add = split_tokens(from_right + jnp.where(last_device, from_suffix, 0.0))

    def finish(grad_full, extra):
        placed = jnp.pad(extra, ((grad_full.shape[0] - margin, 0), (0, 0)))
        return (grad_full + placed).astype(jnp.bfloat16)

    return (
        finish(prompt_grads[0], tail_add[0]),
        finish(prompt_grads[1], tail_add[1]),
        finish(prompt_grads[2], tail_add[2]),
        prefix_ddt,
        conv_grads[0].astype(jnp.bfloat16),
        conv_grads[1].astype(jnp.bfloat16),
        conv_grads[2].astype(jnp.bfloat16),
        suffix_ddt,
    )


def solution(mesh):
    return jax.shard_map(
        shards,
        mesh=mesh,
        in_specs=(
            P(("grp", "suf"), "head"),
            P(("grp", "suf"), "head"),
            P(("grp", "suf"), "head"),
            P("head", ("grp", "suf")),
            P(("grp", "suf"), "head"),
            P(("grp", "suf"), None, "head"),
            P(("grp", "suf"), None, "head"),
            P(("grp", "suf"), None, "head"),
            P("head", ("grp", "suf"), None),
            P(("grp", "suf"), None, "head"),
            P(("grp", "suf")),
            P(("grp", "suf"), None),
            P(("grp", "suf")),
            P(None, "head"),
            P(None, "head"),
            P(None, "head"),
            P("head"),
            P("head"),
            P("head"),
        ),
        out_specs=(
            P(("grp", "suf"), "head"),
            P(("grp", "suf"), "head"),
            P(("grp", "suf"), "head"),
            P("head", ("grp", "suf")),
            P(("grp", "suf"), None, "head"),
            P(("grp", "suf"), None, "head"),
            P(("grp", "suf"), None, "head"),
            P("head", ("grp", "suf"), None),
        ),
        check_vma=False,
    )
```
